32 devices in a mesh: groups: 2 (over y), tiles: 4 (over z), band: 2 (over x), stokes: 2 (over core).
Axes of the slice: x: 2, y: 2, z: 4, core: 2. Of those that a mesh axis runs over, the one named last changes fastest.
Arguments:
- right_side: float32 [3, 128, 2048], P(None, ('groups', 'tiles'), ('band', 'stokes')), parts along dimension 1, may hold values from -4 to 4
- noise_block: float32 [6, 128, 2048], P(None, ('groups', 'tiles'), ('band', 'stokes')), parts along dimension 1, may hold values from -0.09 to 0.4, as said below
- edges: float32 [2, 128, 2048], P(None, ('groups', 'tiles'), ('band', 'stokes')), parts along dimension 1, may hold values from 0.5 to 2
Outputs:
- correction: float32 [3, 128, 2048], P(None, ('groups', 'tiles'), ('band', 'stokes')), parts along dimension 1
The draws below stay inside these ranges and needn't reach their ends.
There are 2 independent parts, one for each index of `groups`. The reference program is written for one: setup_inputs(seed, part) draws one part's arguments, and reference() takes and returns one part's arrays. A program takes and returns all parts, laid end to end along the dimension named above; each array names one. Nothing has to cross between parts.
Inputs may be any that keep to these rules, and one draw needn't show every extreme that they name: `noise_block`: entries 0 to 2 are positive and each exceeds the sum of the magnitudes of the two couplings in its row of the 3 x 3 matrix.
All inputs are finite; a program needn't handle non-finite values.
Results may differ from the reference program's by a relative error of at most 0.00002.
Values sent between devices are 32-bit elements; how exact they have to be, the bound alone decides.
No kernel may reach another device: no remote copies, remote signals or barrier semaphores. Data moves between devices by JAX's collectives and lax.ppermute only.
A program may use at most 64 MiB of HBM per device.

```python
import math
import jax
import jax.numpy as jnp

LEVELS = 5
PRE = 2
POST = 2
COARSE_SWEEPS = 8
NR = 64
NC = 2048


def draw_right_side(key, part):
    return jnp.clip(jax.random.normal(key, (3, NR, NC), jnp.float32), -4.0, 4.0)


def draw_noise_block(key, part):
    hits_key = jax.random.fold_in(key, 11)
    diag_key = jax.random.fold_in(key, 12)
    cross_key = jax.random.fold_in(key, 13)
    hits = jnp.exp(jax.random.uniform(hits_key, (1, NR, NC), jnp.float32, math.log(0.005), math.log(0.2)))
    diagonal = hits * jax.random.uniform(diag_key, (3, NR, NC), jnp.float32, 1.0, 2.0)
    crossed = hits * jax.random.uniform(cross_key, (3, NR, NC), jnp.float32, -0.45, 0.45)
    return jnp.concatenate([diagonal, crossed], axis=0)


def shard_levels(stream_key, extent, pieces, least, high):
    def one(dim, parts):
        draws = jax.random.uniform(jax.random.fold_in(jax.random.fold_in(stream_key, 6), dim), (parts,), jnp.float32, least / len(pieces), high / len(pieces))
        return jnp.repeat(jnp.exp(draws), extent[dim] // parts).reshape((-1,) + (1,) * (len(extent) - dim - 1))

    loudness = one(*pieces[0])
    for cut in pieces[1:]:
        loudness = loudness * one(*cut)
    return loudness


def setup_inputs(seed: int = 0, part: int = 0) -> dict:
    seeds = jax.random.split(jax.random.key(seed), 4)
    part_keys = jax.random.split(jax.random.fold_in(seeds[3], part), 4)
    return {
        "right_side": draw_right_side(jax.random.fold_in(jax.random.fold_in(seeds[3], part), 71), part),
        "noise_block": draw_noise_block(jax.random.fold_in(jax.random.fold_in(seeds[3], part), 71), part),
        "edges": jnp.clip(jnp.exp(math.log(2.0) - 1.3862944 * jax.random.uniform(part_keys[2], (2, NR, NC), jnp.float32) ** shard_levels(part_keys[2], (2, NR, NC), ((1, 4), (2, 4)), -0.2, 0.2)), 0.5, 2.0),
    }


OMEGA = 0.8


def apply_padded(iterate, padded, noise, couplings):
    first = noise[0] * iterate[0] + noise[3] * iterate[1] + noise[4] * iterate[2]
    second = noise[3] * iterate[0] + noise[1] * iterate[1] + noise[5] * iterate[2]
    third = noise[4] * iterate[0] + noise[5] * iterate[1] + noise[2] * iterate[2]
    totals = couplings[0] + couplings[1] + couplings[2] + couplings[3]
    neighbours = (couplings[0] * padded[:, 2:, 1:-1] + couplings[1] * padded[:, :-2, 1:-1]
                  + couplings[2] * padded[:, 1:-1, 2:] + couplings[3] * padded[:, 1:-1, :-2])
    return jnp.stack([first, second, third]) + totals * iterate - neighbours


def zero_rim(iterate):
    return jnp.pad(iterate, ((0, 0), (1, 1), (1, 1)))


def diagonal_of(noise, couplings):
    return noise[0:3] + (couplings[0] + couplings[1] + couplings[2] + couplings[3])


def restrict_sum(field):
    depth, height, width = field.shape
    return field.reshape(depth, height // 2, 2, width // 2, 2).sum(axis=(2, 4))


def coarsen_couplings(couplings):
    depth, height, width = couplings.shape
    blocks = couplings.reshape(4, height // 2, 2, width // 2, 2)
    downward = blocks[0][:, 1, :, :].sum(axis=-1)
    upward = blocks[1][:, 0, :, :].sum(axis=-1)
    rightward = blocks[2][:, :, :, 1].sum(axis=1)
    leftward = blocks[3][:, :, :, 0].sum(axis=1)
    return jnp.stack([downward, upward, rightward, leftward])


def prolong(coarse):
    return jnp.repeat(jnp.repeat(coarse, 2, axis=1), 2, axis=2)


def smooth(iterate, source, noise, couplings, diagonal):
    image = apply_padded(iterate, zero_rim(iterate), noise, couplings)
    return iterate + OMEGA * (source - image) / diagonal


def cycle(source, noise, couplings, level_index):
    diagonal = diagonal_of(noise, couplings)
    iterate = OMEGA * source / diagonal
    if level_index == LEVELS - 1:
        for sweep_index in range(COARSE_SWEEPS - 1):
            iterate = smooth(iterate, source, noise, couplings, diagonal)
        return iterate
    for sweep_index in range(PRE - 1):
        iterate = smooth(iterate, source, noise, couplings, diagonal)
    residual = source - apply_padded(iterate, zero_rim(iterate), noise, couplings)
    coarse = cycle(restrict_sum(residual), restrict_sum(noise), coarsen_couplings(couplings), level_index + 1)
    iterate = iterate + prolong(coarse)
    for sweep_index in range(POST):
        iterate = smooth(iterate, source, noise, couplings, diagonal)
    return iterate


def reference(right_side, noise_block, edges):
    upward = jnp.pad(edges[0], ((1, 0), (0, 0)))[:-1, :]
    leftward = jnp.pad(edges[1], ((0, 0), (1, 0)))[:, :-1]
    couplings = jnp.stack([edges[0], upward, edges[1], leftward])
    return cycle(right_side, noise_block, couplings, 0)
```

```python
import jax
import jax.numpy as jnp
from jax import lax
from jax.sharding import PartitionSpec as P

LEVELS = 5
PRE = 2
POST = 2
COARSE_SWEEPS = 8

OMEGA = 0.8

ROWS = "tiles"
COLS = ("band", "stokes")
GRID = ("tiles", "band", "stokes")

HALO = PRE - 1 + POST
GATHER_PIXELS = 32768


def with_halo(cells, width):
    for axis, dim in ((ROWS, 1), (COLS, 2)):
        count = lax.axis_size(axis)
        ends = count - 1
        head = lax.slice_in_dim(cells, 0, width, axis=dim)
        tail = lax.slice_in_dim(cells, cells.shape[dim] - width, cells.shape[dim], axis=dim)
        cells = jnp.concatenate(
            [
                lax.ppermute(tail, axis, [(i, i + 1) for i in range(ends)]),
                cells,
                lax.ppermute(head, axis, [(i + 1, i) for i in range(ends)]),
            ],
            axis=dim,
        )
    return cells


def crop(x, k):
    if k == 0:
        return x
    return x[..., k:-k, k:-k]


def apply_padded(iterate, padded, noise, couplings):
    first = noise[0] * iterate[0] + noise[3] * iterate[1] + noise[4] * iterate[2]
    second = noise[3] * iterate[0] + noise[1] * iterate[1] + noise[5] * iterate[2]
    third = noise[4] * iterate[0] + noise[5] * iterate[1] + noise[2] * iterate[2]
    totals = couplings[0] + couplings[1] + couplings[2] + couplings[3]
    neighbours = (
        couplings[0] * padded[:, 2:, 1:-1]
        + couplings[1] * padded[:, :-2, 1:-1]
        + couplings[2] * padded[:, 1:-1, 2:]
        + couplings[3] * padded[:, 1:-1, :-2]
    )
    return jnp.stack([first, second, third]) + totals * iterate - neighbours


def apply_ext(padded, noise, couplings):
    return apply_padded(padded[:, 1:-1, 1:-1], padded, noise, couplings)


def diagonal_of(noise, couplings):
    return noise[0:3] + (couplings[0] + couplings[1] + couplings[2] + couplings[3])


def restrict_sum(field):
    depth, height, width = field.shape
    return field.reshape(depth, height // 2, 2, width // 2, 2).sum(axis=(2, 4))


def restrict_down(down):
    height, width = down.shape
    return down.reshape(height // 2, 2, width // 2, 2)[:, 1, :, :].sum(axis=-1)


def restrict_right(right):
    height, width = right.shape
    return right.reshape(height // 2, 2, width // 2, 2)[:, :, :, 1].sum(axis=1)


def coarsen_couplings(couplings):
    depth, height, width = couplings.shape
    blocks = couplings.reshape(4, height // 2, 2, width // 2, 2)
    downward = blocks[0][:, 1, :, :].sum(axis=-1)
    upward = blocks[1][:, 0, :, :].sum(axis=-1)
    rightward = blocks[2][:, :, :, 1].sum(axis=1)
    leftward = blocks[3][:, :, :, 0].sum(axis=1)
    return jnp.stack([downward, upward, rightward, leftward])


def prolong(coarse):
    return jnp.repeat(jnp.repeat(coarse, 2, axis=1), 2, axis=2)


def zero_rim(iterate):
    return jnp.pad(iterate, ((0, 0), (1, 1), (1, 1)))


def couplings_from(down, right):
    upward = jnp.pad(down, ((1, 0), (0, 0)))[:-1, :]
    leftward = jnp.pad(right, ((0, 0), (1, 0)))[:, :-1]
    return jnp.stack([down, upward, right, leftward])


def smooth_whole(iterate, source, noise, couplings, diagonal):
    image = apply_padded(iterate, zero_rim(iterate), noise, couplings)
    return iterate + OMEGA * (source - image) / diagonal


def cycle_whole(source, noise, couplings, level_index):
    diagonal = diagonal_of(noise, couplings)
    iterate = OMEGA * source / diagonal
    if level_index == LEVELS - 1:
        for sweep_index in range(COARSE_SWEEPS - 1):
            iterate = smooth_whole(iterate, source, noise, couplings, diagonal)
        return iterate
    for sweep_index in range(PRE - 1):
        iterate = smooth_whole(iterate, source, noise, couplings, diagonal)
    residual = source - apply_padded(iterate, zero_rim(iterate), noise, couplings)
    coarse = cycle_whole(
        restrict_sum(residual), restrict_sum(noise), coarsen_couplings(couplings), level_index + 1
    )
    iterate = iterate + prolong(coarse)
    for sweep_index in range(POST):
        iterate = smooth_whole(iterate, source, noise, couplings, diagonal)
    return iterate


def gather_grid(block):
    count_rows = lax.axis_size(ROWS)
    count_cols = lax.axis_size(COLS)
    planes, height, width = block.shape
    stacked = lax.all_gather(block, GRID, axis=0, tiled=False)
    stacked = stacked.reshape(count_rows, count_cols, planes, height, width)
    return stacked.transpose(2, 0, 3, 1, 4).reshape(planes, count_rows * height, count_cols * width)


def own_window(whole, height, width, ring):
    row = lax.axis_index(ROWS) * height
    col = lax.axis_index(COLS) * width
    padded = jnp.pad(whole, ((0, 0), (ring, ring), (ring, ring))) if ring else whole
    return lax.dynamic_slice(
        padded, (0, row, col), (whole.shape[0], height + 2 * ring, width + 2 * ring)
    )


def inside(height, width, ext):
    rows = lax.axis_index(ROWS) * height - ext + lax.broadcasted_iota(
        jnp.int32, (height + 2 * ext, width + 2 * ext), 0
    )
    cols = lax.axis_index(COLS) * width - ext + lax.broadcasted_iota(
        jnp.int32, (height + 2 * ext, width + 2 * ext), 1
    )
    return (
        (rows >= 0)
        & (rows < lax.axis_size(ROWS) * height)
        & (cols >= 0)
        & (cols < lax.axis_size(COLS) * width)
    )


def sweep_ext(iterate, source, noise, couplings, diagonal, mask):
    core = iterate[:, 1:-1, 1:-1]
    new = core + OMEGA * (source - apply_ext(iterate, noise, couplings)) / diagonal
    if mask is None:
        return new
    return jnp.where(mask, new, 0.0)


def level_split(source, noise, couplings, below):
    height = source.shape[1] - 2 * HALO
    width = source.shape[2] - 2 * HALO
    diagonal = diagonal_of(noise, couplings)
    ext = HALO
    iterate = jnp.where(inside(height, width, ext), OMEGA * source / diagonal, 0.0)
    for sweep_index in range(PRE - 1):
        ext -= 1
        cut = HALO - ext
        iterate = sweep_ext(
            iterate, crop(source, cut), crop(noise, cut), crop(couplings, cut), crop(diagonal, cut),
            inside(height, width, ext),
        )
    residual = crop(source, HALO) - apply_ext(
        crop(iterate, ext - 1), crop(noise, HALO), crop(couplings, HALO)
    )
    coarse = below(residual)
    ring = (POST + 1) // 2
    fine = prolong(coarse)
    iterate = crop(iterate, ext - POST) + crop(fine, 2 * ring - POST)
    for sweep_index in range(POST):
        ext = POST - 1 - sweep_index
        cut = HALO - ext
        iterate = sweep_ext(
            iterate, crop(source, cut), crop(noise, cut), crop(couplings, cut), crop(diagonal, cut),
            inside(height, width, ext) if ext else None,
        )
    return iterate


def on_device(right_side, noise_block, edges):
    count_rows = lax.axis_size(ROWS)
    count_cols = lax.axis_size(COLS)
    height0, width0 = right_side.shape[1], right_side.shape[2]

    noises = [noise_block]
    downs = [edges[0]]
    rights = [edges[1]]
    for level in range(1, LEVELS):
        noises.append(restrict_sum(noises[-1]))
        downs.append(restrict_down(downs[-1]))
        rights.append(restrict_right(rights[-1]))

    gathered = LEVELS - 1
    for level in range(LEVELS):
        height, width = height0 >> level, width0 >> level
        whole = count_rows * height * count_cols * width
        if whole <= GATHER_PIXELS or height <= HALO or width <= HALO or level == LEVELS - 1:
            gathered = level
            break

    if gathered > 0:
        packed = gather_grid(
            jnp.concatenate([noises[gathered], downs[gathered][None], rights[gathered][None]])
        )
        whole_noise = packed[:6]
        whole_couplings = couplings_from(packed[6], packed[7])
    split_inputs = []
    for level in range(gathered):
        parts = [noises[level], downs[level][None], rights[level][None]]
        if level == 0:
            parts = [right_side] + parts
        ringed = with_halo(jnp.concatenate(parts), HALO + 1)
        if level == 0:
            source, ringed = ringed[:3], ringed[3:]
        else:
            source = None
        down, right = ringed[6], ringed[7]
        noise = crop(ringed[:6], 1)
        couplings = jnp.stack(
            [
                down[1:-1, 1:-1],
                down[:-2, 1:-1],
                right[1:-1, 1:-1],
                right[1:-1, :-2],
            ]
        )
        split_inputs.append((None if source is None else crop(source, 1), noise, couplings))

    if gathered == 0:
        whole = gather_grid(jnp.concatenate([right_side, noise_block, edges]))
        correction = cycle_whole(whole[:3], whole[3:9], couplings_from(whole[9], whole[10]), 0)
        return own_window(correction, height0, width0, 0)

    ring = (POST + 1) // 2

    def run(level, source):
        height, width = height0 >> level, width0 >> level
        _, noise, couplings = split_inputs[level]

        def below(residual):
            coarse_source = restrict_sum(residual)
            if level + 1 == gathered:
                correction = cycle_whole(
                    gather_grid(coarse_source), whole_noise, whole_couplings, gathered
                )
                return own_window(correction, height // 2, width // 2, ring)
            coarse = run(level + 1, with_halo(coarse_source, HALO))
            return with_halo(coarse, ring)

        return level_split(source, noise, couplings, below)

    return run(0, split_inputs[0][0])


def solution(mesh):
    in_specs = (
        P(None, ("groups", "tiles"), ("band", "stokes")),
        P(None, ("groups", "tiles"), ("band", "stokes")),
        P(None, ("groups", "tiles"), ("band", "stokes")),
    )
    out_specs = P(None, ("groups", "tiles"), ("band", "stokes"))
    return jax.shard_map(
        on_device, mesh=mesh, in_specs=in_specs, out_specs=out_specs, check_vma=False
    )
```

```python
import jax
import jax.numpy as jnp
from jax import lax
from jax.sharding import PartitionSpec as P

LEVELS = 5
PRE = 2
POST = 2
COARSE_SWEEPS = 8

OMEGA = 0.8

ROWS = "tiles"
COLS = ("band", "stokes")
GRID = ("tiles", "band", "stokes")

HALO = PRE - 1 + POST
GATHER_PIXELS = 32768


def with_halo(cells, width):
    for axis, dim in ((ROWS, 1), (COLS, 2)):
        count = lax.axis_size(axis)
        ends = count - 1
        head = lax.slice_in_dim(cells, 0, width, axis=dim)
        tail = lax.slice_in_dim(cells, cells.shape[dim] - width, cells.shape[dim], axis=dim)
        cells = jnp.concatenate(
            [
                lax.ppermute(tail, axis, [(i, i + 1) for i in range(ends)]),
                cells,
                lax.ppermute(head, axis, [(i + 1, i) for i in range(ends)]),
            ],
            axis=dim,
        )
    return cells


def crop(x, k):
    if k == 0:
        return x
    return x[..., k:-k, k:-k]


HIGH = lax.Precision.HIGHEST


def pairs(n, pick=None):
    rows = lax.broadcasted_iota(jnp.int32, (n, n // 2), 0)
    cols = lax.broadcasted_iota(jnp.int32, (n, n // 2), 1)
    hit = (rows // 2 == cols) if pick is None else (rows == 2 * cols + pick)
    return hit.astype(jnp.float32)


def sum_rows(x, m):
    return jnp.einsum("...hw,hv->...vw", x, m, precision=HIGH)


def sum_cols(x, m):
    return jnp.einsum("...hw,wv->...hv", x, m, precision=HIGH)


def restrict_sum(x):
    return sum_cols(sum_rows(x, pairs(x.shape[-2])), pairs(x.shape[-1]))


def restrict_down(down):
    return sum_cols(sum_rows(down, pairs(down.shape[-2], 1)), pairs(down.shape[-1]))


def restrict_right(right):
    return sum_rows(sum_cols(right, pairs(right.shape[-1], 1)), pairs(right.shape[-2]))


def prolong(coarse):
    height, width = coarse.shape[-2] * 2, coarse.shape[-1] * 2
    taller = jnp.einsum("...vw,hv->...hw", coarse, pairs(height), precision=HIGH)
    return jnp.einsum("...hv,wv->...hw", taller, pairs(width), precision=HIGH)


def apply_planes(iterate, padded, noise, couplings):
    first = noise[0] * iterate[0] + noise[3] * iterate[1] + noise[4] * iterate[2]
    second = noise[3] * iterate[0] + noise[1] * iterate[1] + noise[5] * iterate[2]
    third = noise[4] * iterate[0] + noise[5] * iterate[1] + noise[2] * iterate[2]
    totals = couplings[0] + couplings[1] + couplings[2] + couplings[3]
    image = []
    for local, core, rim in zip((first, second, third), iterate, padded):
        neighbours = (
            couplings[0] * rim[2:, 1:-1]
            + couplings[1] * rim[:-2, 1:-1]
            + couplings[2] * rim[1:-1, 2:]
            + couplings[3] * rim[1:-1, :-2]
        )
        image.append(local + totals * core - neighbours)
    return image


def apply_ext(padded, noise, couplings):
    return apply_planes([p[1:-1, 1:-1] for p in padded], padded, noise, couplings)


def diagonal_of(noise, couplings):
    totals = couplings[0] + couplings[1] + couplings[2] + couplings[3]
    return [noise[k] + totals for k in range(3)]


def couplings_from(down, right):
    upward = jnp.pad(down, ((1, 0), (0, 0)))[:-1, :]
    leftward = jnp.pad(right, ((0, 0), (1, 0)))[:, :-1]
    return [down, upward, right, leftward]


def crops(planes, k):
    return [crop(p, k) for p in planes]


def smooth_whole(iterate, source, noise, couplings, diagonal):
    image = apply_planes(iterate, [jnp.pad(p, 1) for p in iterate], noise, couplings)
    return [i + OMEGA * (s - a) / d for i, s, a, d in zip(iterate, source, image, diagonal)]


def cycle_whole(source, noise, down, right, level_index):
    couplings = couplings_from(down, right)
    diagonal = diagonal_of(noise, couplings)
    iterate = [OMEGA * s / d for s, d in zip(source, diagonal)]
    if level_index == LEVELS - 1:
        for sweep_index in range(COARSE_SWEEPS - 1):
            iterate = smooth_whole(iterate, source, noise, couplings, diagonal)
        return iterate
    for sweep_index in range(PRE - 1):
        iterate = smooth_whole(iterate, source, noise, couplings, diagonal)
    image = apply_planes(iterate, [jnp.pad(p, 1) for p in iterate], noise, couplings)
    residual = [s - a for s, a in zip(source, image)]
    coarse = cycle_whole(
        [restrict_sum(r) for r in residual],
        [restrict_sum(n) for n in noise],
        restrict_down(down),
        restrict_right(right),
        level_index + 1,
    )
    iterate = [i + prolong(c) for i, c in zip(iterate, coarse)]
    for sweep_index in range(POST):
        iterate = smooth_whole(iterate, source, noise, couplings, diagonal)
    return iterate


def gather_grid(block):
    count_rows = lax.axis_size(ROWS)
    count_cols = lax.axis_size(COLS)
    planes, height, width = block.shape
    stacked = lax.all_gather(block, GRID, axis=0, tiled=False)
    stacked = stacked.reshape(count_rows, count_cols, planes, height, width)
    whole = stacked.transpose(2, 0, 3, 1, 4).reshape(planes, count_rows * height, count_cols * width)
    return [whole[k] for k in range(planes)]


def own_window(whole, height, width, ring):
    row = lax.axis_index(ROWS) * height
    col = lax.axis_index(COLS) * width
    padded = jnp.pad(whole, ring) if ring else whole
    return lax.dynamic_slice(padded, (row, col), (height + 2 * ring, width + 2 * ring))


def inside(height, width, ext):
    rows = lax.axis_index(ROWS) * height - ext + lax.broadcasted_iota(
        jnp.int32, (height + 2 * ext, width + 2 * ext), 0
    )
    cols = lax.axis_index(COLS) * width - ext + lax.broadcasted_iota(
        jnp.int32, (height + 2 * ext, width + 2 * ext), 1
    )
    return (
        (rows >= 0)
        & (rows < lax.axis_size(ROWS) * height)
        & (cols >= 0)
        & (cols < lax.axis_size(COLS) * width)
    )


def sweep_ext(iterate, source, noise, couplings, diagonal, mask):
    image = apply_ext(iterate, noise, couplings)
    new = [
        i[1:-1, 1:-1] + OMEGA * (s - a) / d for i, s, a, d in zip(iterate, source, image, diagonal)
    ]
    if mask is None:
        return new
    return [jnp.where(mask, n, 0.0) for n in new]


def level_split(source, noise, couplings, below):
    height = source[0].shape[0] - 2 * HALO
    width = source[0].shape[1] - 2 * HALO
    diagonal = diagonal_of(noise, couplings)
    ext = HALO
    mask = inside(height, width, ext)
    iterate = [jnp.where(mask, OMEGA * s / d, 0.0) for s, d in zip(source, diagonal)]
    for sweep_index in range(PRE - 1):
        ext -= 1
        cut = HALO - ext
        iterate = sweep_ext(
            iterate, crops(source, cut), crops(noise, cut), crops(couplings, cut),
            crops(diagonal, cut), inside(height, width, ext),
        )
    image = apply_ext(crops(iterate, ext - 1), crops(noise, HALO), crops(couplings, HALO))
    residual = [s - a for s, a in zip(crops(source, HALO), image)]
    coarse = below(residual)
    ring = (POST + 1) // 2
    iterate = [
        i + crop(prolong(c), 2 * ring - POST) for i, c in zip(crops(iterate, ext - POST), coarse)
    ]
    for sweep_index in range(POST):
        ext = POST - 1 - sweep_index
        cut = HALO - ext
        iterate = sweep_ext(
            iterate, crops(source, cut), crops(noise, cut), crops(couplings, cut),
            crops(diagonal, cut), inside(height, width, ext) if ext else None,
        )
    return iterate


def on_device(right_side, noise_block, edges):
    count_rows = lax.axis_size(ROWS)
    count_cols = lax.axis_size(COLS)
    height0, width0 = right_side.shape[1], right_side.shape[2]

    noises = [noise_block]
    downs = [edges[0]]
    rights = [edges[1]]
    for level in range(1, LEVELS):
        noises.append(restrict_sum(noises[-1]))
        downs.append(restrict_down(downs[-1]))
        rights.append(restrict_right(rights[-1]))

    gathered = LEVELS - 1
    for level in range(LEVELS):
        height, width = height0 >> level, width0 >> level
        whole = count_rows * height * count_cols * width
        if whole <= GATHER_PIXELS or height <= HALO or width <= HALO or level == LEVELS - 1:
            gathered = level
            break

    if gathered == 0:
        whole = gather_grid(jnp.concatenate([right_side, noise_block, edges]))
        correction = cycle_whole(whole[:3], whole[3:9], whole[9], whole[10], 0)
        return jnp.stack([own_window(c, height0, width0, 0) for c in correction])

    packed = gather_grid(
        jnp.concatenate([noises[gathered], downs[gathered][None], rights[gathered][None]])
    )
    whole_noise, whole_down, whole_right = packed[:6], packed[6], packed[7]
    split_inputs = []
    for level in range(gathered):
        parts = [noises[level], downs[level][None], rights[level][None]]
        if level == 0:
            parts = [right_side] + parts
        ringed = with_halo(jnp.concatenate(parts), HALO + 1)
        ringed = [ringed[k] for k in range(ringed.shape[0])]
        source = crops(ringed[:3], 1) if level == 0 else None
        if level == 0:
            ringed = ringed[3:]
        down, right = ringed[6], ringed[7]
        couplings = [down[1:-1, 1:-1], down[:-2, 1:-1], right[1:-1, 1:-1], right[1:-1, :-2]]
        split_inputs.append((source, crops(ringed[:6], 1), couplings))

    ring = (POST + 1) // 2

    def run(level, source):
        height, width = height0 >> level, width0 >> level
        _, noise, couplings = split_inputs[level]

        def below(residual):
            coarse_source = jnp.stack([restrict_sum(r) for r in residual])
            if level + 1 == gathered:
                correction = cycle_whole(
                    gather_grid(coarse_source), whole_noise, whole_down, whole_right, gathered
                )
                return [own_window(c, height // 2, width // 2, ring) for c in correction]
            coarse = run(level + 1, list(with_halo(coarse_source, HALO)))
            return list(with_halo(jnp.stack(coarse), ring))

        return level_split(source, noise, couplings, below)

    return jnp.stack(run(0, split_inputs[0][0]))


def solution(mesh):
    in_specs = (
        P(None, ("groups", "tiles"), ("band", "stokes")),
        P(None, ("groups", "tiles"), ("band", "stokes")),
        P(None, ("groups", "tiles"), ("band", "stokes")),
    )
    out_specs = P(None, ("groups", "tiles"), ("band", "stokes"))
    return jax.shard_map(
        on_device, mesh=mesh, in_specs=in_specs, out_specs=out_specs, check_vma=False
    )
```

```python
import jax
import jax.numpy as jnp
from jax import lax
from jax.sharding import PartitionSpec as P

LEVELS = 5
PRE = 2
POST = 2
COARSE_SWEEPS = 8

OMEGA = 0.8

ROWS = "tiles"
COLS = ("band", "stokes")
GRID = ("tiles", "band", "stokes")

HALO = PRE - 1 + POST
GATHER_PIXELS = 8192


def with_halo(cells, width):
    for axis, dim in ((ROWS, 1), (COLS, 2)):
        count = lax.axis_size(axis)
        ends = count - 1
        head = lax.slice_in_dim(cells, 0, width, axis=dim)
        tail = lax.slice_in_dim(cells, cells.shape[dim] - width, cells.shape[dim], axis=dim)
        cells = jnp.concatenate(
            [
                lax.ppermute(tail, axis, [(i, i + 1) for i in range(ends)]),
                cells,
                lax.ppermute(head, axis, [(i + 1, i) for i in range(ends)]),
            ],
            axis=dim,
        )
    return cells


def crop(x, k):
    if k == 0:
        return x
    return x[..., k:-k, k:-k]


HIGH = lax.Precision.HIGHEST


def pairs(n, pick=None):
    rows = lax.broadcasted_iota(jnp.int32, (n, n // 2), 0)
    cols = lax.broadcasted_iota(jnp.int32, (n, n // 2), 1)
    hit = (rows // 2 == cols) if pick is None else (rows == 2 * cols + pick)
    return hit.astype(jnp.float32)


def sum_rows(x, m):
    return jnp.einsum("...hw,hv->...vw", x, m, precision=HIGH)


def sum_cols(x, m):
    return jnp.einsum("...hw,wv->...hv", x, m, precision=HIGH)


def restrict_sum(x):
    return sum_cols(sum_rows(x, pairs(x.shape[-2])), pairs(x.shape[-1]))


def restrict_down(down):
    return sum_cols(sum_rows(down, pairs(down.shape[-2], 1)), pairs(down.shape[-1]))


def restrict_right(right):
    return sum_rows(sum_cols(right, pairs(right.shape[-1], 1)), pairs(right.shape[-2]))


def prolong(coarse):
    height, width = coarse.shape[-2] * 2, coarse.shape[-1] * 2
    taller = jnp.einsum("...vw,hv->...hw", coarse, pairs(height), precision=HIGH)
    return jnp.einsum("...hv,wv->...hw", taller, pairs(width), precision=HIGH)


def apply_planes(iterate, padded, noise, couplings):
    first = noise[0] * iterate[0] + noise[3] * iterate[1] + noise[4] * iterate[2]
    second = noise[3] * iterate[0] + noise[1] * iterate[1] + noise[5] * iterate[2]
    third = noise[4] * iterate[0] + noise[5] * iterate[1] + noise[2] * iterate[2]
    totals = couplings[0] + couplings[1] + couplings[2] + couplings[3]
    image = []
    for local, core, rim in zip((first, second, third), iterate, padded):
        neighbours = (
            couplings[0] * rim[2:, 1:-1]
            + couplings[1] * rim[:-2, 1:-1]
            + couplings[2] * rim[1:-1, 2:]
            + couplings[3] * rim[1:-1, :-2]
        )
        image.append(local + totals * core - neighbours)
    return image


def apply_ext(padded, noise, couplings):
    return apply_planes([p[1:-1, 1:-1] for p in padded], padded, noise, couplings)


def diagonal_of(noise, couplings):
    totals = couplings[0] + couplings[1] + couplings[2] + couplings[3]
    return [noise[k] + totals for k in range(3)]


def couplings_from(down, right):
    upward = jnp.pad(down, ((1, 0), (0, 0)))[:-1, :]
    leftward = jnp.pad(right, ((0, 0), (1, 0)))[:, :-1]
    return [down, upward, right, leftward]


def crops(planes, k):
    return [crop(p, k) for p in planes]


def smooth_whole(iterate, source, noise, couplings, diagonal):
    image = apply_planes(iterate, [jnp.pad(p, 1) for p in iterate], noise, couplings)
    return [i + OMEGA * (s - a) / d for i, s, a, d in zip(iterate, source, image, diagonal)]


def cycle_whole(source, noise, down, right, level_index):
    couplings = couplings_from(down, right)
    diagonal = diagonal_of(noise, couplings)
    iterate = [OMEGA * s / d for s, d in zip(source, diagonal)]
    if level_index == LEVELS - 1:
        for sweep_index in range(COARSE_SWEEPS - 1):
            iterate = smooth_whole(iterate, source, noise, couplings, diagonal)
        return iterate
    for sweep_index in range(PRE - 1):
        iterate = smooth_whole(iterate, source, noise, couplings, diagonal)
    image = apply_planes(iterate, [jnp.pad(p, 1) for p in iterate], noise, couplings)
    residual = [s - a for s, a in zip(source, image)]
    coarse = cycle_whole(
        [restrict_sum(r) for r in residual],
        [restrict_sum(n) for n in noise],
        restrict_down(down),
        restrict_right(right),
        level_index + 1,
    )
    iterate = [i + prolong(c) for i, c in zip(iterate, coarse)]
    for sweep_index in range(POST):
        iterate = smooth_whole(iterate, source, noise, couplings, diagonal)
    return iterate


def gather_grid(block):
    count_rows = lax.axis_size(ROWS)
    count_cols = lax.axis_size(COLS)
    planes, height, width = block.shape
    stacked = lax.all_gather(block, GRID, axis=0, tiled=False)
    stacked = stacked.reshape(count_rows, count_cols, planes, height, width)
    whole = stacked.transpose(2, 0, 3, 1, 4).reshape(planes, count_rows * height, count_cols * width)
    return [whole[k] for k in range(planes)]


def own_window(whole, height, width, ring):
    row = lax.axis_index(ROWS) * height
    col = lax.axis_index(COLS) * width
    padded = jnp.pad(whole, ring) if ring else whole
    return lax.dynamic_slice(padded, (row, col), (height + 2 * ring, width + 2 * ring))


def inside(height, width, ext):
    rows = lax.axis_index(ROWS) * height - ext + lax.broadcasted_iota(
        jnp.int32, (height + 2 * ext, width + 2 * ext), 0
    )
    cols = lax.axis_index(COLS) * width - ext + lax.broadcasted_iota(
        jnp.int32, (height + 2 * ext, width + 2 * ext), 1
    )
    return (
        (rows >= 0)
        & (rows < lax.axis_size(ROWS) * height)
        & (cols >= 0)
        & (cols < lax.axis_size(COLS) * width)
    )


def sweep_ext(iterate, source, noise, couplings, diagonal, mask):
    image = apply_ext(iterate, noise, couplings)
    new = [
        i[1:-1, 1:-1] + OMEGA * (s - a) / d for i, s, a, d in zip(iterate, source, image, diagonal)
    ]
    if mask is None:
        return new
    return [jnp.where(mask, n, 0.0) for n in new]


def level_split(source, noise, couplings, below):
    height = source[0].shape[0] - 2 * HALO
    width = source[0].shape[1] - 2 * HALO
    diagonal = diagonal_of(noise, couplings)
    ext = HALO
    mask = inside(height, width, ext)
    iterate = [jnp.where(mask, OMEGA * s / d, 0.0) for s, d in zip(source, diagonal)]
    for sweep_index in range(PRE - 1):
        ext -= 1
        cut = HALO - ext
        iterate = sweep_ext(
            iterate, crops(source, cut), crops(noise, cut), crops(couplings, cut),
            crops(diagonal, cut), inside(height, width, ext),
        )
    image = apply_ext(crops(iterate, ext - 1), crops(noise, HALO), crops(couplings, HALO))
    residual = [s - a for s, a in zip(crops(source, HALO), image)]
    coarse = below(residual)
    ring = (POST + 1) // 2
    iterate = [
        i + crop(prolong(c), 2 * ring - POST) for i, c in zip(crops(iterate, ext - POST), coarse)
    ]
    for sweep_index in range(POST):
        ext = POST - 1 - sweep_index
        cut = HALO - ext
        iterate = sweep_ext(
            iterate, crops(source, cut), crops(noise, cut), crops(couplings, cut),
            crops(diagonal, cut), inside(height, width, ext) if ext else None,
        )
    return iterate


def on_device(right_side, noise_block, edges):
    count_rows = lax.axis_size(ROWS)
    count_cols = lax.axis_size(COLS)
    height0, width0 = right_side.shape[1], right_side.shape[2]

    noises = [noise_block]
    downs = [edges[0]]
    rights = [edges[1]]
    for level in range(1, LEVELS):
        noises.append(restrict_sum(noises[-1]))
        downs.append(restrict_down(downs[-1]))
        rights.append(restrict_right(rights[-1]))

    gathered = LEVELS - 1
    for level in range(LEVELS):
        height, width = height0 >> level, width0 >> level
        whole = count_rows * height * count_cols * width
        if whole <= GATHER_PIXELS or height <= HALO or width <= HALO or level == LEVELS - 1:
            gathered = level
            break

    if gathered == 0:
        whole = gather_grid(jnp.concatenate([right_side, noise_block, edges]))
        correction = cycle_whole(whole[:3], whole[3:9], whole[9], whole[10], 0)
        return jnp.stack([own_window(c, height0, width0, 0) for c in correction])

    packed = gather_grid(
        jnp.concatenate([noises[gathered], downs[gathered][None], rights[gathered][None]])
    )
    whole_noise, whole_down, whole_right = packed[:6], packed[6], packed[7]
    split_inputs = []
    for level in range(gathered):
        parts = [noises[level], downs[level][None], rights[level][None]]
        if level == 0:
            parts = [right_side] + parts
        ringed = with_halo(jnp.concatenate(parts), HALO + 1)
        ringed = [ringed[k] for k in range(ringed.shape[0])]
        source = crops(ringed[:3], 1) if level == 0 else None
        if level == 0:
            ringed = ringed[3:]
        down, right = ringed[6], ringed[7]
        couplings = [down[1:-1, 1:-1], down[:-2, 1:-1], right[1:-1, 1:-1], right[1:-1, :-2]]
        split_inputs.append((source, crops(ringed[:6], 1), couplings))

    ring = (POST + 1) // 2

    def run(level, source):
        height, width = height0 >> level, width0 >> level
        _, noise, couplings = split_inputs[level]

        def below(residual):
            coarse_source = jnp.stack([restrict_sum(r) for r in residual])
            if level + 1 == gathered:
                correction = cycle_whole(
                    gather_grid(coarse_source), whole_noise, whole_down, whole_right, gathered
                )
                return [own_window(c, height // 2, width // 2, ring) for c in correction]
            coarse = run(level + 1, list(with_halo(coarse_source, HALO)))
            return list(with_halo(jnp.stack(coarse), ring))

        return level_split(source, noise, couplings, below)

    return jnp.stack(run(0, split_inputs[0][0]))


def solution(mesh):
    in_specs = (
        P(None, ("groups", "tiles"), ("band", "stokes")),
        P(None, ("groups", "tiles"), ("band", "stokes")),
        P(None, ("groups", "tiles"), ("band", "stokes")),
    )
    out_specs = P(None, ("groups", "tiles"), ("band", "stokes"))
    return jax.shard_map(
        on_device, mesh=mesh, in_specs=in_specs, out_specs=out_specs, check_vma=False
    )
```

```python
import jax
import jax.numpy as jnp
from jax import lax
from jax.sharding import PartitionSpec as P

LEVELS = 5
PRE = 2
POST = 2
COARSE_SWEEPS = 8

OMEGA = 0.8

ROWS = "tiles"
COLS = ("band", "stokes")
GRID = ("tiles", "band", "stokes")

HALO = PRE - 1 + POST
GATHER_PIXELS = 32768


def with_halo(cells, width):
    for axis, dim in ((ROWS, 1), (COLS, 2)):
        count = lax.axis_size(axis)
        ends = count - 1
        head = lax.slice_in_dim(cells, 0, width, axis=dim)
        tail = lax.slice_in_dim(cells, cells.shape[dim] - width, cells.shape[dim], axis=dim)
        cells = jnp.concatenate(
            [
                lax.ppermute(tail, axis, [(i, i + 1) for i in range(ends)]),
                cells,
                lax.ppermute(head, axis, [(i + 1, i) for i in range(ends)]),
            ],
            axis=dim,
        )
    return cells


def crop(x, k):
    if k == 0:
        return x
    return x[..., k:-k, k:-k]


HIGH = lax.Precision.HIGHEST


def pairs(n, pick=None):
    rows = lax.broadcasted_iota(jnp.int32, (n, n // 2), 0)
    cols = lax.broadcasted_iota(jnp.int32, (n, n // 2), 1)
    hit = (rows // 2 == cols) if pick is None else (rows == 2 * cols + pick)
    return hit.astype(jnp.float32)


def sum_rows(x, m):
    return jnp.einsum("...hw,hv->...vw", x, m, precision=HIGH)


def sum_cols(x, m):
    return jnp.einsum("...hw,wv->...hv", x, m, precision=HIGH)


def restrict_sum(x):
    return sum_cols(sum_rows(x, pairs(x.shape[-2])), pairs(x.shape[-1]))


def restrict_down(down):
    return sum_cols(sum_rows(down, pairs(down.shape[-2], 1)), pairs(down.shape[-1]))


def restrict_right(right):
    return sum_rows(sum_cols(right, pairs(right.shape[-1], 1)), pairs(right.shape[-2]))


def prolong(coarse):
    height, width = coarse.shape[-2] * 2, coarse.shape[-1] * 2
    taller = jnp.einsum("...vw,hv->...hw", coarse, pairs(height), precision=HIGH)
    return jnp.einsum("...hv,wv->...hw", taller, pairs(width), precision=HIGH)


def apply_planes(iterate, padded, noise, couplings):
    first = noise[0] * iterate[0] + noise[3] * iterate[1] + noise[4] * iterate[2]
    second = noise[3] * iterate[0] + noise[1] * iterate[1] + noise[5] * iterate[2]
    third = noise[4] * iterate[0] + noise[5] * iterate[1] + noise[2] * iterate[2]
    totals = couplings[0] + couplings[1] + couplings[2] + couplings[3]
    image = []
    for local, core, rim in zip((first, second, third), iterate, padded):
        neighbours = (
            couplings[0] * rim[2:, 1:-1]
            + couplings[1] * rim[:-2, 1:-1]
            + couplings[2] * rim[1:-1, 2:]
            + couplings[3] * rim[1:-1, :-2]
        )
        image.append(local + totals * core - neighbours)
    return image


def apply_ext(padded, noise, couplings):
    return apply_planes([p[1:-1, 1:-1] for p in padded], padded, noise, couplings)


def diagonal_of(noise, couplings):
    totals = couplings[0] + couplings[1] + couplings[2] + couplings[3]
    return [noise[k] + totals for k in range(3)]


def couplings_from(down, right):
    upward = jnp.pad(down, ((1, 0), (0, 0)))[:-1, :]
    leftward = jnp.pad(right, ((0, 0), (1, 0)))[:, :-1]
    return [down, upward, right, leftward]


def crops(planes, k):
    return [crop(p, k) for p in planes]


def smooth_whole(iterate, source, noise, couplings, diagonal):
    image = apply_planes(iterate, [jnp.pad(p, 1) for p in iterate], noise, couplings)
    return [i + OMEGA * (s - a) / d for i, s, a, d in zip(iterate, source, image, diagonal)]


def cycle_whole(source, hierarchy, level_index):
    noise, down, right = hierarchy[0]
    couplings = couplings_from(down, right)
    diagonal = diagonal_of(noise, couplings)
    iterate = [OMEGA * s / d for s, d in zip(source, diagonal)]
    if level_index == LEVELS - 1:
        for sweep_index in range(COARSE_SWEEPS - 1):
            iterate = smooth_whole(iterate, source, noise, couplings, diagonal)
        return iterate
    for sweep_index in range(PRE - 1):
        iterate = smooth_whole(iterate, source, noise, couplings, diagonal)
    image = apply_planes(iterate, [jnp.pad(p, 1) for p in iterate], noise, couplings)
    residual = restrict_sum(jnp.stack([s - a for s, a in zip(source, image)]))
    coarse = prolong(
        jnp.stack(cycle_whole([residual[k] for k in range(3)], hierarchy[1:], level_index + 1))
    )
    iterate = [iterate[k] + coarse[k] for k in range(3)]
    for sweep_index in range(POST):
        iterate = smooth_whole(iterate, source, noise, couplings, diagonal)
    return iterate


def gather_grid(block):
    return gather_grids([block])[0]


def gather_grids(blocks):
    count_rows = lax.axis_size(ROWS)
    count_cols = lax.axis_size(COLS)
    planes = blocks[0].shape[0]
    flat = jnp.concatenate([b.reshape(planes, -1) for b in blocks], axis=1)
    stacked = lax.all_gather(flat, GRID, axis=0, tiled=False)
    grids = []
    offset = 0
    for b in blocks:
        _, height, width = b.shape
        part = stacked[:, :, offset:offset + height * width]
        offset += height * width
        part = part.reshape(count_rows, count_cols, planes, height, width)
        whole = part.transpose(2, 0, 3, 1, 4).reshape(
            planes, count_rows * height, count_cols * width
        )
        grids.append([whole[k] for k in range(planes)])
    return grids


def own_window(whole, height, width, ring):
    row = lax.axis_index(ROWS) * height
    col = lax.axis_index(COLS) * width
    padded = jnp.pad(whole, ring) if ring else whole
    return lax.dynamic_slice(padded, (row, col), (height + 2 * ring, width + 2 * ring))


def inside(height, width, ext):
    rows = lax.axis_index(ROWS) * height - ext + lax.broadcasted_iota(
        jnp.int32, (height + 2 * ext, width + 2 * ext), 0
    )
    cols = lax.axis_index(COLS) * width - ext + lax.broadcasted_iota(
        jnp.int32, (height + 2 * ext, width + 2 * ext), 1
    )
    return (
        (rows >= 0)
        & (rows < lax.axis_size(ROWS) * height)
        & (cols >= 0)
        & (cols < lax.axis_size(COLS) * width)
    )


def sweep_ext(iterate, source, noise, couplings, diagonal, mask):
    image = apply_ext(iterate, noise, couplings)
    new = [
        i[1:-1, 1:-1] + OMEGA * (s - a) / d for i, s, a, d in zip(iterate, source, image, diagonal)
    ]
    if mask is None:
        return new
    return [jnp.where(mask, n, 0.0) for n in new]


def level_split(source, noise, couplings, below):
    height = source[0].shape[0] - 2 * HALO
    width = source[0].shape[1] - 2 * HALO
    diagonal = diagonal_of(noise, couplings)
    ext = HALO
    mask = inside(height, width, ext)
    iterate = [jnp.where(mask, OMEGA * s / d, 0.0) for s, d in zip(source, diagonal)]
    for sweep_index in range(PRE - 1):
        ext -= 1
        cut = HALO - ext
        iterate = sweep_ext(
            iterate, crops(source, cut), crops(noise, cut), crops(couplings, cut),
            crops(diagonal, cut), inside(height, width, ext),
        )
    image = apply_ext(crops(iterate, ext - 1), crops(noise, HALO), crops(couplings, HALO))
    residual = [s - a for s, a in zip(crops(source, HALO), image)]
    coarse = below(residual)
    ring = (POST + 1) // 2
    iterate = [
        i + crop(prolong(c), 2 * ring - POST) for i, c in zip(crops(iterate, ext - POST), coarse)
    ]
    for sweep_index in range(POST):
        ext = POST - 1 - sweep_index
        cut = HALO - ext
        iterate = sweep_ext(
            iterate, crops(source, cut), crops(noise, cut), crops(couplings, cut),
            crops(diagonal, cut), inside(height, width, ext) if ext else None,
        )
    return iterate


def on_device(right_side, noise_block, edges):
    count_rows = lax.axis_size(ROWS)
    count_cols = lax.axis_size(COLS)
    height0, width0 = right_side.shape[1], right_side.shape[2]

    noises = [noise_block]
    downs = [edges[0]]
    rights = [edges[1]]
    for level in range(1, LEVELS):
        noises.append(restrict_sum(noises[-1]))
        downs.append(restrict_down(downs[-1]))
        rights.append(restrict_right(rights[-1]))

    gathered = LEVELS - 1
    for level in range(LEVELS):
        height, width = height0 >> level, width0 >> level
        whole = count_rows * height * count_cols * width
        if whole <= GATHER_PIXELS or height <= HALO or width <= HALO or level == LEVELS - 1:
            gathered = level
            break

    if gathered == 0:
        packed = gather_grids(
            [jnp.concatenate([noises[l], downs[l][None], rights[l][None]]) for l in range(LEVELS)]
        )
        hierarchy = [(p[:6], p[6], p[7]) for p in packed]
        correction = cycle_whole(gather_grid(right_side), hierarchy, 0)
        return jnp.stack([own_window(c, height0, width0, 0) for c in correction])

    packed = gather_grids(
        [
            jnp.concatenate([noises[l], downs[l][None], rights[l][None]])
            for l in range(gathered, LEVELS)
        ]
    )
    hierarchy = [(p[:6], p[6], p[7]) for p in packed]
    split_inputs = []
    for level in range(gathered):
        parts = [noises[level], downs[level][None], rights[level][None]]
        if level == 0:
            parts = [right_side] + parts
        ringed = with_halo(jnp.concatenate(parts), HALO + 1)
        ringed = [ringed[k] for k in range(ringed.shape[0])]
        source = crops(ringed[:3], 1) if level == 0 else None
        if level == 0:
            ringed = ringed[3:]
        down, right = ringed[6], ringed[7]
        couplings = [down[1:-1, 1:-1], down[:-2, 1:-1], right[1:-1, 1:-1], right[1:-1, :-2]]
        split_inputs.append((source, crops(ringed[:6], 1), couplings))

    ring = (POST + 1) // 2

    def run(level, source):
        height, width = height0 >> level, width0 >> level
        _, noise, couplings = split_inputs[level]

        def below(residual):
            coarse_source = restrict_sum(jnp.stack(residual))
            if level + 1 == gathered:
                correction = cycle_whole(gather_grid(coarse_source), hierarchy, gathered)
                return [own_window(c, height // 2, width // 2, ring) for c in correction]
            coarse = run(level + 1, list(with_halo(coarse_source, HALO)))
            return list(with_halo(jnp.stack(coarse), ring))

        return level_split(source, noise, couplings, below)

    return jnp.stack(run(0, split_inputs[0][0]))


def solution(mesh):
    in_specs = (
        P(None, ("groups", "tiles"), ("band", "stokes")),
        P(None, ("groups", "tiles"), ("band", "stokes")),
        P(None, ("groups", "tiles"), ("band", "stokes")),
    )
    out_specs = P(None, ("groups", "tiles"), ("band", "stokes"))
    return jax.shard_map(
        on_device, mesh=mesh, in_specs=in_specs, out_specs=out_specs, check_vma=False
    )
```

```python
import jax
import jax.numpy as jnp
from jax import lax
from jax.sharding import PartitionSpec as P

LEVELS = 5
PRE = 2
POST = 2
COARSE_SWEEPS = 8

OMEGA = 0.8

ROWS = "tiles"
COLS = ("band", "stokes")
GRID = ("tiles", "band", "stokes")

HALO = PRE - 1 + POST
GATHER_PIXELS = 32768


def with_halo(cells, width):
    for axis, dim in ((ROWS, 1), (COLS, 2)):
        count = lax.axis_size(axis)
        ends = count - 1
        head = lax.slice_in_dim(cells, 0, width, axis=dim)
        tail = lax.slice_in_dim(cells, cells.shape[dim] - width, cells.shape[dim], axis=dim)
        cells = jnp.concatenate(
            [
                lax.ppermute(tail, axis, [(i, i + 1) for i in range(ends)]),
                cells,
                lax.ppermute(head, axis, [(i + 1, i) for i in range(ends)]),
            ],
            axis=dim,
        )
    return cells


def crop(x, k):
    if k == 0:
        return x
    return x[..., k:-k, k:-k]


HIGH = lax.Precision.HIGHEST


def pairs(n, pick=None):
    rows = lax.broadcasted_iota(jnp.int32, (n, n // 2), 0)
    cols = lax.broadcasted_iota(jnp.int32, (n, n // 2), 1)
    hit = (rows // 2 == cols) if pick is None else (rows == 2 * cols + pick)
    return hit.astype(jnp.float32)


def sum_rows(x, m):
    return jnp.einsum("...hw,hv->...vw", x, m, precision=HIGH)


def sum_cols(x, m):
    return jnp.einsum("...hw,wv->...hv", x, m, precision=HIGH)


def restrict_sum(x):
    return sum_cols(sum_rows(x, pairs(x.shape[-2])), pairs(x.shape[-1]))


def restrict_down(down):
    return sum_cols(sum_rows(down, pairs(down.shape[-2], 1)), pairs(down.shape[-1]))


def restrict_right(right):
    return sum_rows(sum_cols(right, pairs(right.shape[-1], 1)), pairs(right.shape[-2]))


def prolong(coarse):
    height, width = coarse.shape[-2] * 2, coarse.shape[-1] * 2
    taller = jnp.einsum("...vw,hv->...hw", coarse, pairs(height), precision=HIGH)
    return jnp.einsum("...hv,wv->...hw", taller, pairs(width), precision=HIGH)


def apply_planes(iterate, padded, noise, couplings):
    first = noise[0] * iterate[0] + noise[3] * iterate[1] + noise[4] * iterate[2]
    second = noise[3] * iterate[0] + noise[1] * iterate[1] + noise[5] * iterate[2]
    third = noise[4] * iterate[0] + noise[5] * iterate[1] + noise[2] * iterate[2]
    totals = couplings[0] + couplings[1] + couplings[2] + couplings[3]
    image = []
    for local, core, rim in zip((first, second, third), iterate, padded):
        neighbours = (
            couplings[0] * rim[2:, 1:-1]
            + couplings[1] * rim[:-2, 1:-1]
            + couplings[2] * rim[1:-1, 2:]
            + couplings[3] * rim[1:-1, :-2]
        )
        image.append(local + totals * core - neighbours)
    return image


def apply_ext(padded, noise, couplings):
    return apply_planes([p[1:-1, 1:-1] for p in padded], padded, noise, couplings)


def diagonal_of(noise, couplings):
    totals = couplings[0] + couplings[1] + couplings[2] + couplings[3]
    return [noise[k] + totals for k in range(3)]


def couplings_from(down, right):
    upward = jnp.pad(down, ((1, 0), (0, 0)))[:-1, :]
    leftward = jnp.pad(right, ((0, 0), (1, 0)))[:, :-1]
    return [down, upward, right, leftward]


def crops(planes, k):
    return [crop(p, k) for p in planes]


def smooth_whole(iterate, source, noise, couplings, diagonal):
    image = apply_planes(iterate, [jnp.pad(p, 1) for p in iterate], noise, couplings)
    return [i + OMEGA * (s - a) / d for i, s, a, d in zip(iterate, source, image, diagonal)]


def cycle_whole(source, hierarchy, level_index):
    noise, down, right = hierarchy[0]
    couplings = couplings_from(down, right)
    diagonal = diagonal_of(noise, couplings)
    iterate = [OMEGA * s / d for s, d in zip(source, diagonal)]
    if level_index == LEVELS - 1:
        for sweep_index in range(COARSE_SWEEPS - 1):
            iterate = smooth_whole(iterate, source, noise, couplings, diagonal)
        return iterate
    for sweep_index in range(PRE - 1):
        iterate = smooth_whole(iterate, source, noise, couplings, diagonal)
    image = apply_planes(iterate, [jnp.pad(p, 1) for p in iterate], noise, couplings)
    residual = restrict_sum(jnp.stack([s - a for s, a in zip(source, image)]))
    coarse = prolong(
        jnp.stack(cycle_whole([residual[k] for k in range(3)], hierarchy[1:], level_index + 1))
    )
    iterate = [iterate[k] + coarse[k] for k in range(3)]
    for sweep_index in range(POST):
        iterate = smooth_whole(iterate, source, noise, couplings, diagonal)
    return iterate


def gather_grid(block):
    return gather_grids([block])[0]


def gather_axis(x, axis):
    count = lax.axis_size(axis)
    me = lax.axis_index(axis)
    pieces = [x] + [
        lax.ppermute(x, axis, [(i, (i + k) % count) for i in range(count)]) for k in range(1, count)
    ]
    order = (me - jnp.arange(count)) % count
    return jnp.take(jnp.stack(pieces), order, axis=0, mode="clip")


def gather_grids(blocks):
    count_rows = lax.axis_size(ROWS)
    count_cols = lax.axis_size(COLS)
    planes = blocks[0].shape[0]
    flat = jnp.concatenate([b.reshape(planes, -1) for b in blocks], axis=1)
    stacked = gather_axis(gather_axis(flat, COLS), ROWS)
    stacked = stacked.reshape((count_rows * count_cols,) + flat.shape)
    grids = []
    offset = 0
    for b in blocks:
        _, height, width = b.shape
        part = stacked[:, :, offset:offset + height * width]
        offset += height * width
        part = part.reshape(count_rows, count_cols, planes, height, width)
        whole = part.transpose(2, 0, 3, 1, 4).reshape(
            planes, count_rows * height, count_cols * width
        )
        grids.append([whole[k] for k in range(planes)])
    return grids


def own_window(whole, height, width, ring):
    row = lax.axis_index(ROWS) * height
    col = lax.axis_index(COLS) * width
    padded = jnp.pad(whole, ring) if ring else whole
    return lax.dynamic_slice(padded, (row, col), (height + 2 * ring, width + 2 * ring))


def inside(height, width, ext):
    rows = lax.axis_index(ROWS) * height - ext + lax.broadcasted_iota(
        jnp.int32, (height + 2 * ext, width + 2 * ext), 0
    )
    cols = lax.axis_index(COLS) * width - ext + lax.broadcasted_iota(
        jnp.int32, (height + 2 * ext, width + 2 * ext), 1
    )
    return (
        (rows >= 0)
        & (rows < lax.axis_size(ROWS) * height)
        & (cols >= 0)
        & (cols < lax.axis_size(COLS) * width)
    )


def sweep_ext(iterate, source, noise, couplings, diagonal, mask):
    image = apply_ext(iterate, noise, couplings)
    new = [
        i[1:-1, 1:-1] + OMEGA * (s - a) / d for i, s, a, d in zip(iterate, source, image, diagonal)
    ]
    if mask is None:
        return new
    return [jnp.where(mask, n, 0.0) for n in new]


def level_split(source, noise, couplings, below):
    height = source[0].shape[0] - 2 * HALO
    width = source[0].shape[1] - 2 * HALO
    diagonal = diagonal_of(noise, couplings)
    ext = HALO
    mask = inside(height, width, ext)
    iterate = [jnp.where(mask, OMEGA * s / d, 0.0) for s, d in zip(source, diagonal)]
    for sweep_index in range(PRE - 1):
        ext -= 1
        cut = HALO - ext
        iterate = sweep_ext(
            iterate, crops(source, cut), crops(noise, cut), crops(couplings, cut),
            crops(diagonal, cut), inside(height, width, ext),
        )
    image = apply_ext(crops(iterate, ext - 1), crops(noise, HALO), crops(couplings, HALO))
    residual = [s - a for s, a in zip(crops(source, HALO), image)]
    coarse = below(residual)
    ring = (POST + 1) // 2
    iterate = [
        i + crop(prolong(c), 2 * ring - POST) for i, c in zip(crops(iterate, ext - POST), coarse)
    ]
    for sweep_index in range(POST):
        ext = POST - 1 - sweep_index
        cut = HALO - ext
        iterate = sweep_ext(
            iterate, crops(source, cut), crops(noise, cut), crops(couplings, cut),
            crops(diagonal, cut), inside(height, width, ext) if ext else None,
        )
    return iterate


def on_device(right_side, noise_block, edges):
    count_rows = lax.axis_size(ROWS)
    count_cols = lax.axis_size(COLS)
    height0, width0 = right_side.shape[1], right_side.shape[2]

    noises = [noise_block]
    downs = [edges[0]]
    rights = [edges[1]]
    for level in range(1, LEVELS):
        noises.append(restrict_sum(noises[-1]))
        downs.append(restrict_down(downs[-1]))
        rights.append(restrict_right(rights[-1]))

    gathered = LEVELS - 1
    for level in range(LEVELS):
        height, width = height0 >> level, width0 >> level
        whole = count_rows * height * count_cols * width
        if whole <= GATHER_PIXELS or height <= HALO or width <= HALO or level == LEVELS - 1:
            gathered = level
            break

    if gathered == 0:
        packed = gather_grids(
            [jnp.concatenate([noises[l], downs[l][None], rights[l][None]]) for l in range(LEVELS)]
        )
        hierarchy = [(p[:6], p[6], p[7]) for p in packed]
        correction = cycle_whole(gather_grid(right_side), hierarchy, 0)
        return jnp.stack([own_window(c, height0, width0, 0) for c in correction])

    packed = gather_grids(
        [
            jnp.concatenate([noises[l], downs[l][None], rights[l][None]])
            for l in range(gathered, LEVELS)
        ]
    )
    hierarchy = [(p[:6], p[6], p[7]) for p in packed]
    split_inputs = []
    for level in range(gathered):
        parts = [noises[level], downs[level][None], rights[level][None]]
        if level == 0:
            parts = [right_side] + parts
        ringed = with_halo(jnp.concatenate(parts), HALO + 1)
        ringed = [ringed[k] for k in range(ringed.shape[0])]
        source = crops(ringed[:3], 1) if level == 0 else None
        if level == 0:
            ringed = ringed[3:]
        down, right = ringed[6], ringed[7]
        couplings = [down[1:-1, 1:-1], down[:-2, 1:-1], right[1:-1, 1:-1], right[1:-1, :-2]]
        split_inputs.append((source, crops(ringed[:6], 1), couplings))

    ring = (POST + 1) // 2

    def run(level, source):
        height, width = height0 >> level, width0 >> level
        _, noise, couplings = split_inputs[level]

        def below(residual):
            coarse_source = restrict_sum(jnp.stack(residual))
            if level + 1 == gathered:
                correction = cycle_whole(gather_grid(coarse_source), hierarchy, gathered)
                return [own_window(c, height // 2, width // 2, ring) for c in correction]
            coarse = run(level + 1, list(with_halo(coarse_source, HALO)))
            return list(with_halo(jnp.stack(coarse), ring))

        return level_split(source, noise, couplings, below)

    return jnp.stack(run(0, split_inputs[0][0]))


def solution(mesh):
    in_specs = (
        P(None, ("groups", "tiles"), ("band", "stokes")),
        P(None, ("groups", "tiles"), ("band", "stokes")),
        P(None, ("groups", "tiles"), ("band", "stokes")),
    )
    out_specs = P(None, ("groups", "tiles"), ("band", "stokes"))
    return jax.shard_map(
        on_device, mesh=mesh, in_specs=in_specs, out_specs=out_specs, check_vma=False
    )
```

```python
import jax
import jax.numpy as jnp
from jax import lax
from jax.sharding import PartitionSpec as P

LEVELS = 5
PRE = 2
POST = 2
COARSE_SWEEPS = 8

OMEGA = 0.8

ROWS = "tiles"
COLS = ("band", "stokes")
GRID = ("tiles", "band", "stokes")

HALO = PRE - 1 + POST
GATHER_PIXELS = 32768


def with_halo(cells, width):
    for axis, dim in ((ROWS, 1), (COLS, 2)):
        count = lax.axis_size(axis)
        ends = count - 1
        head = lax.slice_in_dim(cells, 0, width, axis=dim)
        tail = lax.slice_in_dim(cells, cells.shape[dim] - width, cells.shape[dim], axis=dim)
        cells = jnp.concatenate(
            [
                lax.ppermute(tail, axis, [(i, i + 1) for i in range(ends)]),
                cells,
                lax.ppermute(head, axis, [(i + 1, i) for i in range(ends)]),
            ],
            axis=dim,
        )
    return cells


def crop(x, k):
    if k == 0:
        return x
    return x[..., k:-k, k:-k]


HIGH = lax.Precision.HIGHEST


def pairs(n, pick=None):
    rows = lax.broadcasted_iota(jnp.int32, (n, n // 2), 0)
    cols = lax.broadcasted_iota(jnp.int32, (n, n // 2), 1)
    hit = (rows // 2 == cols) if pick is None else (rows == 2 * cols + pick)
    return hit.astype(jnp.float32)


def sum_rows(x, m):
    return jnp.einsum("...hw,hv->...vw", x, m, precision=HIGH)


def sum_cols(x, m):
    return jnp.einsum("...hw,wv->...hv", x, m, precision=HIGH)


def restrict_sum(x):
    return sum_cols(sum_rows(x, pairs(x.shape[-2])), pairs(x.shape[-1]))


def restrict_down(down):
    return sum_cols(sum_rows(down, pairs(down.shape[-2], 1)), pairs(down.shape[-1]))


def restrict_right(right):
    return sum_rows(sum_cols(right, pairs(right.shape[-1], 1)), pairs(right.shape[-2]))


def prolong(coarse):
    height, width = coarse.shape[-2] * 2, coarse.shape[-1] * 2
    taller = jnp.einsum("...vw,hv->...hw", coarse, pairs(height), precision=HIGH)
    return jnp.einsum("...hv,wv->...hw", taller, pairs(width), precision=HIGH)


def apply_planes(iterate, padded, noise, couplings):
    first = noise[0] * iterate[0] + noise[3] * iterate[1] + noise[4] * iterate[2]
    second = noise[3] * iterate[0] + noise[1] * iterate[1] + noise[5] * iterate[2]
    third = noise[4] * iterate[0] + noise[5] * iterate[1] + noise[2] * iterate[2]
    totals = couplings[0] + couplings[1] + couplings[2] + couplings[3]
    image = []
    for local, core, rim in zip((first, second, third), iterate, padded):
        neighbours = (
            couplings[0] * rim[2:, 1:-1]
            + couplings[1] * rim[:-2, 1:-1]
            + couplings[2] * rim[1:-1, 2:]
            + couplings[3] * rim[1:-1, :-2]
        )
        image.append(local + totals * core - neighbours)
    return image


def apply_ext(padded, noise, couplings):
    return apply_planes([p[1:-1, 1:-1] for p in padded], padded, noise, couplings)


def diagonal_of(noise, couplings):
    totals = couplings[0] + couplings[1] + couplings[2] + couplings[3]
    return [noise[k] + totals for k in range(3)]


def couplings_from(down, right):
    upward = jnp.pad(down, ((1, 0), (0, 0)))[:-1, :]
    leftward = jnp.pad(right, ((0, 0), (1, 0)))[:, :-1]
    return [down, upward, right, leftward]


def crops(planes, k):
    return [crop(p, k) for p in planes]


def smooth_whole(iterate, source, noise, couplings, diagonal):
    image = apply_planes(iterate, [jnp.pad(p, 1) for p in iterate], noise, couplings)
    return [i + OMEGA * (s - a) / d for i, s, a, d in zip(iterate, source, image, diagonal)]


def cycle_whole(source, hierarchy, level_index):
    noise, down, right = hierarchy[0]
    couplings = couplings_from(down, right)
    diagonal = diagonal_of(noise, couplings)
    iterate = [OMEGA * s / d for s, d in zip(source, diagonal)]
    if level_index == LEVELS - 1:
        for sweep_index in range(COARSE_SWEEPS - 1):
            iterate = smooth_whole(iterate, source, noise, couplings, diagonal)
        return iterate
    for sweep_index in range(PRE - 1):
        iterate = smooth_whole(iterate, source, noise, couplings, diagonal)
    image = apply_planes(iterate, [jnp.pad(p, 1) for p in iterate], noise, couplings)
    residual = restrict_sum(jnp.stack([s - a for s, a in zip(source, image)]))
    coarse = prolong(
        jnp.stack(cycle_whole([residual[k] for k in range(3)], hierarchy[1:], level_index + 1))
    )
    iterate = [iterate[k] + coarse[k] for k in range(3)]
    for sweep_index in range(POST):
        iterate = smooth_whole(iterate, source, noise, couplings, diagonal)
    return iterate


def gather_grid(block):
    return gather_grids([block])[0]


def gather_grids(blocks):
    count_rows = lax.axis_size(ROWS)
    count_cols = lax.axis_size(COLS)
    planes = blocks[0].shape[0]
    runs = [-(-b.shape[1] * b.shape[2] // 128) * 128 for b in blocks]
    flat = jnp.concatenate(
        [
            jnp.pad(b.reshape(planes, -1), ((0, 0), (0, run - b.shape[1] * b.shape[2])))
            for b, run in zip(blocks, runs)
        ],
        axis=1,
    )
    stacked = lax.all_gather(flat, GRID, axis=0, tiled=False)
    grids = []
    offset = 0
    for b, run in zip(blocks, runs):
        _, height, width = b.shape
        part = stacked[:, :, offset:offset + height * width]
        offset += run
        part = part.reshape(count_rows, count_cols, planes, height, width)
        whole = part.transpose(2, 0, 3, 1, 4).reshape(
            planes, count_rows * height, count_cols * width
        )
        grids.append([whole[k] for k in range(planes)])
    return grids


def own_window(whole, height, width, ring):
    row = lax.axis_index(ROWS) * height
    col = lax.axis_index(COLS) * width
    padded = jnp.pad(whole, ring) if ring else whole
    return lax.dynamic_slice(padded, (row, col), (height + 2 * ring, width + 2 * ring))


def inside(height, width, ext):
    rows = lax.axis_index(ROWS) * height - ext + lax.broadcasted_iota(
        jnp.int32, (height + 2 * ext, width + 2 * ext), 0
    )
    cols = lax.axis_index(COLS) * width - ext + lax.broadcasted_iota(
        jnp.int32, (height + 2 * ext, width + 2 * ext), 1
    )
    return (
        (rows >= 0)
        & (rows < lax.axis_size(ROWS) * height)
        & (cols >= 0)
        & (cols < lax.axis_size(COLS) * width)
    )


def sweep_ext(iterate, source, noise, couplings, diagonal, mask):
    image = apply_ext(iterate, noise, couplings)
    new = [
        i[1:-1, 1:-1] + OMEGA * (s - a) / d for i, s, a, d in zip(iterate, source, image, diagonal)
    ]
    if mask is None:
        return new
    return [jnp.where(mask, n, 0.0) for n in new]


def level_split(source, noise, couplings, below):
    height = source[0].shape[0] - 2 * HALO
    width = source[0].shape[1] - 2 * HALO
    diagonal = diagonal_of(noise, couplings)
    ext = HALO
    mask = inside(height, width, ext)
    iterate = [jnp.where(mask, OMEGA * s / d, 0.0) for s, d in zip(source, diagonal)]
    for sweep_index in range(PRE - 1):
        ext -= 1
        cut = HALO - ext
        iterate = sweep_ext(
            iterate, crops(source, cut), crops(noise, cut), crops(couplings, cut),
            crops(diagonal, cut), inside(height, width, ext),
        )
    image = apply_ext(crops(iterate, ext - 1), crops(noise, HALO), crops(couplings, HALO))
    residual = [s - a for s, a in zip(crops(source, HALO), image)]
    coarse = below(residual)
    ring = (POST + 1) // 2
    iterate = [
        i + crop(prolong(c), 2 * ring - POST) for i, c in zip(crops(iterate, ext - POST), coarse)
    ]
    for sweep_index in range(POST):
        ext = POST - 1 - sweep_index
        cut = HALO - ext
        iterate = sweep_ext(
            iterate, crops(source, cut), crops(noise, cut), crops(couplings, cut),
            crops(diagonal, cut), inside(height, width, ext) if ext else None,
        )
    return iterate


def on_device(right_side, noise_block, edges):
    count_rows = lax.axis_size(ROWS)
    count_cols = lax.axis_size(COLS)
    height0, width0 = right_side.shape[1], right_side.shape[2]

    noises = [noise_block]
    downs = [edges[0]]
    rights = [edges[1]]
    for level in range(1, LEVELS):
        noises.append(restrict_sum(noises[-1]))
        downs.append(restrict_down(downs[-1]))
        rights.append(restrict_right(rights[-1]))

    gathered = LEVELS - 1
    for level in range(LEVELS):
        height, width = height0 >> level, width0 >> level
        whole = count_rows * height * count_cols * width
        if whole <= GATHER_PIXELS or height <= HALO or width <= HALO or level == LEVELS - 1:
            gathered = level
            break

    if gathered == 0:
        packed = gather_grids(
            [jnp.concatenate([noises[l], downs[l][None], rights[l][None]]) for l in range(LEVELS)]
        )
        hierarchy = [(p[:6], p[6], p[7]) for p in packed]
        correction = cycle_whole(gather_grid(right_side), hierarchy, 0)
        return jnp.stack([own_window(c, height0, width0, 0) for c in correction])

    packed = gather_grids(
        [
            jnp.concatenate([noises[l], downs[l][None], rights[l][None]])
            for l in range(gathered, LEVELS)
        ]
    )
    hierarchy = [(p[:6], p[6], p[7]) for p in packed]
    split_inputs = []
    for level in range(gathered):
        parts = [noises[level], downs[level][None], rights[level][None]]
        if level == 0:
            parts = [right_side] + parts
        ringed = with_halo(jnp.concatenate(parts), HALO + 1)
        ringed = [ringed[k] for k in range(ringed.shape[0])]
        source = crops(ringed[:3], 1) if level == 0 else None
        if level == 0:
            ringed = ringed[3:]
        down, right = ringed[6], ringed[7]
        couplings = [down[1:-1, 1:-1], down[:-2, 1:-1], right[1:-1, 1:-1], right[1:-1, :-2]]
        split_inputs.append((source, crops(ringed[:6], 1), couplings))

    ring = (POST + 1) // 2

    def run(level, source):
        height, width = height0 >> level, width0 >> level
        _, noise, couplings = split_inputs[level]

        def below(residual):
            coarse_source = restrict_sum(jnp.stack(residual))
            if level + 1 == gathered:
                correction = cycle_whole(gather_grid(coarse_source), hierarchy, gathered)
                return [own_window(c, height // 2, width // 2, ring) for c in correction]
            coarse = run(level + 1, list(with_halo(coarse_source, HALO)))
            return list(with_halo(jnp.stack(coarse), ring))

        return level_split(source, noise, couplings, below)

    return jnp.stack(run(0, split_inputs[0][0]))


def solution(mesh):
    in_specs = (
        P(None, ("groups", "tiles"), ("band", "stokes")),
        P(None, ("groups", "tiles"), ("band", "stokes")),
        P(None, ("groups", "tiles"), ("band", "stokes")),
    )
    out_specs = P(None, ("groups", "tiles"), ("band", "stokes"))
    return jax.shard_map(
        on_device, mesh=mesh, in_specs=in_specs, out_specs=out_specs, check_vma=False
    )
```

```python
import jax
import jax.numpy as jnp
from jax import lax
from jax.sharding import PartitionSpec as P

LEVELS = 5
PRE = 2
POST = 2
COARSE_SWEEPS = 8

OMEGA = 0.8

ROWS = "tiles"
COLS = ("band", "stokes")
GRID = ("tiles", "band", "stokes")

HALO = PRE - 1 + POST
GATHER_PIXELS = 32768


def with_halo(cells, width):
    for axis, dim in ((ROWS, 1), (COLS, 2)):
        count = lax.axis_size(axis)
        ends = count - 1
        head = lax.slice_in_dim(cells, 0, width, axis=dim)
        tail = lax.slice_in_dim(cells, cells.shape[dim] - width, cells.shape[dim], axis=dim)
        cells = jnp.concatenate(
            [
                lax.ppermute(tail, axis, [(i, i + 1) for i in range(ends)]),
                cells,
                lax.ppermute(head, axis, [(i + 1, i) for i in range(ends)]),
            ],
            axis=dim,
        )
    return cells


def crop(x, k):
    if k == 0:
        return x
    return x[..., k:-k, k:-k]


HIGH = lax.Precision.HIGHEST


def pairs(n, pick=None):
    rows = lax.broadcasted_iota(jnp.int32, (n, n // 2), 0)
    cols = lax.broadcasted_iota(jnp.int32, (n, n // 2), 1)
    hit = (rows // 2 == cols) if pick is None else (rows == 2 * cols + pick)
    return hit.astype(jnp.float32)


def sum_rows(x, m):
    return jnp.einsum("...hw,hv->...vw", x, m, precision=HIGH)


def sum_cols(x, m):
    return jnp.einsum("...hw,wv->...hv", x, m, precision=HIGH)


def restrict_sum(x):
    return sum_cols(sum_rows(x, pairs(x.shape[-2])), pairs(x.shape[-1]))


def restrict_down(down):
    return sum_cols(sum_rows(down, pairs(down.shape[-2], 1)), pairs(down.shape[-1]))


def restrict_right(right):
    return sum_rows(sum_cols(right, pairs(right.shape[-1], 1)), pairs(right.shape[-2]))


def prolong(coarse):
    height, width = coarse.shape[-2] * 2, coarse.shape[-1] * 2
    taller = jnp.einsum("...vw,hv->...hw", coarse, pairs(height), precision=HIGH)
    return jnp.einsum("...hv,wv->...hw", taller, pairs(width), precision=HIGH)


def apply_planes(iterate, padded, noise, couplings):
    first = noise[0] * iterate[0] + noise[3] * iterate[1] + noise[4] * iterate[2]
    second = noise[3] * iterate[0] + noise[1] * iterate[1] + noise[5] * iterate[2]
    third = noise[4] * iterate[0] + noise[5] * iterate[1] + noise[2] * iterate[2]
    totals = couplings[0] + couplings[1] + couplings[2] + couplings[3]
    image = []
    for local, core, rim in zip((first, second, third), iterate, padded):
        neighbours = (
            couplings[0] * rim[2:, 1:-1]
            + couplings[1] * rim[:-2, 1:-1]
            + couplings[2] * rim[1:-1, 2:]
            + couplings[3] * rim[1:-1, :-2]
        )
        image.append(local + totals * core - neighbours)
    return image


def apply_ext(padded, noise, couplings):
    return apply_planes([p[1:-1, 1:-1] for p in padded], padded, noise, couplings)


def diagonal_of(noise, couplings):
    totals = couplings[0] + couplings[1] + couplings[2] + couplings[3]
    return [noise[k] + totals for k in range(3)]


def couplings_from(down, right):
    upward = jnp.pad(down, ((1, 0), (0, 0)))[:-1, :]
    leftward = jnp.pad(right, ((0, 0), (1, 0)))[:, :-1]
    return [down, upward, right, leftward]


def crops(planes, k):
    return [crop(p, k) for p in planes]


def smooth_whole(iterate, source, noise, couplings, diagonal):
    image = apply_planes(iterate, [jnp.pad(p, 1) for p in iterate], noise, couplings)
    return [i + OMEGA * (s - a) / d for i, s, a, d in zip(iterate, source, image, diagonal)]


def cycle_whole(source, hierarchy, level_index):
    noise, down, right = hierarchy[0]
    couplings = couplings_from(down, right)
    diagonal = diagonal_of(noise, couplings)
    iterate = [OMEGA * s / d for s, d in zip(source, diagonal)]
    if level_index == LEVELS - 1:
        for sweep_index in range(COARSE_SWEEPS - 1):
            iterate = smooth_whole(iterate, source, noise, couplings, diagonal)
        return iterate
    for sweep_index in range(PRE - 1):
        iterate = smooth_whole(iterate, source, noise, couplings, diagonal)
    image = apply_planes(iterate, [jnp.pad(p, 1) for p in iterate], noise, couplings)
    residual = restrict_sum(jnp.stack([s - a for s, a in zip(source, image)]))
    coarse = prolong(
        jnp.stack(cycle_whole([residual[k] for k in range(3)], hierarchy[1:], level_index + 1))
    )
    iterate = [iterate[k] + coarse[k] for k in range(3)]
    for sweep_index in range(POST):
        iterate = smooth_whole(iterate, source, noise, couplings, diagonal)
    return iterate


def gather_grid(block):
    return gather_grids([block])[0]


def gather_axis(x, axis):
    count = lax.axis_size(axis)
    me = lax.axis_index(axis)
    pieces = [x] + [
        lax.ppermute(x, axis, [(i, (i + k) % count) for i in range(count)]) for k in range(1, count)
    ]
    order = (me - jnp.arange(count)) % count
    return jnp.take(jnp.stack(pieces), order, axis=0, mode="clip")


def gather_grids(blocks):
    count_rows = lax.axis_size(ROWS)
    count_cols = lax.axis_size(COLS)
    planes = blocks[0].shape[0]
    runs = [-(-b.shape[1] * b.shape[2] // 128) * 128 for b in blocks]
    flat = jnp.concatenate(
        [
            jnp.pad(b.reshape(planes, -1), ((0, 0), (0, run - b.shape[1] * b.shape[2])))
            for b, run in zip(blocks, runs)
        ],
        axis=1,
    )
    paired = gather_axis(flat, "stokes")
    stacked = lax.all_gather(paired, ("tiles", "band"), axis=0, tiled=False)
    stacked = stacked.reshape((count_rows * count_cols,) + flat.shape)
    grids = []
    offset = 0
    for b, run in zip(blocks, runs):
        _, height, width = b.shape
        part = stacked[:, :, offset:offset + height * width]
        offset += run
        part = part.reshape(count_rows, count_cols, planes, height, width)
        whole = part.transpose(2, 0, 3, 1, 4).reshape(
            planes, count_rows * height, count_cols * width
        )
        grids.append([whole[k] for k in range(planes)])
    return grids


def own_window(whole, height, width, ring):
    row = lax.axis_index(ROWS) * height
    col = lax.axis_index(COLS) * width
    padded = jnp.pad(whole, ring) if ring else whole
    return lax.dynamic_slice(padded, (row, col), (height + 2 * ring, width + 2 * ring))


def inside(height, width, ext):
    rows = lax.axis_index(ROWS) * height - ext + lax.broadcasted_iota(
        jnp.int32, (height + 2 * ext, width + 2 * ext), 0
    )
    cols = lax.axis_index(COLS) * width - ext + lax.broadcasted_iota(
        jnp.int32, (height + 2 * ext, width + 2 * ext), 1
    )
    return (
        (rows >= 0)
        & (rows < lax.axis_size(ROWS) * height)
        & (cols >= 0)
        & (cols < lax.axis_size(COLS) * width)
    )


def sweep_ext(iterate, source, noise, couplings, diagonal, mask):
    image = apply_ext(iterate, noise, couplings)
    new = [
        i[1:-1, 1:-1] + OMEGA * (s - a) / d for i, s, a, d in zip(iterate, source, image, diagonal)
    ]
    if mask is None:
        return new
    return [jnp.where(mask, n, 0.0) for n in new]


def level_split(source, noise, couplings, below):
    height = source[0].shape[0] - 2 * HALO
    width = source[0].shape[1] - 2 * HALO
    diagonal = diagonal_of(noise, couplings)
    ext = HALO
    mask = inside(height, width, ext)
    iterate = [jnp.where(mask, OMEGA * s / d, 0.0) for s, d in zip(source, diagonal)]
    for sweep_index in range(PRE - 1):
        ext -= 1
        cut = HALO - ext
        iterate = sweep_ext(
            iterate, crops(source, cut), crops(noise, cut), crops(couplings, cut),
            crops(diagonal, cut), inside(height, width, ext),
        )
    image = apply_ext(crops(iterate, ext - 1), crops(noise, HALO), crops(couplings, HALO))
    residual = [s - a for s, a in zip(crops(source, HALO), image)]
    coarse = below(residual)
    ring = (POST + 1) // 2
    iterate = [
        i + crop(prolong(c), 2 * ring - POST) for i, c in zip(crops(iterate, ext - POST), coarse)
    ]
    for sweep_index in range(POST):
        ext = POST - 1 - sweep_index
        cut = HALO - ext
        iterate = sweep_ext(
            iterate, crops(source, cut), crops(noise, cut), crops(couplings, cut),
            crops(diagonal, cut), inside(height, width, ext) if ext else None,
        )
    return iterate


def on_device(right_side, noise_block, edges):
    count_rows = lax.axis_size(ROWS)
    count_cols = lax.axis_size(COLS)
    height0, width0 = right_side.shape[1], right_side.shape[2]

    noises = [noise_block]
    downs = [edges[0]]
    rights = [edges[1]]
    for level in range(1, LEVELS):
        noises.append(restrict_sum(noises[-1]))
        downs.append(restrict_down(downs[-1]))
        rights.append(restrict_right(rights[-1]))

    gathered = LEVELS - 1
    for level in range(LEVELS):
        height, width = height0 >> level, width0 >> level
        whole = count_rows * height * count_cols * width
        if whole <= GATHER_PIXELS or height <= HALO or width <= HALO or level == LEVELS - 1:
            gathered = level
            break

    if gathered == 0:
        packed = gather_grids(
            [jnp.concatenate([noises[l], downs[l][None], rights[l][None]]) for l in range(LEVELS)]
        )
        hierarchy = [(p[:6], p[6], p[7]) for p in packed]
        correction = cycle_whole(gather_grid(right_side), hierarchy, 0)
        return jnp.stack([own_window(c, height0, width0, 0) for c in correction])

    packed = gather_grids(
        [
            jnp.concatenate([noises[l], downs[l][None], rights[l][None]])
            for l in range(gathered, LEVELS)
        ]
    )
    hierarchy = [(p[:6], p[6], p[7]) for p in packed]
    split_inputs = []
    for level in range(gathered):
        parts = [noises[level], downs[level][None], rights[level][None]]
        if level == 0:
            parts = [right_side] + parts
        ringed = with_halo(jnp.concatenate(parts), HALO + 1)
        ringed = [ringed[k] for k in range(ringed.shape[0])]
        source = crops(ringed[:3], 1) if level == 0 else None
        if level == 0:
            ringed = ringed[3:]
        down, right = ringed[6], ringed[7]
        couplings = [down[1:-1, 1:-1], down[:-2, 1:-1], right[1:-1, 1:-1], right[1:-1, :-2]]
        split_inputs.append((source, crops(ringed[:6], 1), couplings))

    ring = (POST + 1) // 2

    def run(level, source):
        height, width = height0 >> level, width0 >> level
        _, noise, couplings = split_inputs[level]

        def below(residual):
            coarse_source = restrict_sum(jnp.stack(residual))
            if level + 1 == gathered:
                correction = cycle_whole(gather_grid(coarse_source), hierarchy, gathered)
                return [own_window(c, height // 2, width // 2, ring) for c in correction]
            coarse = run(level + 1, list(with_halo(coarse_source, HALO)))
            return list(with_halo(jnp.stack(coarse), ring))

        return level_split(source, noise, couplings, below)

    return jnp.stack(run(0, split_inputs[0][0]))


def solution(mesh):
    in_specs = (
        P(None, ("groups", "tiles"), ("band", "stokes")),
        P(None, ("groups", "tiles"), ("band", "stokes")),
        P(None, ("groups", "tiles"), ("band", "stokes")),
    )
    out_specs = P(None, ("groups", "tiles"), ("band", "stokes"))
    return jax.shard_map(
        on_device, mesh=mesh, in_specs=in_specs, out_specs=out_specs, check_vma=False
    )
```

```python
import jax
import jax.numpy as jnp
from jax import lax
from jax.sharding import PartitionSpec as P

LEVELS = 5
PRE = 2
POST = 2
COARSE_SWEEPS = 8

OMEGA = 0.8

ROWS = "tiles"
COLS = ("band", "stokes")
GRID = ("tiles", "band", "stokes")

HALO = PRE - 1 + POST
GATHER_PIXELS = 32768


def with_halo(cells, width):
    for axis, dim in ((ROWS, 1), (COLS, 2)):
        count = lax.axis_size(axis)
        ends = count - 1
        head = lax.slice_in_dim(cells, 0, width, axis=dim)
        tail = lax.slice_in_dim(cells, cells.shape[dim] - width, cells.shape[dim], axis=dim)
        cells = jnp.concatenate(
            [
                lax.ppermute(tail, axis, [(i, i + 1) for i in range(ends)]),
                cells,
                lax.ppermute(head, axis, [(i + 1, i) for i in range(ends)]),
            ],
            axis=dim,
        )
    return cells


def crop(x, k):
    if k == 0:
        return x
    return x[..., k:-k, k:-k]


HIGH = lax.Precision.HIGHEST


def pairs(n, pick=None):
    rows = lax.broadcasted_iota(jnp.int32, (n, n // 2), 0)
    cols = lax.broadcasted_iota(jnp.int32, (n, n // 2), 1)
    hit = (rows // 2 == cols) if pick is None else (rows == 2 * cols + pick)
    return hit.astype(jnp.float32)


def sum_rows(x, m):
    return jnp.einsum("...hw,hv->...vw", x, m, precision=HIGH)


def sum_cols(x, m):
    return jnp.einsum("...hw,wv->...hv", x, m, precision=HIGH)


def restrict_sum(x):
    return sum_cols(sum_rows(x, pairs(x.shape[-2])), pairs(x.shape[-1]))


def restrict_down(down):
    return sum_cols(sum_rows(down, pairs(down.shape[-2], 1)), pairs(down.shape[-1]))


def restrict_right(right):
    return sum_rows(sum_cols(right, pairs(right.shape[-1], 1)), pairs(right.shape[-2]))


def prolong(coarse):
    height, width = coarse.shape[-2] * 2, coarse.shape[-1] * 2
    taller = jnp.einsum("...vw,hv->...hw", coarse, pairs(height), precision=HIGH)
    return jnp.einsum("...hv,wv->...hw", taller, pairs(width), precision=HIGH)


def apply_planes(iterate, padded, noise, couplings):
    first = noise[0] * iterate[0] + noise[3] * iterate[1] + noise[4] * iterate[2]
    second = noise[3] * iterate[0] + noise[1] * iterate[1] + noise[5] * iterate[2]
    third = noise[4] * iterate[0] + noise[5] * iterate[1] + noise[2] * iterate[2]
    totals = couplings[0] + couplings[1] + couplings[2] + couplings[3]
    image = []
    for local, core, rim in zip((first, second, third), iterate, padded):
        neighbours = (
            couplings[0] * rim[2:, 1:-1]
            + couplings[1] * rim[:-2, 1:-1]
            + couplings[2] * rim[1:-1, 2:]
            + couplings[3] * rim[1:-1, :-2]
        )
        image.append(local + totals * core - neighbours)
    return image


def apply_ext(padded, noise, couplings):
    return apply_planes([p[1:-1, 1:-1] for p in padded], padded, noise, couplings)


def diagonal_of(noise, couplings):
    totals = couplings[0] + couplings[1] + couplings[2] + couplings[3]
    return [noise[k] + totals for k in range(3)]


def couplings_from(down, right):
    upward = jnp.pad(down, ((1, 0), (0, 0)))[:-1, :]
    leftward = jnp.pad(right, ((0, 0), (1, 0)))[:, :-1]
    return [down, upward, right, leftward]


def crops(planes, k):
    return [crop(p, k) for p in planes]


def smooth_whole(iterate, source, noise, couplings, diagonal):
    image = apply_planes(iterate, [jnp.pad(p, 1) for p in iterate], noise, couplings)
    return [i + OMEGA * (s - a) / d for i, s, a, d in zip(iterate, source, image, diagonal)]


def cycle_whole(source, hierarchy, level_index):
    noise, down, right = hierarchy[0]
    couplings = couplings_from(down, right)
    diagonal = diagonal_of(noise, couplings)
    iterate = [OMEGA * s / d for s, d in zip(source, diagonal)]
    if level_index == LEVELS - 1:
        for sweep_index in range(COARSE_SWEEPS - 1):
            iterate = smooth_whole(iterate, source, noise, couplings, diagonal)
        return iterate
    for sweep_index in range(PRE - 1):
        iterate = smooth_whole(iterate, source, noise, couplings, diagonal)
    image = apply_planes(iterate, [jnp.pad(p, 1) for p in iterate], noise, couplings)
    residual = restrict_sum(jnp.stack([s - a for s, a in zip(source, image)]))
    coarse = prolong(
        jnp.stack(cycle_whole([residual[k] for k in range(3)], hierarchy[1:], level_index + 1))
    )
    iterate = [iterate[k] + coarse[k] for k in range(3)]
    for sweep_index in range(POST):
        iterate = smooth_whole(iterate, source, noise, couplings, diagonal)
    return iterate


def gather_grid(block):
    return gather_grids([block])[0]


def gather_grids(blocks):
    count_rows = lax.axis_size(ROWS)
    count_cols = lax.axis_size(COLS)
    planes = blocks[0].shape[0]
    runs = [-(-b.shape[1] * b.shape[2] // 128) * 128 for b in blocks]
    flat = jnp.concatenate(
        [
            jnp.pad(b.reshape(planes, -1), ((0, 0), (0, run - b.shape[1] * b.shape[2])))
            for b, run in zip(blocks, runs)
        ],
        axis=1,
    )
    stacked = lax.all_gather(flat, GRID, axis=0, tiled=False)
    grids = []
    offset = 0
    for b, run in zip(blocks, runs):
        _, height, width = b.shape
        part = stacked[:, :, offset:offset + height * width]
        offset += run
        part = part.reshape(count_rows, count_cols, planes, height, width)
        whole = part.transpose(2, 0, 3, 1, 4).reshape(
            planes, count_rows * height, count_cols * width
        )
        grids.append([whole[k] for k in range(planes)])
    return grids


def own_window(whole, height, width, ring):
    row = lax.axis_index(ROWS) * height
    col = lax.axis_index(COLS) * width
    padded = jnp.pad(whole, ring) if ring else whole
    return lax.dynamic_slice(padded, (row, col), (height + 2 * ring, width + 2 * ring))


def inside(height, width, ext):
    rows = lax.axis_index(ROWS) * height - ext + lax.broadcasted_iota(
        jnp.int32, (height + 2 * ext, width + 2 * ext), 0
    )
    cols = lax.axis_index(COLS) * width - ext + lax.broadcasted_iota(
        jnp.int32, (height + 2 * ext, width + 2 * ext), 1
    )
    return (
        (rows >= 0)
        & (rows < lax.axis_size(ROWS) * height)
        & (cols >= 0)
        & (cols < lax.axis_size(COLS) * width)
    )


def sweep_ext(iterate, source, noise, couplings, diagonal, mask):
    image = apply_ext(iterate, noise, couplings)
    new = [
        i[1:-1, 1:-1] + OMEGA * (s - a) / d for i, s, a, d in zip(iterate, source, image, diagonal)
    ]
    if mask is None:
        return new
    return [jnp.where(mask, n, 0.0) for n in new]


def level_split(source, noise, couplings, below):
    height = source[0].shape[0] - 2 * HALO
    width = source[0].shape[1] - 2 * HALO
    diagonal = diagonal_of(noise, couplings)
    ext = HALO
    mask = inside(height, width, ext)
    iterate = [jnp.where(mask, OMEGA * s / d, 0.0) for s, d in zip(source, diagonal)]
    for sweep_index in range(PRE - 1):
        ext -= 1
        cut = HALO - ext
        iterate = sweep_ext(
            iterate, crops(source, cut), crops(noise, cut), crops(couplings, cut),
            crops(diagonal, cut), inside(height, width, ext),
        )
    image = apply_ext(crops(iterate, ext - 1), crops(noise, HALO), crops(couplings, HALO))
    residual = [s - a for s, a in zip(crops(source, HALO), image)]
    coarse = below(residual)
    ring = (POST + 1) // 2
    iterate = [
        i + crop(prolong(c), 2 * ring - POST) for i, c in zip(crops(iterate, ext - POST), coarse)
    ]
    for sweep_index in range(POST):
        ext = POST - 1 - sweep_index
        cut = HALO - ext
        iterate = sweep_ext(
            iterate, crops(source, cut), crops(noise, cut), crops(couplings, cut),
            crops(diagonal, cut), inside(height, width, ext) if ext else None,
        )
    return iterate


def spans(n, pick_last):
    mats = []
    for level in range(1, LEVELS):
        size = 1 << level
        rows = lax.broadcasted_iota(jnp.int32, (n, n // size), 0)
        cols = lax.broadcasted_iota(jnp.int32, (n, n // size), 1)
        hit = (rows == cols * size + size - 1) if pick_last else (rows // size == cols)
        mats.append(hit.astype(jnp.float32))
    return jnp.concatenate(mats, axis=1)


def hierarchy_of(noise, down, right):
    height, width = down.shape
    row_sum, row_last = spans(height, False), spans(height, True)
    col_sum, col_last = spans(width, False), spans(width, True)
    tall = jnp.concatenate(
        [
            jnp.einsum("phw,hv->pvw", noise, row_sum, precision=HIGH),
            jnp.einsum("hw,hv->vw", down, row_last, precision=HIGH)[None],
        ]
    )
    both = jnp.einsum("pvw,wu->pvu", tall, col_sum, precision=HIGH)
    wide = jnp.einsum(
        "hv,hw->vw", row_sum, jnp.einsum("hw,wu->hu", right, col_last, precision=HIGH),
        precision=HIGH,
    )
    noises, downs, rights = [noise], [down], [right]
    row, col = 0, 0
    for level in range(1, LEVELS):
        rows, cols = height >> level, width >> level
        noises.append(both[:6, row:row + rows, col:col + cols])
        downs.append(both[6, row:row + rows, col:col + cols])
        rights.append(wide[row:row + rows, col:col + cols])
        row, col = row + rows, col + cols
    return noises, downs, rights


def on_device(right_side, noise_block, edges):
    count_rows = lax.axis_size(ROWS)
    count_cols = lax.axis_size(COLS)
    height0, width0 = right_side.shape[1], right_side.shape[2]

    noises, downs, rights = hierarchy_of(noise_block, edges[0], edges[1])

    gathered = LEVELS - 1
    for level in range(LEVELS):
        height, width = height0 >> level, width0 >> level
        whole = count_rows * height * count_cols * width
        if whole <= GATHER_PIXELS or height <= HALO or width <= HALO or level == LEVELS - 1:
            gathered = level
            break

    if gathered == 0:
        packed = gather_grids(
            [jnp.concatenate([noises[l], downs[l][None], rights[l][None]]) for l in range(LEVELS)]
        )
        hierarchy = [(p[:6], p[6], p[7]) for p in packed]
        correction = cycle_whole(gather_grid(right_side), hierarchy, 0)
        return jnp.stack([own_window(c, height0, width0, 0) for c in correction])

    packed = gather_grids(
        [
            jnp.concatenate([noises[l], downs[l][None], rights[l][None]])
            for l in range(gathered, LEVELS)
        ]
    )
    hierarchy = [(p[:6], p[6], p[7]) for p in packed]
    split_inputs = []
    for level in range(gathered):
        parts = [noises[level], downs[level][None], rights[level][None]]
        if level == 0:
            parts = [right_side] + parts
        ringed = with_halo(jnp.concatenate(parts), HALO + 1)
        ringed = [ringed[k] for k in range(ringed.shape[0])]
        source = crops(ringed[:3], 1) if level == 0 else None
        if level == 0:
            ringed = ringed[3:]
        down, right = ringed[6], ringed[7]
        couplings = [down[1:-1, 1:-1], down[:-2, 1:-1], right[1:-1, 1:-1], right[1:-1, :-2]]
        split_inputs.append((source, crops(ringed[:6], 1), couplings))

    ring = (POST + 1) // 2

    def run(level, source):
        height, width = height0 >> level, width0 >> level
        _, noise, couplings = split_inputs[level]

        def below(residual):
            coarse_source = restrict_sum(jnp.stack(residual))
            if level + 1 == gathered:
                correction = cycle_whole(gather_grid(coarse_source), hierarchy, gathered)
                return [own_window(c, height // 2, width // 2, ring) for c in correction]
            coarse = run(level + 1, list(with_halo(coarse_source, HALO)))
            return list(with_halo(jnp.stack(coarse), ring))

        return level_split(source, noise, couplings, below)

    return jnp.stack(run(0, split_inputs[0][0]))


def solution(mesh):
    in_specs = (
        P(None, ("groups", "tiles"), ("band", "stokes")),
        P(None, ("groups", "tiles"), ("band", "stokes")),
        P(None, ("groups", "tiles"), ("band", "stokes")),
    )
    out_specs = P(None, ("groups", "tiles"), ("band", "stokes"))
    return jax.shard_map(
        on_device, mesh=mesh, in_specs=in_specs, out_specs=out_specs, check_vma=False
    )
```

```python
import jax
import jax.numpy as jnp
from jax import lax
from jax.sharding import PartitionSpec as P

LEVELS = 5
PRE = 2
POST = 2
COARSE_SWEEPS = 8

OMEGA = 0.8

ROWS = "tiles"
COLS = ("band", "stokes")
GRID = ("tiles", "band", "stokes")

HALO = PRE - 1 + POST
GATHER_PIXELS = 32768


def with_halo(cells, width):
    for axis, dim in ((ROWS, 1), (COLS, 2)):
        count = lax.axis_size(axis)
        ends = count - 1
        head = lax.slice_in_dim(cells, 0, width, axis=dim)
        tail = lax.slice_in_dim(cells, cells.shape[dim] - width, cells.shape[dim], axis=dim)
        cells = jnp.concatenate(
            [
                lax.ppermute(tail, axis, [(i, i + 1) for i in range(ends)]),
                cells,
                lax.ppermute(head, axis, [(i + 1, i) for i in range(ends)]),
            ],
            axis=dim,
        )
    return cells


def crop(x, k):
    if k == 0:
        return x
    return x[..., k:-k, k:-k]


HIGH = lax.Precision.HIGHEST


def pairs(n, pick=None):
    rows = lax.broadcasted_iota(jnp.int32, (n, n // 2), 0)
    cols = lax.broadcasted_iota(jnp.int32, (n, n // 2), 1)
    hit = (rows // 2 == cols) if pick is None else (rows == 2 * cols + pick)
    return hit.astype(jnp.float32)


def sum_rows(x, m):
    return jnp.einsum("...hw,hv->...vw", x, m, precision=HIGH)


def sum_cols(x, m):
    return jnp.einsum("...hw,wv->...hv", x, m, precision=HIGH)


def restrict_sum(x):
    return sum_cols(sum_rows(x, pairs(x.shape[-2])), pairs(x.shape[-1]))


def restrict_down(down):
    return sum_cols(sum_rows(down, pairs(down.shape[-2], 1)), pairs(down.shape[-1]))


def restrict_right(right):
    return sum_rows(sum_cols(right, pairs(right.shape[-1], 1)), pairs(right.shape[-2]))


def prolong(coarse):
    height, width = coarse.shape[-2] * 2, coarse.shape[-1] * 2
    wider = jnp.einsum("...hv,wv->...hw", coarse, pairs(width), precision=HIGH)
    return jnp.einsum("...vw,hv->...hw", wider, pairs(height), precision=HIGH)


def apply_planes(iterate, padded, noise, couplings):
    first = noise[0] * iterate[0] + noise[3] * iterate[1] + noise[4] * iterate[2]
    second = noise[3] * iterate[0] + noise[1] * iterate[1] + noise[5] * iterate[2]
    third = noise[4] * iterate[0] + noise[5] * iterate[1] + noise[2] * iterate[2]
    totals = couplings[0] + couplings[1] + couplings[2] + couplings[3]
    image = []
    for local, core, rim in zip((first, second, third), iterate, padded):
        neighbours = (
            couplings[0] * rim[2:, 1:-1]
            + couplings[1] * rim[:-2, 1:-1]
            + couplings[2] * rim[1:-1, 2:]
            + couplings[3] * rim[1:-1, :-2]
        )
        image.append(local + totals * core - neighbours)
    return image


def apply_ext(padded, noise, couplings):
    return apply_planes([p[1:-1, 1:-1] for p in padded], padded, noise, couplings)


def diagonal_of(noise, couplings):
    totals = couplings[0] + couplings[1] + couplings[2] + couplings[3]
    return [noise[k] + totals for k in range(3)]


def couplings_from(down, right):
    upward = jnp.pad(down, ((1, 0), (0, 0)))[:-1, :]
    leftward = jnp.pad(right, ((0, 0), (1, 0)))[:, :-1]
    return [down, upward, right, leftward]


def crops(planes, k):
    return [crop(p, k) for p in planes]


def smooth_whole(iterate, source, noise, couplings, diagonal):
    image = apply_planes(iterate, [jnp.pad(p, 1) for p in iterate], noise, couplings)
    return [i + OMEGA * (s - a) / d for i, s, a, d in zip(iterate, source, image, diagonal)]


def cycle_whole(source, hierarchy, level_index):
    noise, down, right = hierarchy[0]
    couplings = couplings_from(down, right)
    diagonal = diagonal_of(noise, couplings)
    iterate = [OMEGA * s / d for s, d in zip(source, diagonal)]
    if level_index == LEVELS - 1:
        for sweep_index in range(COARSE_SWEEPS - 1):
            iterate = smooth_whole(iterate, source, noise, couplings, diagonal)
        return iterate
    for sweep_index in range(PRE - 1):
        iterate = smooth_whole(iterate, source, noise, couplings, diagonal)
    image = apply_planes(iterate, [jnp.pad(p, 1) for p in iterate], noise, couplings)
    residual = restrict_sum(jnp.stack([s - a for s, a in zip(source, image)]))
    coarse = prolong(
        jnp.stack(cycle_whole([residual[k] for k in range(3)], hierarchy[1:], level_index + 1))
    )
    iterate = [iterate[k] + coarse[k] for k in range(3)]
    for sweep_index in range(POST):
        iterate = smooth_whole(iterate, source, noise, couplings, diagonal)
    return iterate


def gather_grid(block):
    return gather_grids([block])[0]


def gather_grids(blocks):
    count_rows = lax.axis_size(ROWS)
    count_cols = lax.axis_size(COLS)
    planes = blocks[0].shape[0]
    runs = [-(-b.shape[1] * b.shape[2] // 128) * 128 for b in blocks]
    flat = jnp.concatenate(
        [
            jnp.pad(b.reshape(planes, -1), ((0, 0), (0, run - b.shape[1] * b.shape[2])))
            for b, run in zip(blocks, runs)
        ],
        axis=1,
    )
    stacked = lax.all_gather(flat, GRID, axis=0, tiled=False)
    grids = []
    offset = 0
    for b, run in zip(blocks, runs):
        _, height, width = b.shape
        part = stacked[:, :, offset:offset + height * width]
        offset += run
        part = part.reshape(count_rows, count_cols, planes, height, width)
        whole = part.transpose(2, 0, 3, 1, 4).reshape(
            planes, count_rows * height, count_cols * width
        )
        grids.append([whole[k] for k in range(planes)])
    return grids


def own_window(whole, height, width, ring):
    row = lax.axis_index(ROWS) * height
    col = lax.axis_index(COLS) * width
    padded = jnp.pad(whole, ring) if ring else whole
    return lax.dynamic_slice(padded, (row, col), (height + 2 * ring, width + 2 * ring))


def inside(height, width, ext):
    rows = lax.axis_index(ROWS) * height - ext + lax.broadcasted_iota(
        jnp.int32, (height + 2 * ext, width + 2 * ext), 0
    )
    cols = lax.axis_index(COLS) * width - ext + lax.broadcasted_iota(
        jnp.int32, (height + 2 * ext, width + 2 * ext), 1
    )
    return (
        (rows >= 0)
        & (rows < lax.axis_size(ROWS) * height)
        & (cols >= 0)
        & (cols < lax.axis_size(COLS) * width)
    )


def sweep_ext(iterate, source, noise, couplings, diagonal, mask):
    image = apply_ext(iterate, noise, couplings)
    new = [
        i[1:-1, 1:-1] + OMEGA * (s - a) / d for i, s, a, d in zip(iterate, source, image, diagonal)
    ]
    if mask is None:
        return new
    return [jnp.where(mask, n, 0.0) for n in new]


def level_split(source, noise, couplings, below):
    height = source[0].shape[0] - 2 * HALO
    width = source[0].shape[1] - 2 * HALO
    diagonal = diagonal_of(noise, couplings)
    ext = HALO
    mask = inside(height, width, ext)
    iterate = [jnp.where(mask, OMEGA * s / d, 0.0) for s, d in zip(source, diagonal)]
    for sweep_index in range(PRE - 1):
        ext -= 1
        cut = HALO - ext
        iterate = sweep_ext(
            iterate, crops(source, cut), crops(noise, cut), crops(couplings, cut),
            crops(diagonal, cut), inside(height, width, ext),
        )
    image = apply_ext(crops(iterate, ext - 1), crops(noise, HALO), crops(couplings, HALO))
    residual = [s - a for s, a in zip(crops(source, HALO), image)]
    coarse = below(residual)
    ring = (POST + 1) // 2
    iterate = [
        i + crop(prolong(c), 2 * ring - POST) for i, c in zip(crops(iterate, ext - POST), coarse)
    ]
    for sweep_index in range(POST):
        ext = POST - 1 - sweep_index
        cut = HALO - ext
        iterate = sweep_ext(
            iterate, crops(source, cut), crops(noise, cut), crops(couplings, cut),
            crops(diagonal, cut), inside(height, width, ext) if ext else None,
        )
    return iterate


def spans(n, pick_last):
    mats = []
    for level in range(1, LEVELS):
        size = 1 << level
        rows = lax.broadcasted_iota(jnp.int32, (n, n // size), 0)
        cols = lax.broadcasted_iota(jnp.int32, (n, n // size), 1)
        hit = (rows == cols * size + size - 1) if pick_last else (rows // size == cols)
        mats.append(hit.astype(jnp.float32))
    return jnp.concatenate(mats, axis=1)


def hierarchy_of(noise, down, right):
    height, width = down.shape
    row_sum, row_last = spans(height, False), spans(height, True)
    col_sum, col_last = spans(width, False), spans(width, True)
    tall = jnp.concatenate(
        [
            jnp.einsum("phw,hv->pvw", noise, row_sum, precision=HIGH),
            jnp.einsum("hw,hv->vw", down, row_last, precision=HIGH)[None],
        ]
    )
    both = jnp.einsum("pvw,wu->pvu", tall, col_sum, precision=HIGH)
    wide = jnp.einsum(
        "hv,hw->vw", row_sum, jnp.einsum("hw,wu->hu", right, col_last, precision=HIGH),
        precision=HIGH,
    )
    noises, downs, rights = [noise], [down], [right]
    row, col = 0, 0
    for level in range(1, LEVELS):
        rows, cols = height >> level, width >> level
        noises.append(both[:6, row:row + rows, col:col + cols])
        downs.append(both[6, row:row + rows, col:col + cols])
        rights.append(wide[row:row + rows, col:col + cols])
        row, col = row + rows, col + cols
    return noises, downs, rights


def on_device(right_side, noise_block, edges):
    count_rows = lax.axis_size(ROWS)
    count_cols = lax.axis_size(COLS)
    height0, width0 = right_side.shape[1], right_side.shape[2]

    noises, downs, rights = hierarchy_of(noise_block, edges[0], edges[1])

    gathered = LEVELS - 1
    for level in range(LEVELS):
        height, width = height0 >> level, width0 >> level
        whole = count_rows * height * count_cols * width
        if whole <= GATHER_PIXELS or height <= HALO or width <= HALO or level == LEVELS - 1:
            gathered = level
            break

    if gathered == 0:
        packed = gather_grids(
            [jnp.concatenate([noises[l], downs[l][None], rights[l][None]]) for l in range(LEVELS)]
        )
        hierarchy = [(p[:6], p[6], p[7]) for p in packed]
        correction = cycle_whole(gather_grid(right_side), hierarchy, 0)
        return jnp.stack([own_window(c, height0, width0, 0) for c in correction])

    packed = gather_grids(
        [
            jnp.concatenate([noises[l], downs[l][None], rights[l][None]])
            for l in range(gathered, LEVELS)
        ]
    )
    hierarchy = [(p[:6], p[6], p[7]) for p in packed]
    split_inputs = []
    for level in range(gathered):
        parts = [noises[level], downs[level][None], rights[level][None]]
        if level == 0:
            parts = [right_side] + parts
        ringed = with_halo(jnp.concatenate(parts), HALO + 1)
        ringed = [ringed[k] for k in range(ringed.shape[0])]
        source = crops(ringed[:3], 1) if level == 0 else None
        if level == 0:
            ringed = ringed[3:]
        down, right = ringed[6], ringed[7]
        couplings = [down[1:-1, 1:-1], down[:-2, 1:-1], right[1:-1, 1:-1], right[1:-1, :-2]]
        split_inputs.append((source, crops(ringed[:6], 1), couplings))

    ring = (POST + 1) // 2

    def run(level, source):
        height, width = height0 >> level, width0 >> level
        _, noise, couplings = split_inputs[level]

        def below(residual):
            coarse_source = restrict_sum(jnp.stack(residual))
            if level + 1 == gathered:
                correction = cycle_whole(gather_grid(coarse_source), hierarchy, gathered)
                return [own_window(c, height // 2, width // 2, ring) for c in correction]
            coarse = run(level + 1, list(with_halo(coarse_source, HALO)))
            return list(with_halo(jnp.stack(coarse), ring))

        return level_split(source, noise, couplings, below)

    return jnp.stack(run(0, split_inputs[0][0]))


def solution(mesh):
    in_specs = (
        P(None, ("groups", "tiles"), ("band", "stokes")),
        P(None, ("groups", "tiles"), ("band", "stokes")),
        P(None, ("groups", "tiles"), ("band", "stokes")),
    )
    out_specs = P(None, ("groups", "tiles"), ("band", "stokes"))
    return jax.shard_map(
        on_device, mesh=mesh, in_specs=in_specs, out_specs=out_specs, check_vma=False
    )
```

```python
import jax
import jax.numpy as jnp
from jax import lax
from jax.sharding import PartitionSpec as P

LEVELS = 5
PRE = 2
POST = 2
COARSE_SWEEPS = 8

OMEGA = 0.8

ROWS = "tiles"
COLS = ("band", "stokes")
GRID = ("tiles", "band", "stokes")

HALO = PRE - 1 + POST
GATHER_PIXELS = 32768


def with_halo(cells, width):
    for axis, dim in ((ROWS, 1), (COLS, 2)):
        count = lax.axis_size(axis)
        ends = count - 1
        head = lax.slice_in_dim(cells, 0, width, axis=dim)
        tail = lax.slice_in_dim(cells, cells.shape[dim] - width, cells.shape[dim], axis=dim)
        cells = jnp.concatenate(
            [
                lax.ppermute(tail, axis, [(i, i + 1) for i in range(ends)]),
                cells,
                lax.ppermute(head, axis, [(i + 1, i) for i in range(ends)]),
            ],
            axis=dim,
        )
    return cells


def crop(x, k):
    if k == 0:
        return x
    return x[..., k:-k, k:-k]


HIGH = lax.Precision.HIGHEST


def pairs(n, pick=None):
    rows = lax.broadcasted_iota(jnp.int32, (n, n // 2), 0)
    cols = lax.broadcasted_iota(jnp.int32, (n, n // 2), 1)
    hit = (rows // 2 == cols) if pick is None else (rows == 2 * cols + pick)
    return hit.astype(jnp.float32)


def sum_rows(x, m):
    return jnp.einsum("...hw,hv->...vw", x, m, precision=HIGH)


def sum_cols(x, m):
    return jnp.einsum("...hw,wv->...hv", x, m, precision=HIGH)


def restrict_sum(x):
    return sum_cols(sum_rows(x, pairs(x.shape[-2])), pairs(x.shape[-1]))


def restrict_down(down):
    return sum_cols(sum_rows(down, pairs(down.shape[-2], 1)), pairs(down.shape[-1]))


def restrict_right(right):
    return sum_rows(sum_cols(right, pairs(right.shape[-1], 1)), pairs(right.shape[-2]))


def prolong(coarse):
    height, width = coarse.shape[-2] * 2, coarse.shape[-1] * 2
    wider = jnp.einsum("...hv,wv->...hw", coarse, pairs(width), precision=HIGH)
    return jnp.einsum("...vw,hv->...hw", wider, pairs(height), precision=HIGH)


def apply_planes(iterate, padded, noise, couplings):
    first = noise[0] * iterate[0] + noise[3] * iterate[1] + noise[4] * iterate[2]
    second = noise[3] * iterate[0] + noise[1] * iterate[1] + noise[5] * iterate[2]
    third = noise[4] * iterate[0] + noise[5] * iterate[1] + noise[2] * iterate[2]
    totals = couplings[0] + couplings[1] + couplings[2] + couplings[3]
    image = []
    for local, core, rim in zip((first, second, third), iterate, padded):
        neighbours = (
            couplings[0] * rim[2:, 1:-1]
            + couplings[1] * rim[:-2, 1:-1]
            + couplings[2] * rim[1:-1, 2:]
            + couplings[3] * rim[1:-1, :-2]
        )
        image.append(local + totals * core - neighbours)
    return image


def apply_ext(padded, noise, couplings):
    return apply_planes([p[1:-1, 1:-1] for p in padded], padded, noise, couplings)


def diagonal_of(noise, couplings):
    totals = couplings[0] + couplings[1] + couplings[2] + couplings[3]
    return [noise[k] + totals for k in range(3)]


def couplings_from(down, right):
    upward = jnp.pad(down, ((1, 0), (0, 0)))[:-1, :]
    leftward = jnp.pad(right, ((0, 0), (1, 0)))[:, :-1]
    return [down, upward, right, leftward]


def crops(planes, k):
    return [crop(p, k) for p in planes]


def smooth_whole(iterate, source, noise, couplings, diagonal):
    image = apply_planes(iterate, [jnp.pad(p, 1) for p in iterate], noise, couplings)
    return [i + OMEGA * (s - a) / d for i, s, a, d in zip(iterate, source, image, diagonal)]


def cycle_whole(source, hierarchy, level_index):
    noise, down, right = hierarchy[0]
    couplings = couplings_from(down, right)
    diagonal = diagonal_of(noise, couplings)
    iterate = [OMEGA * s / d for s, d in zip(source, diagonal)]
    if level_index == LEVELS - 1:
        for sweep_index in range(COARSE_SWEEPS - 1):
            iterate = smooth_whole(iterate, source, noise, couplings, diagonal)
        return iterate
    for sweep_index in range(PRE - 1):
        iterate = smooth_whole(iterate, source, noise, couplings, diagonal)
    image = apply_planes(iterate, [jnp.pad(p, 1) for p in iterate], noise, couplings)
    residual = restrict_sum(jnp.stack([s - a for s, a in zip(source, image)]))
    coarse = prolong(
        jnp.stack(cycle_whole([residual[k] for k in range(3)], hierarchy[1:], level_index + 1))
    )
    iterate = [iterate[k] + coarse[k] for k in range(3)]
    for sweep_index in range(POST):
        iterate = smooth_whole(iterate, source, noise, couplings, diagonal)
    return iterate


def gather_grid(block):
    return gather_grids([block])[0]


def gather_grids(blocks):
    count_rows = lax.axis_size(ROWS)
    count_cols = lax.axis_size(COLS)
    planes = blocks[0].shape[0]
    runs = [-(-b.shape[1] * b.shape[2] // 128) * 128 for b in blocks]
    flat = jnp.concatenate(
        [
            jnp.pad(b.reshape(planes, -1), ((0, 0), (0, run - b.shape[1] * b.shape[2])))
            for b, run in zip(blocks, runs)
        ],
        axis=1,
    )
    stacked = lax.all_gather(flat, GRID, axis=0, tiled=False)
    grids = []
    offset = 0
    for b, run in zip(blocks, runs):
        _, height, width = b.shape
        part = stacked[:, :, offset:offset + height * width]
        offset += run
        part = part.reshape(count_rows, count_cols, planes, height, width)
        whole = part.transpose(2, 0, 3, 1, 4).reshape(
            planes, count_rows * height, count_cols * width
        )
        grids.append([whole[k] for k in range(planes)])
    return grids


def own_window(whole, height, width, ring):
    row = lax.axis_index(ROWS) * height
    col = lax.axis_index(COLS) * width
    lead = whole.shape[:-2]
    pads = [(0, 0)] * len(lead) + [(ring, ring), (ring, ring)]
    padded = jnp.pad(whole, pads) if ring else whole
    return lax.dynamic_slice(
        padded, (0,) * len(lead) + (row, col), lead + (height + 2 * ring, width + 2 * ring)
    )


def inside(height, width, ext):
    rows = lax.axis_index(ROWS) * height - ext + lax.broadcasted_iota(
        jnp.int32, (height + 2 * ext, width + 2 * ext), 0
    )
    cols = lax.axis_index(COLS) * width - ext + lax.broadcasted_iota(
        jnp.int32, (height + 2 * ext, width + 2 * ext), 1
    )
    return (
        (rows >= 0)
        & (rows < lax.axis_size(ROWS) * height)
        & (cols >= 0)
        & (cols < lax.axis_size(COLS) * width)
    )


def sweep_ext(iterate, source, noise, couplings, diagonal, mask):
    image = apply_ext(iterate, noise, couplings)
    new = [
        i[1:-1, 1:-1] + OMEGA * (s - a) / d for i, s, a, d in zip(iterate, source, image, diagonal)
    ]
    if mask is None:
        return new
    return [jnp.where(mask, n, 0.0) for n in new]


def level_split(source, noise, couplings, below):
    height = source[0].shape[0] - 2 * HALO
    width = source[0].shape[1] - 2 * HALO
    diagonal = diagonal_of(noise, couplings)
    ext = HALO
    mask = inside(height, width, ext)
    iterate = [jnp.where(mask, OMEGA * s / d, 0.0) for s, d in zip(source, diagonal)]
    for sweep_index in range(PRE - 1):
        ext -= 1
        cut = HALO - ext
        iterate = sweep_ext(
            iterate, crops(source, cut), crops(noise, cut), crops(couplings, cut),
            crops(diagonal, cut), inside(height, width, ext),
        )
    image = apply_ext(crops(iterate, ext - 1), crops(noise, HALO), crops(couplings, HALO))
    residual = [s - a for s, a in zip(crops(source, HALO), image)]
    coarse = below(residual)
    ring = (POST + 1) // 2
    fine = crop(prolong(coarse), 2 * ring - POST)
    iterate = [i + fine[k] for k, i in enumerate(crops(iterate, ext - POST))]
    for sweep_index in range(POST):
        ext = POST - 1 - sweep_index
        cut = HALO - ext
        iterate = sweep_ext(
            iterate, crops(source, cut), crops(noise, cut), crops(couplings, cut),
            crops(diagonal, cut), inside(height, width, ext) if ext else None,
        )
    return iterate


def spans(n, pick_last):
    mats = []
    for level in range(1, LEVELS):
        size = 1 << level
        rows = lax.broadcasted_iota(jnp.int32, (n, n // size), 0)
        cols = lax.broadcasted_iota(jnp.int32, (n, n // size), 1)
        hit = (rows == cols * size + size - 1) if pick_last else (rows // size == cols)
        mats.append(hit.astype(jnp.float32))
    return jnp.concatenate(mats, axis=1)


def hierarchy_of(noise, down, right):
    height, width = down.shape
    row_sum, row_last = spans(height, False), spans(height, True)
    col_sum, col_last = spans(width, False), spans(width, True)
    tall = jnp.concatenate(
        [
            jnp.einsum("phw,hv->pvw", noise, row_sum, precision=HIGH),
            jnp.einsum("hw,hv->vw", down, row_last, precision=HIGH)[None],
        ]
    )
    both = jnp.einsum("pvw,wu->pvu", tall, col_sum, precision=HIGH)
    wide = jnp.einsum(
        "hv,hw->vw", row_sum, jnp.einsum("hw,wu->hu", right, col_last, precision=HIGH),
        precision=HIGH,
    )
    noises, downs, rights = [noise], [down], [right]
    row, col = 0, 0
    for level in range(1, LEVELS):
        rows, cols = height >> level, width >> level
        noises.append(both[:6, row:row + rows, col:col + cols])
        downs.append(both[6, row:row + rows, col:col + cols])
        rights.append(wide[row:row + rows, col:col + cols])
        row, col = row + rows, col + cols
    return noises, downs, rights


def on_device(right_side, noise_block, edges):
    count_rows = lax.axis_size(ROWS)
    count_cols = lax.axis_size(COLS)
    height0, width0 = right_side.shape[1], right_side.shape[2]

    noises, downs, rights = hierarchy_of(noise_block, edges[0], edges[1])

    gathered = LEVELS - 1
    for level in range(LEVELS):
        height, width = height0 >> level, width0 >> level
        whole = count_rows * height * count_cols * width
        if whole <= GATHER_PIXELS or height <= HALO or width <= HALO or level == LEVELS - 1:
            gathered = level
            break

    if gathered == 0:
        packed = gather_grids(
            [jnp.concatenate([noises[l], downs[l][None], rights[l][None]]) for l in range(LEVELS)]
        )
        hierarchy = [(p[:6], p[6], p[7]) for p in packed]
        correction = cycle_whole(gather_grid(right_side), hierarchy, 0)
        return jnp.stack([own_window(c, height0, width0, 0) for c in correction])

    packed = gather_grids(
        [
            jnp.concatenate([noises[l], downs[l][None], rights[l][None]])
            for l in range(gathered, LEVELS)
        ]
    )
    hierarchy = [(p[:6], p[6], p[7]) for p in packed]
    split_inputs = []
    for level in range(gathered):
        parts = [noises[level], downs[level][None], rights[level][None]]
        if level == 0:
            parts = [right_side] + parts
        ringed = with_halo(jnp.concatenate(parts), HALO + 1)
        ringed = [ringed[k] for k in range(ringed.shape[0])]
        source = crops(ringed[:3], 1) if level == 0 else None
        if level == 0:
            ringed = ringed[3:]
        down, right = ringed[6], ringed[7]
        couplings = [down[1:-1, 1:-1], down[:-2, 1:-1], right[1:-1, 1:-1], right[1:-1, :-2]]
        split_inputs.append((source, crops(ringed[:6], 1), couplings))

    ring = (POST + 1) // 2

    def run(level, source):
        height, width = height0 >> level, width0 >> level
        _, noise, couplings = split_inputs[level]

        def below(residual):
            coarse_source = restrict_sum(jnp.stack(residual))
            if level + 1 == gathered:
                correction = cycle_whole(gather_grid(coarse_source), hierarchy, gathered)
                return own_window(jnp.stack(correction), height // 2, width // 2, ring)
            coarse = run(level + 1, list(with_halo(coarse_source, HALO)))
            return with_halo(jnp.stack(coarse), ring)

        return level_split(source, noise, couplings, below)

    return jnp.stack(run(0, split_inputs[0][0]))


def solution(mesh):
    in_specs = (
        P(None, ("groups", "tiles"), ("band", "stokes")),
        P(None, ("groups", "tiles"), ("band", "stokes")),
        P(None, ("groups", "tiles"), ("band", "stokes")),
    )
    out_specs = P(None, ("groups", "tiles"), ("band", "stokes"))
    return jax.shard_map(
        on_device, mesh=mesh, in_specs=in_specs, out_specs=out_specs, check_vma=False
    )
```

```python
import jax
import jax.numpy as jnp
from jax import lax
from jax.sharding import PartitionSpec as P

LEVELS = 5
PRE = 2
POST = 2
COARSE_SWEEPS = 8

OMEGA = 0.8

ROWS = "tiles"
COLS = ("band", "stokes")
GRID = ("tiles", "band", "stokes")

HALO = PRE - 1 + POST
GATHER_PIXELS = 32768


def with_halo(cells, width):
    for axis, dim in ((ROWS, 1), (COLS, 2)):
        count = lax.axis_size(axis)
        ends = count - 1
        head = lax.slice_in_dim(cells, 0, width, axis=dim)
        tail = lax.slice_in_dim(cells, cells.shape[dim] - width, cells.shape[dim], axis=dim)
        cells = jnp.concatenate(
            [
                lax.ppermute(tail, axis, [(i, i + 1) for i in range(ends)]),
                cells,
                lax.ppermute(head, axis, [(i + 1, i) for i in range(ends)]),
            ],
            axis=dim,
        )
    return cells


def crop(x, k):
    if k == 0:
        return x
    return x[..., k:-k, k:-k]


HIGH = lax.Precision.HIGHEST


def pairs(n, pick=None):
    rows = lax.broadcasted_iota(jnp.int32, (n, n // 2), 0)
    cols = lax.broadcasted_iota(jnp.int32, (n, n // 2), 1)
    hit = (rows // 2 == cols) if pick is None else (rows == 2 * cols + pick)
    return hit.astype(jnp.float32)


def sum_rows(x, m):
    return jnp.einsum("...hw,hv->...vw", x, m, precision=HIGH)


def sum_cols(x, m):
    return jnp.einsum("...hw,wv->...hv", x, m, precision=HIGH)


def restrict_sum(x):
    return sum_cols(sum_rows(x, pairs(x.shape[-2])), pairs(x.shape[-1]))


def restrict_down(down):
    return sum_cols(sum_rows(down, pairs(down.shape[-2], 1)), pairs(down.shape[-1]))


def restrict_right(right):
    return sum_rows(sum_cols(right, pairs(right.shape[-1], 1)), pairs(right.shape[-2]))


def prolong(coarse):
    height, width = coarse.shape[-2] * 2, coarse.shape[-1] * 2
    wider = jnp.einsum("...hv,wv->...hw", coarse, pairs(width), precision=HIGH)
    return jnp.einsum("...vw,hv->...hw", wider, pairs(height), precision=HIGH)


def apply_planes(iterate, padded, noise, couplings):
    first = noise[0] * iterate[0] + noise[3] * iterate[1] + noise[4] * iterate[2]
    second = noise[3] * iterate[0] + noise[1] * iterate[1] + noise[5] * iterate[2]
    third = noise[4] * iterate[0] + noise[5] * iterate[1] + noise[2] * iterate[2]
    totals = couplings[0] + couplings[1] + couplings[2] + couplings[3]
    image = []
    for local, core, rim in zip((first, second, third), iterate, padded):
        neighbours = (
            couplings[0] * rim[2:, 1:-1]
            + couplings[1] * rim[:-2, 1:-1]
            + couplings[2] * rim[1:-1, 2:]
            + couplings[3] * rim[1:-1, :-2]
        )
        image.append(local + totals * core - neighbours)
    return image


def apply_ext(padded, noise, couplings):
    return apply_planes([p[1:-1, 1:-1] for p in padded], padded, noise, couplings)


def diagonal_of(noise, couplings):
    totals = couplings[0] + couplings[1] + couplings[2] + couplings[3]
    return [noise[k] + totals for k in range(3)]


def couplings_from(down, right):
    upward = jnp.pad(down, ((1, 0), (0, 0)))[:-1, :]
    leftward = jnp.pad(right, ((0, 0), (1, 0)))[:, :-1]
    return [down, upward, right, leftward]


def crops(planes, k):
    return [crop(p, k) for p in planes]


def smooth_whole(iterate, source, noise, couplings, diagonal):
    image = apply_planes(iterate, [jnp.pad(p, 1) for p in iterate], noise, couplings)
    return [i + OMEGA * (s - a) / d for i, s, a, d in zip(iterate, source, image, diagonal)]


def cycle_whole(source, hierarchy, level_index):
    noise, down, right = hierarchy[0]
    couplings = couplings_from(down, right)
    diagonal = diagonal_of(noise, couplings)
    iterate = [OMEGA * s / d for s, d in zip(source, diagonal)]
    if level_index == LEVELS - 1:
        for sweep_index in range(COARSE_SWEEPS - 1):
            iterate = smooth_whole(iterate, source, noise, couplings, diagonal)
        return iterate
    for sweep_index in range(PRE - 1):
        iterate = smooth_whole(iterate, source, noise, couplings, diagonal)
    image = apply_planes(iterate, [jnp.pad(p, 1) for p in iterate], noise, couplings)
    residual = restrict_sum(jnp.stack([s - a for s, a in zip(source, image)]))
    coarse = prolong(
        jnp.stack(cycle_whole([residual[k] for k in range(3)], hierarchy[1:], level_index + 1))
    )
    iterate = [iterate[k] + coarse[k] for k in range(3)]
    for sweep_index in range(POST):
        iterate = smooth_whole(iterate, source, noise, couplings, diagonal)
    return iterate


def gather_grid(block):
    return gather_grids([block])[0]


def gather_axis(x, axis):
    count = lax.axis_size(axis)
    me = lax.axis_index(axis)
    pieces = [x] + [
        lax.ppermute(x, axis, [(i, (i + k) % count) for i in range(count)]) for k in range(1, count)
    ]
    order = (me - jnp.arange(count)) % count
    return jnp.take(jnp.stack(pieces), order, axis=0, mode="clip")


def gather_by_shifts(block):
    count_rows = lax.axis_size(ROWS)
    count_cols = lax.axis_size(COLS)
    planes, height, width = block.shape
    stacked = gather_axis(gather_axis(block, COLS), ROWS)
    whole = stacked.transpose(2, 0, 3, 1, 4).reshape(
        planes, count_rows * height, count_cols * width
    )
    return [whole[k] for k in range(planes)]


def gather_grids(blocks):
    count_rows = lax.axis_size(ROWS)
    count_cols = lax.axis_size(COLS)
    planes = blocks[0].shape[0]
    runs = [-(-b.shape[1] * b.shape[2] // 128) * 128 for b in blocks]
    flat = jnp.concatenate(
        [
            jnp.pad(b.reshape(planes, -1), ((0, 0), (0, run - b.shape[1] * b.shape[2])))
            for b, run in zip(blocks, runs)
        ],
        axis=1,
    )
    stacked = lax.all_gather(flat, GRID, axis=0, tiled=False)
    grids = []
    offset = 0
    for b, run in zip(blocks, runs):
        _, height, width = b.shape
        part = stacked[:, :, offset:offset + height * width]
        offset += run
        part = part.reshape(count_rows, count_cols, planes, height, width)
        whole = part.transpose(2, 0, 3, 1, 4).reshape(
            planes, count_rows * height, count_cols * width
        )
        grids.append([whole[k] for k in range(planes)])
    return grids


def own_window(whole, height, width, ring):
    row = lax.axis_index(ROWS) * height
    col = lax.axis_index(COLS) * width
    lead = whole.shape[:-2]
    pads = [(0, 0)] * len(lead) + [(ring, ring), (ring, ring)]
    padded = jnp.pad(whole, pads) if ring else whole
    return lax.dynamic_slice(
        padded, (0,) * len(lead) + (row, col), lead + (height + 2 * ring, width + 2 * ring)
    )


def inside(height, width, ext):
    rows = lax.axis_index(ROWS) * height - ext + lax.broadcasted_iota(
        jnp.int32, (height + 2 * ext, width + 2 * ext), 0
    )
    cols = lax.axis_index(COLS) * width - ext + lax.broadcasted_iota(
        jnp.int32, (height + 2 * ext, width + 2 * ext), 1
    )
    return (
        (rows >= 0)
        & (rows < lax.axis_size(ROWS) * height)
        & (cols >= 0)
        & (cols < lax.axis_size(COLS) * width)
    )


def sweep_ext(iterate, source, noise, couplings, diagonal, mask):
    image = apply_ext(iterate, noise, couplings)
    new = [
        i[1:-1, 1:-1] + OMEGA * (s - a) / d for i, s, a, d in zip(iterate, source, image, diagonal)
    ]
    if mask is None:
        return new
    return [jnp.where(mask, n, 0.0) for n in new]


def level_split(source, noise, couplings, below):
    height = source[0].shape[0] - 2 * HALO
    width = source[0].shape[1] - 2 * HALO
    diagonal = diagonal_of(noise, couplings)
    ext = HALO
    mask = inside(height, width, ext)
    iterate = [jnp.where(mask, OMEGA * s / d, 0.0) for s, d in zip(source, diagonal)]
    for sweep_index in range(PRE - 1):
        ext -= 1
        cut = HALO - ext
        iterate = sweep_ext(
            iterate, crops(source, cut), crops(noise, cut), crops(couplings, cut),
            crops(diagonal, cut), inside(height, width, ext),
        )
    image = apply_ext(crops(iterate, ext - 1), crops(noise, HALO), crops(couplings, HALO))
    residual = [s - a for s, a in zip(crops(source, HALO), image)]
    coarse = below(residual)
    ring = (POST + 1) // 2
    fine = crop(prolong(coarse), 2 * ring - POST)
    iterate = [i + fine[k] for k, i in enumerate(crops(iterate, ext - POST))]
    for sweep_index in range(POST):
        ext = POST - 1 - sweep_index
        cut = HALO - ext
        iterate = sweep_ext(
            iterate, crops(source, cut), crops(noise, cut), crops(couplings, cut),
            crops(diagonal, cut), inside(height, width, ext) if ext else None,
        )
    return iterate


def spans(n, pick_last):
    mats = []
    for level in range(1, LEVELS):
        size = 1 << level
        rows = lax.broadcasted_iota(jnp.int32, (n, n // size), 0)
        cols = lax.broadcasted_iota(jnp.int32, (n, n // size), 1)
        hit = (rows == cols * size + size - 1) if pick_last else (rows // size == cols)
        mats.append(hit.astype(jnp.float32))
    return jnp.concatenate(mats, axis=1)


def hierarchy_of(noise, down, right):
    height, width = down.shape
    row_sum, row_last = spans(height, False), spans(height, True)
    col_sum, col_last = spans(width, False), spans(width, True)
    tall = jnp.concatenate(
        [
            jnp.einsum("phw,hv->pvw", noise, row_sum, precision=HIGH),
            jnp.einsum("hw,hv->vw", down, row_last, precision=HIGH)[None],
        ]
    )
    both = jnp.einsum("pvw,wu->pvu", tall, col_sum, precision=HIGH)
    wide = jnp.einsum(
        "hv,hw->vw", row_sum, jnp.einsum("hw,wu->hu", right, col_last, precision=HIGH),
        precision=HIGH,
    )
    noises, downs, rights = [noise], [down], [right]
    row, col = 0, 0
    for level in range(1, LEVELS):
        rows, cols = height >> level, width >> level
        noises.append(both[:6, row:row + rows, col:col + cols])
        downs.append(both[6, row:row + rows, col:col + cols])
        rights.append(wide[row:row + rows, col:col + cols])
        row, col = row + rows, col + cols
    return noises, downs, rights


def on_device(right_side, noise_block, edges):
    count_rows = lax.axis_size(ROWS)
    count_cols = lax.axis_size(COLS)
    height0, width0 = right_side.shape[1], right_side.shape[2]

    noises, downs, rights = hierarchy_of(noise_block, edges[0], edges[1])

    gathered = LEVELS - 1
    for level in range(LEVELS):
        height, width = height0 >> level, width0 >> level
        whole = count_rows * height * count_cols * width
        if whole <= GATHER_PIXELS or height <= HALO or width <= HALO or level == LEVELS - 1:
            gathered = level
            break

    if gathered == 0:
        packed = gather_grids(
            [jnp.concatenate([noises[l], downs[l][None], rights[l][None]]) for l in range(LEVELS)]
        )
        hierarchy = [(p[:6], p[6], p[7]) for p in packed]
        correction = cycle_whole(gather_grid(right_side), hierarchy, 0)
        return jnp.stack([own_window(c, height0, width0, 0) for c in correction])

    packed = gather_grids(
        [
            jnp.concatenate([noises[l], downs[l][None], rights[l][None]])
            for l in range(gathered, LEVELS)
        ]
    )
    hierarchy = [(p[:6], p[6], p[7]) for p in packed]
    split_inputs = []
    for level in range(gathered):
        parts = [noises[level], downs[level][None], rights[level][None]]
        if level == 0:
            parts = [right_side] + parts
        ringed = with_halo(jnp.concatenate(parts), HALO + 1)
        ringed = [ringed[k] for k in range(ringed.shape[0])]
        source = crops(ringed[:3], 1) if level == 0 else None
        if level == 0:
            ringed = ringed[3:]
        down, right = ringed[6], ringed[7]
        couplings = [down[1:-1, 1:-1], down[:-2, 1:-1], right[1:-1, 1:-1], right[1:-1, :-2]]
        split_inputs.append((source, crops(ringed[:6], 1), couplings))

    ring = (POST + 1) // 2

    def run(level, source):
        height, width = height0 >> level, width0 >> level
        _, noise, couplings = split_inputs[level]

        def below(residual):
            coarse_source = restrict_sum(jnp.stack(residual))
            if level + 1 == gathered:
                correction = cycle_whole(gather_by_shifts(coarse_source), hierarchy, gathered)
                return own_window(jnp.stack(correction), height // 2, width // 2, ring)
            coarse = run(level + 1, list(with_halo(coarse_source, HALO)))
            return with_halo(jnp.stack(coarse), ring)

        return level_split(source, noise, couplings, below)

    return jnp.stack(run(0, split_inputs[0][0]))


def solution(mesh):
    in_specs = (
        P(None, ("groups", "tiles"), ("band", "stokes")),
        P(None, ("groups", "tiles"), ("band", "stokes")),
        P(None, ("groups", "tiles"), ("band", "stokes")),
    )
    out_specs = P(None, ("groups", "tiles"), ("band", "stokes"))
    return jax.shard_map(
        on_device, mesh=mesh, in_specs=in_specs, out_specs=out_specs, check_vma=False
    )
```

```python
import jax
import jax.numpy as jnp
from jax import lax
from jax.sharding import PartitionSpec as P

LEVELS = 5
PRE = 2
POST = 2
COARSE_SWEEPS = 8

OMEGA = 0.8

ROWS = "tiles"
COLS = ("band", "stokes")
GRID = ("tiles", "band", "stokes")

HALO = PRE - 1 + POST
GATHER_PIXELS = 32768


def with_halo(cells, width):
    for axis, dim in ((ROWS, 1), (COLS, 2)):
        count = lax.axis_size(axis)
        ends = count - 1
        head = lax.slice_in_dim(cells, 0, width, axis=dim)
        tail = lax.slice_in_dim(cells, cells.shape[dim] - width, cells.shape[dim], axis=dim)
        cells = jnp.concatenate(
            [
                lax.ppermute(tail, axis, [(i, i + 1) for i in range(ends)]),
                cells,
                lax.ppermute(head, axis, [(i + 1, i) for i in range(ends)]),
            ],
            axis=dim,
        )
    return cells


def crop(x, k):
    if k == 0:
        return x
    return x[..., k:-k, k:-k]


HIGH = lax.Precision.HIGHEST


def pairs(n, pick=None):
    rows = lax.broadcasted_iota(jnp.int32, (n, n // 2), 0)
    cols = lax.broadcasted_iota(jnp.int32, (n, n // 2), 1)
    hit = (rows // 2 == cols) if pick is None else (rows == 2 * cols + pick)
    return hit.astype(jnp.float32)


def sum_rows(x, m):
    return jnp.einsum("...hw,hv->...vw", x, m, precision=HIGH)


def sum_cols(x, m):
    return jnp.einsum("...hw,wv->...hv", x, m, precision=HIGH)


def restrict_sum(x):
    return sum_cols(sum_rows(x, pairs(x.shape[-2])), pairs(x.shape[-1]))


def restrict_down(down):
    return sum_cols(sum_rows(down, pairs(down.shape[-2], 1)), pairs(down.shape[-1]))


def restrict_right(right):
    return sum_rows(sum_cols(right, pairs(right.shape[-1], 1)), pairs(right.shape[-2]))


def prolong(coarse):
    height, width = coarse.shape[-2] * 2, coarse.shape[-1] * 2
    wider = jnp.einsum("...hv,wv->...hw", coarse, pairs(width), precision=HIGH)
    return jnp.einsum("...vw,hv->...hw", wider, pairs(height), precision=HIGH)


def apply_planes(iterate, padded, noise, couplings):
    first = noise[0] * iterate[0] + noise[3] * iterate[1] + noise[4] * iterate[2]
    second = noise[3] * iterate[0] + noise[1] * iterate[1] + noise[5] * iterate[2]
    third = noise[4] * iterate[0] + noise[5] * iterate[1] + noise[2] * iterate[2]
    totals = couplings[0] + couplings[1] + couplings[2] + couplings[3]
    image = []
    for local, core, rim in zip((first, second, third), iterate, padded):
        neighbours = (
            couplings[0] * rim[2:, 1:-1]
            + couplings[1] * rim[:-2, 1:-1]
            + couplings[2] * rim[1:-1, 2:]
            + couplings[3] * rim[1:-1, :-2]
        )
        image.append(local + totals * core - neighbours)
    return image


def apply_ext(padded, noise, couplings):
    return apply_planes([p[1:-1, 1:-1] for p in padded], padded, noise, couplings)


def diagonal_of(noise, couplings):
    totals = couplings[0] + couplings[1] + couplings[2] + couplings[3]
    return [noise[k] + totals for k in range(3)]


def couplings_from(down, right):
    upward = jnp.pad(down, ((1, 0), (0, 0)))[:-1, :]
    leftward = jnp.pad(right, ((0, 0), (1, 0)))[:, :-1]
    return [down, upward, right, leftward]


def crops(planes, k):
    return [crop(p, k) for p in planes]


def smooth_whole(iterate, source, noise, couplings, diagonal):
    image = apply_planes(iterate, [jnp.pad(p, 1) for p in iterate], noise, couplings)
    return [i + OMEGA * (s - a) / d for i, s, a, d in zip(iterate, source, image, diagonal)]


def cycle_whole(source, hierarchy, level_index):
    noise, down, right = hierarchy[0]
    couplings = couplings_from(down, right)
    diagonal = diagonal_of(noise, couplings)
    iterate = [OMEGA * s / d for s, d in zip(source, diagonal)]
    if level_index == LEVELS - 1:
        for sweep_index in range(COARSE_SWEEPS - 1):
            iterate = smooth_whole(iterate, source, noise, couplings, diagonal)
        return iterate
    for sweep_index in range(PRE - 1):
        iterate = smooth_whole(iterate, source, noise, couplings, diagonal)
    image = apply_planes(iterate, [jnp.pad(p, 1) for p in iterate], noise, couplings)
    residual = restrict_sum(jnp.stack([s - a for s, a in zip(source, image)]))
    coarse = prolong(
        jnp.stack(cycle_whole([residual[k] for k in range(3)], hierarchy[1:], level_index + 1))
    )
    iterate = [iterate[k] + coarse[k] for k in range(3)]
    for sweep_index in range(POST):
        iterate = smooth_whole(iterate, source, noise, couplings, diagonal)
    return iterate


def gather_grid(block):
    return gather_grids([block])[0]


def gather_grids(blocks):
    count_rows = lax.axis_size(ROWS)
    count_cols = lax.axis_size(COLS)
    planes = blocks[0].shape[0]
    tiles = []
    for b in blocks:
        run = b.shape[1] * b.shape[2]
        padded = jnp.pad(b.reshape(planes, run), ((0, 0), (0, -run % 128)))
        tiles.append(padded.reshape(planes, -1, 128).transpose(1, 0, 2))
    packed = jnp.concatenate(tiles, axis=0)
    stacked = lax.all_gather(packed, GRID, axis=1, tiled=False)
    grids = []
    first = 0
    for b, t in zip(blocks, tiles):
        _, height, width = b.shape
        part = stacked[first:first + t.shape[0]]
        first += t.shape[0]
        if width % 128 == 0:
            part = part.reshape(height, width // 128, count_rows, count_cols, planes, 128)
            whole = part.transpose(4, 2, 0, 3, 1, 5)
        else:
            part = part.transpose(2, 1, 0, 3).reshape(planes, count_rows, count_cols, -1)
            part = part[..., : height * width].reshape(planes, count_rows, count_cols, height, width)
            whole = part.transpose(0, 1, 3, 2, 4)
        whole = whole.reshape(planes, count_rows * height, count_cols * width)
        grids.append([whole[k] for k in range(planes)])
    return grids


def own_window(whole, height, width, ring):
    row = lax.axis_index(ROWS) * height
    col = lax.axis_index(COLS) * width
    lead = whole.shape[:-2]
    pads = [(0, 0)] * len(lead) + [(ring, ring), (ring, ring)]
    padded = jnp.pad(whole, pads) if ring else whole
    return lax.dynamic_slice(
        padded, (0,) * len(lead) + (row, col), lead + (height + 2 * ring, width + 2 * ring)
    )


def inside(height, width, ext):
    rows = lax.axis_index(ROWS) * height - ext + lax.broadcasted_iota(
        jnp.int32, (height + 2 * ext, width + 2 * ext), 0
    )
    cols = lax.axis_index(COLS) * width - ext + lax.broadcasted_iota(
        jnp.int32, (height + 2 * ext, width + 2 * ext), 1
    )
    return (
        (rows >= 0)
        & (rows < lax.axis_size(ROWS) * height)
        & (cols >= 0)
        & (cols < lax.axis_size(COLS) * width)
    )


def sweep_ext(iterate, source, noise, couplings, diagonal, mask):
    image = apply_ext(iterate, noise, couplings)
    new = [
        i[1:-1, 1:-1] + OMEGA * (s - a) / d for i, s, a, d in zip(iterate, source, image, diagonal)
    ]
    if mask is None:
        return new
    return [jnp.where(mask, n, 0.0) for n in new]


def level_split(source, noise, couplings, below):
    height = source[0].shape[0] - 2 * HALO
    width = source[0].shape[1] - 2 * HALO
    diagonal = diagonal_of(noise, couplings)
    ext = HALO
    mask = inside(height, width, ext)
    iterate = [jnp.where(mask, OMEGA * s / d, 0.0) for s, d in zip(source, diagonal)]
    for sweep_index in range(PRE - 1):
        ext -= 1
        cut = HALO - ext
        iterate = sweep_ext(
            iterate, crops(source, cut), crops(noise, cut), crops(couplings, cut),
            crops(diagonal, cut), inside(height, width, ext),
        )
    image = apply_ext(crops(iterate, ext - 1), crops(noise, HALO), crops(couplings, HALO))
    residual = [s - a for s, a in zip(crops(source, HALO), image)]
    coarse = below(residual)
    ring = (POST + 1) // 2
    fine = crop(prolong(coarse), 2 * ring - POST)
    iterate = [i + fine[k] for k, i in enumerate(crops(iterate, ext - POST))]
    for sweep_index in range(POST):
        ext = POST - 1 - sweep_index
        cut = HALO - ext
        iterate = sweep_ext(
            iterate, crops(source, cut), crops(noise, cut), crops(couplings, cut),
            crops(diagonal, cut), inside(height, width, ext) if ext else None,
        )
    return iterate


def spans(n, pick_last):
    mats = []
    for level in range(1, LEVELS):
        size = 1 << level
        rows = lax.broadcasted_iota(jnp.int32, (n, n // size), 0)
        cols = lax.broadcasted_iota(jnp.int32, (n, n // size), 1)
        hit = (rows == cols * size + size - 1) if pick_last else (rows // size == cols)
        mats.append(hit.astype(jnp.float32))
    return jnp.concatenate(mats, axis=1)


def hierarchy_of(noise, down, right):
    height, width = down.shape
    row_sum, row_last = spans(height, False), spans(height, True)
    col_sum, col_last = spans(width, False), spans(width, True)
    tall = jnp.concatenate(
        [
            jnp.einsum("phw,hv->pvw", noise, row_sum, precision=HIGH),
            jnp.einsum("hw,hv->vw", down, row_last, precision=HIGH)[None],
        ]
    )
    both = jnp.einsum("pvw,wu->pvu", tall, col_sum, precision=HIGH)
    wide = jnp.einsum(
        "hv,hw->vw", row_sum, jnp.einsum("hw,wu->hu", right, col_last, precision=HIGH),
        precision=HIGH,
    )
    noises, downs, rights = [noise], [down], [right]
    row, col = 0, 0
    for level in range(1, LEVELS):
        rows, cols = height >> level, width >> level
        noises.append(both[:6, row:row + rows, col:col + cols])
        downs.append(both[6, row:row + rows, col:col + cols])
        rights.append(wide[row:row + rows, col:col + cols])
        row, col = row + rows, col + cols
    return noises, downs, rights


def on_device(right_side, noise_block, edges):
    count_rows = lax.axis_size(ROWS)
    count_cols = lax.axis_size(COLS)
    height0, width0 = right_side.shape[1], right_side.shape[2]

    noises, downs, rights = hierarchy_of(noise_block, edges[0], edges[1])

    gathered = LEVELS - 1
    for level in range(LEVELS):
        height, width = height0 >> level, width0 >> level
        whole = count_rows * height * count_cols * width
        if whole <= GATHER_PIXELS or height <= HALO or width <= HALO or level == LEVELS - 1:
            gathered = level
            break

    if gathered == 0:
        packed = gather_grids(
            [jnp.concatenate([noises[l], downs[l][None], rights[l][None]]) for l in range(LEVELS)]
        )
        hierarchy = [(p[:6], p[6], p[7]) for p in packed]
        correction = cycle_whole(gather_grid(right_side), hierarchy, 0)
        return jnp.stack([own_window(c, height0, width0, 0) for c in correction])

    packed = gather_grids(
        [
            jnp.concatenate([noises[l], downs[l][None], rights[l][None]])
            for l in range(gathered, LEVELS)
        ]
    )
    hierarchy = [(p[:6], p[6], p[7]) for p in packed]
    split_inputs = []
    for level in range(gathered):
        parts = [noises[level], downs[level][None], rights[level][None]]
        if level == 0:
            parts = [right_side] + parts
        ringed = with_halo(jnp.concatenate(parts), HALO + 1)
        ringed = [ringed[k] for k in range(ringed.shape[0])]
        source = crops(ringed[:3], 1) if level == 0 else None
        if level == 0:
            ringed = ringed[3:]
        down, right = ringed[6], ringed[7]
        couplings = [down[1:-1, 1:-1], down[:-2, 1:-1], right[1:-1, 1:-1], right[1:-1, :-2]]
        split_inputs.append((source, crops(ringed[:6], 1), couplings))

    ring = (POST + 1) // 2

    def run(level, source):
        height, width = height0 >> level, width0 >> level
        _, noise, couplings = split_inputs[level]

        def below(residual):
            coarse_source = restrict_sum(jnp.stack(residual))
            if level + 1 == gathered:
                correction = cycle_whole(gather_grid(coarse_source), hierarchy, gathered)
                return own_window(jnp.stack(correction), height // 2, width // 2, ring)
            coarse = run(level + 1, list(with_halo(coarse_source, HALO)))
            return with_halo(jnp.stack(coarse), ring)

        return level_split(source, noise, couplings, below)

    return jnp.stack(run(0, split_inputs[0][0]))


def solution(mesh):
    in_specs = (
        P(None, ("groups", "tiles"), ("band", "stokes")),
        P(None, ("groups", "tiles"), ("band", "stokes")),
        P(None, ("groups", "tiles"), ("band", "stokes")),
    )
    out_specs = P(None, ("groups", "tiles"), ("band", "stokes"))
    return jax.shard_map(
        on_device, mesh=mesh, in_specs=in_specs, out_specs=out_specs, check_vma=False
    )
```

```python
import jax
import jax.numpy as jnp
from jax import lax
from jax.sharding import PartitionSpec as P

LEVELS = 5
PRE = 2
POST = 2
COARSE_SWEEPS = 8

OMEGA = 0.8

ROWS = "tiles"
COLS = ("band", "stokes")
GRID = ("tiles", "band", "stokes")

HALO = PRE - 1 + POST
GATHER_PIXELS = 32768


def with_halo(cells, width):
    for axis, dim in ((ROWS, 1), (COLS, 2)):
        count = lax.axis_size(axis)
        ends = count - 1
        head = lax.slice_in_dim(cells, 0, width, axis=dim)
        tail = lax.slice_in_dim(cells, cells.shape[dim] - width, cells.shape[dim], axis=dim)
        cells = jnp.concatenate(
            [
                lax.ppermute(tail, axis, [(i, i + 1) for i in range(ends)]),
                cells,
                lax.ppermute(head, axis, [(i + 1, i) for i in range(ends)]),
            ],
            axis=dim,
        )
    return cells


def crop(x, k):
    if k == 0:
        return x
    return x[..., k:-k, k:-k]


HIGH = lax.Precision.HIGHEST


def pairs(n, pick=None):
    rows = lax.broadcasted_iota(jnp.int32, (n, n // 2), 0)
    cols = lax.broadcasted_iota(jnp.int32, (n, n // 2), 1)
    hit = (rows // 2 == cols) if pick is None else (rows == 2 * cols + pick)
    return hit.astype(jnp.float32)


def sum_rows(x, m):
    return jnp.einsum("...hw,hv->...vw", x, m, precision=HIGH)


def sum_cols(x, m):
    return jnp.einsum("...hw,wv->...hv", x, m, precision=HIGH)


def restrict_sum(x):
    return sum_cols(sum_rows(x, pairs(x.shape[-2])), pairs(x.shape[-1]))


def restrict_down(down):
    return sum_cols(sum_rows(down, pairs(down.shape[-2], 1)), pairs(down.shape[-1]))


def restrict_right(right):
    return sum_rows(sum_cols(right, pairs(right.shape[-1], 1)), pairs(right.shape[-2]))


def prolong(coarse):
    height, width = coarse.shape[-2] * 2, coarse.shape[-1] * 2
    wider = jnp.einsum("...hv,wv->...hw", coarse, pairs(width), precision=HIGH)
    return jnp.einsum("...vw,hv->...hw", wider, pairs(height), precision=HIGH)


def apply_planes(iterate, padded, noise, couplings):
    first = noise[0] * iterate[0] + noise[3] * iterate[1] + noise[4] * iterate[2]
    second = noise[3] * iterate[0] + noise[1] * iterate[1] + noise[5] * iterate[2]
    third = noise[4] * iterate[0] + noise[5] * iterate[1] + noise[2] * iterate[2]
    totals = couplings[0] + couplings[1] + couplings[2] + couplings[3]
    image = []
    for local, core, rim in zip((first, second, third), iterate, padded):
        neighbours = (
            couplings[0] * rim[2:, 1:-1]
            + couplings[1] * rim[:-2, 1:-1]
            + couplings[2] * rim[1:-1, 2:]
            + couplings[3] * rim[1:-1, :-2]
        )
        image.append(local + totals * core - neighbours)
    return image


def apply_ext(padded, noise, couplings):
    return apply_planes([p[1:-1, 1:-1] for p in padded], padded, noise, couplings)


def diagonal_of(noise, couplings):
    totals = couplings[0] + couplings[1] + couplings[2] + couplings[3]
    return [noise[k] + totals for k in range(3)]


def couplings_from(down, right):
    upward = jnp.pad(down, ((1, 0), (0, 0)))[:-1, :]
    leftward = jnp.pad(right, ((0, 0), (1, 0)))[:, :-1]
    return [down, upward, right, leftward]


def crops(planes, k):
    return [crop(p, k) for p in planes]


def smooth_whole(iterate, source, noise, couplings, diagonal):
    image = apply_planes(iterate, [jnp.pad(p, 1) for p in iterate], noise, couplings)
    return [i + OMEGA * (s - a) / d for i, s, a, d in zip(iterate, source, image, diagonal)]


def cycle_whole(source, hierarchy, level_index):
    noise, down, right = hierarchy[0]
    couplings = couplings_from(down, right)
    diagonal = diagonal_of(noise, couplings)
    iterate = [OMEGA * s / d for s, d in zip(source, diagonal)]
    if level_index == LEVELS - 1:
        for sweep_index in range(COARSE_SWEEPS - 1):
            iterate = smooth_whole(iterate, source, noise, couplings, diagonal)
        return iterate
    for sweep_index in range(PRE - 1):
        iterate = smooth_whole(iterate, source, noise, couplings, diagonal)
    image = apply_planes(iterate, [jnp.pad(p, 1) for p in iterate], noise, couplings)
    residual = restrict_sum(jnp.stack([s - a for s, a in zip(source, image)]))
    coarse = prolong(cycle_stacked(residual, hierarchy[1:], level_index + 1))
    iterate = [iterate[k] + coarse[k] for k in range(3)]
    for sweep_index in range(POST):
        iterate = smooth_whole(iterate, source, noise, couplings, diagonal)
    return iterate


def apply_stacked(iterate, noise, couplings):
    padded = jnp.pad(iterate, ((0, 0), (1, 1), (1, 1)))
    first = noise[0] * iterate[0] + noise[3] * iterate[1] + noise[4] * iterate[2]
    second = noise[3] * iterate[0] + noise[1] * iterate[1] + noise[5] * iterate[2]
    third = noise[4] * iterate[0] + noise[5] * iterate[1] + noise[2] * iterate[2]
    totals = couplings[0] + couplings[1] + couplings[2] + couplings[3]
    neighbours = (
        couplings[0] * padded[:, 2:, 1:-1]
        + couplings[1] * padded[:, :-2, 1:-1]
        + couplings[2] * padded[:, 1:-1, 2:]
        + couplings[3] * padded[:, 1:-1, :-2]
    )
    return jnp.stack([first, second, third]) + totals * iterate - neighbours


def cycle_stacked(source, hierarchy, level_index):
    noise, down, right = hierarchy[0]
    noise = jnp.stack(noise)
    couplings = jnp.stack(couplings_from(down, right))
    diagonal = noise[0:3] + (couplings[0] + couplings[1] + couplings[2] + couplings[3])
    iterate = OMEGA * source / diagonal
    sweeps = COARSE_SWEEPS - 1 if level_index == LEVELS - 1 else PRE - 1
    for sweep_index in range(sweeps):
        iterate = iterate + OMEGA * (source - apply_stacked(iterate, noise, couplings)) / diagonal
    if level_index == LEVELS - 1:
        return iterate
    residual = restrict_sum(source - apply_stacked(iterate, noise, couplings))
    iterate = iterate + prolong(cycle_stacked(residual, hierarchy[1:], level_index + 1))
    for sweep_index in range(POST):
        iterate = iterate + OMEGA * (source - apply_stacked(iterate, noise, couplings)) / diagonal
    return iterate


def gather_grid(block):
    return gather_grids([block])[0]


def gather_grids(blocks):
    count_rows = lax.axis_size(ROWS)
    count_cols = lax.axis_size(COLS)
    planes = blocks[0].shape[0]
    tiles = []
    for b in blocks:
        run = b.shape[1] * b.shape[2]
        padded = jnp.pad(b.reshape(planes, run), ((0, 0), (0, -run % 128)))
        tiles.append(padded.reshape(planes, -1, 128).transpose(1, 0, 2))
    packed = jnp.concatenate(tiles, axis=0)
    stacked = lax.all_gather(packed, GRID, axis=1, tiled=False)
    grids = []
    first = 0
    for b, t in zip(blocks, tiles):
        _, height, width = b.shape
        part = stacked[first:first + t.shape[0]]
        first += t.shape[0]
        if width % 128 == 0:
            part = part.reshape(height, width // 128, count_rows, count_cols, planes, 128)
            whole = part.transpose(4, 2, 0, 3, 1, 5)
        else:
            part = part.transpose(2, 1, 0, 3).reshape(planes, count_rows, count_cols, -1)
            part = part[..., : height * width].reshape(planes, count_rows, count_cols, height, width)
            whole = part.transpose(0, 1, 3, 2, 4)
        whole = whole.reshape(planes, count_rows * height, count_cols * width)
        grids.append([whole[k] for k in range(planes)])
    return grids


def own_window(whole, height, width, ring):
    row = lax.axis_index(ROWS) * height
    col = lax.axis_index(COLS) * width
    lead = whole.shape[:-2]
    pads = [(0, 0)] * len(lead) + [(ring, ring), (ring, ring)]
    padded = jnp.pad(whole, pads) if ring else whole
    return lax.dynamic_slice(
        padded, (0,) * len(lead) + (row, col), lead + (height + 2 * ring, width + 2 * ring)
    )


def inside(height, width, ext):
    rows = lax.axis_index(ROWS) * height - ext + lax.broadcasted_iota(
        jnp.int32, (height + 2 * ext, width + 2 * ext), 0
    )
    cols = lax.axis_index(COLS) * width - ext + lax.broadcasted_iota(
        jnp.int32, (height + 2 * ext, width + 2 * ext), 1
    )
    return (
        (rows >= 0)
        & (rows < lax.axis_size(ROWS) * height)
        & (cols >= 0)
        & (cols < lax.axis_size(COLS) * width)
    )


def sweep_ext(iterate, source, noise, couplings, diagonal, mask):
    image = apply_ext(iterate, noise, couplings)
    new = [
        i[1:-1, 1:-1] + OMEGA * (s - a) / d for i, s, a, d in zip(iterate, source, image, diagonal)
    ]
    if mask is None:
        return new
    return [jnp.where(mask, n, 0.0) for n in new]


def level_split(source, noise, couplings, below):
    height = source[0].shape[0] - 2 * HALO
    width = source[0].shape[1] - 2 * HALO
    diagonal = diagonal_of(noise, couplings)
    ext = HALO
    mask = inside(height, width, ext)
    iterate = [jnp.where(mask, OMEGA * s / d, 0.0) for s, d in zip(source, diagonal)]
    for sweep_index in range(PRE - 1):
        ext -= 1
        cut = HALO - ext
        iterate = sweep_ext(
            iterate, crops(source, cut), crops(noise, cut), crops(couplings, cut),
            crops(diagonal, cut), inside(height, width, ext),
        )
    image = apply_ext(crops(iterate, ext - 1), crops(noise, HALO), crops(couplings, HALO))
    residual = [s - a for s, a in zip(crops(source, HALO), image)]
    coarse = below(residual)
    ring = (POST + 1) // 2
    fine = crop(prolong(coarse), 2 * ring - POST)
    iterate = [i + fine[k] for k, i in enumerate(crops(iterate, ext - POST))]
    for sweep_index in range(POST):
        ext = POST - 1 - sweep_index
        cut = HALO - ext
        iterate = sweep_ext(
            iterate, crops(source, cut), crops(noise, cut), crops(couplings, cut),
            crops(diagonal, cut), inside(height, width, ext) if ext else None,
        )
    return iterate


def spans(n, pick_last):
    mats = []
    for level in range(1, LEVELS):
        size = 1 << level
        rows = lax.broadcasted_iota(jnp.int32, (n, n // size), 0)
        cols = lax.broadcasted_iota(jnp.int32, (n, n // size), 1)
        hit = (rows == cols * size + size - 1) if pick_last else (rows // size == cols)
        mats.append(hit.astype(jnp.float32))
    return jnp.concatenate(mats, axis=1)


def hierarchy_of(noise, down, right):
    height, width = down.shape
    row_sum, row_last = spans(height, False), spans(height, True)
    col_sum, col_last = spans(width, False), spans(width, True)
    tall = jnp.concatenate(
        [
            jnp.einsum("phw,hv->pvw", noise, row_sum, precision=HIGH),
            jnp.einsum("hw,hv->vw", down, row_last, precision=HIGH)[None],
        ]
    )
    both = jnp.einsum("pvw,wu->pvu", tall, col_sum, precision=HIGH)
    wide = jnp.einsum(
        "hv,hw->vw", row_sum, jnp.einsum("hw,wu->hu", right, col_last, precision=HIGH),
        precision=HIGH,
    )
    noises, downs, rights = [noise], [down], [right]
    row, col = 0, 0
    for level in range(1, LEVELS):
        rows, cols = height >> level, width >> level
        noises.append(both[:6, row:row + rows, col:col + cols])
        downs.append(both[6, row:row + rows, col:col + cols])
        rights.append(wide[row:row + rows, col:col + cols])
        row, col = row + rows, col + cols
    return noises, downs, rights


def on_device(right_side, noise_block, edges):
    count_rows = lax.axis_size(ROWS)
    count_cols = lax.axis_size(COLS)
    height0, width0 = right_side.shape[1], right_side.shape[2]

    noises, downs, rights = hierarchy_of(noise_block, edges[0], edges[1])

    gathered = LEVELS - 1
    for level in range(LEVELS):
        height, width = height0 >> level, width0 >> level
        whole = count_rows * height * count_cols * width
        if whole <= GATHER_PIXELS or height <= HALO or width <= HALO or level == LEVELS - 1:
            gathered = level
            break

    if gathered == 0:
        packed = gather_grids(
            [jnp.concatenate([noises[l], downs[l][None], rights[l][None]]) for l in range(LEVELS)]
        )
        hierarchy = [(p[:6], p[6], p[7]) for p in packed]
        correction = cycle_whole(gather_grid(right_side), hierarchy, 0)
        return jnp.stack([own_window(c, height0, width0, 0) for c in correction])

    packed = gather_grids(
        [
            jnp.concatenate([noises[l], downs[l][None], rights[l][None]])
            for l in range(gathered, LEVELS)
        ]
    )
    hierarchy = [(p[:6], p[6], p[7]) for p in packed]
    split_inputs = []
    for level in range(gathered):
        parts = [noises[level], downs[level][None], rights[level][None]]
        if level == 0:
            parts = [right_side] + parts
        ringed = with_halo(jnp.concatenate(parts), HALO + 1)
        ringed = [ringed[k] for k in range(ringed.shape[0])]
        source = crops(ringed[:3], 1) if level == 0 else None
        if level == 0:
            ringed = ringed[3:]
        down, right = ringed[6], ringed[7]
        couplings = [down[1:-1, 1:-1], down[:-2, 1:-1], right[1:-1, 1:-1], right[1:-1, :-2]]
        split_inputs.append((source, crops(ringed[:6], 1), couplings))

    ring = (POST + 1) // 2

    def run(level, source):
        height, width = height0 >> level, width0 >> level
        _, noise, couplings = split_inputs[level]

        def below(residual):
            coarse_source = restrict_sum(jnp.stack(residual))
            if level + 1 == gathered:
                correction = cycle_whole(gather_grid(coarse_source), hierarchy, gathered)
                return own_window(jnp.stack(correction), height // 2, width // 2, ring)
            coarse = run(level + 1, list(with_halo(coarse_source, HALO)))
            return with_halo(jnp.stack(coarse), ring)

        return level_split(source, noise, couplings, below)

    return jnp.stack(run(0, split_inputs[0][0]))


def solution(mesh):
    in_specs = (
        P(None, ("groups", "tiles"), ("band", "stokes")),
        P(None, ("groups", "tiles"), ("band", "stokes")),
        P(None, ("groups", "tiles"), ("band", "stokes")),
    )
    out_specs = P(None, ("groups", "tiles"), ("band", "stokes"))
    return jax.shard_map(
        on_device, mesh=mesh, in_specs=in_specs, out_specs=out_specs, check_vma=False
    )
```

```python
import jax
import jax.numpy as jnp
from jax import lax
from jax.sharding import PartitionSpec as P

LEVELS = 5
PRE = 2
POST = 2
COARSE_SWEEPS = 8

OMEGA = 0.8

ROWS = "tiles"
COLS = ("band", "stokes")
GRID = ("tiles", "band", "stokes")

HALO = PRE - 1 + POST
GATHER_PIXELS = 32768


def with_halo(cells, width):
    for axis, dim in ((ROWS, 1), (COLS, 2)):
        count = lax.axis_size(axis)
        ends = count - 1
        head = lax.slice_in_dim(cells, 0, width, axis=dim)
        tail = lax.slice_in_dim(cells, cells.shape[dim] - width, cells.shape[dim], axis=dim)
        cells = jnp.concatenate(
            [
                lax.ppermute(tail, axis, [(i, i + 1) for i in range(ends)]),
                cells,
                lax.ppermute(head, axis, [(i + 1, i) for i in range(ends)]),
            ],
            axis=dim,
        )
    return cells


def crop(x, k):
    if k == 0:
        return x
    return x[..., k:-k, k:-k]


HIGH = lax.Precision.HIGHEST


def pairs(n, pick=None):
    rows = lax.broadcasted_iota(jnp.int32, (n, n // 2), 0)
    cols = lax.broadcasted_iota(jnp.int32, (n, n // 2), 1)
    hit = (rows // 2 == cols) if pick is None else (rows == 2 * cols + pick)
    return hit.astype(jnp.float32)


def sum_rows(x, m):
    return jnp.einsum("...hw,hv->...vw", x, m, precision=HIGH)


def sum_cols(x, m):
    return jnp.einsum("...hw,wv->...hv", x, m, precision=HIGH)


def restrict_sum(x):
    return sum_cols(sum_rows(x, pairs(x.shape[-2])), pairs(x.shape[-1]))


def restrict_down(down):
    return sum_cols(sum_rows(down, pairs(down.shape[-2], 1)), pairs(down.shape[-1]))


def restrict_right(right):
    return sum_rows(sum_cols(right, pairs(right.shape[-1], 1)), pairs(right.shape[-2]))


def prolong(coarse):
    height, width = coarse.shape[-2] * 2, coarse.shape[-1] * 2
    wider = copy_dot("...hv,wv->...hw", coarse, pairs(width))
    return copy_dot("...vw,hv->...hw", wider, pairs(height))


def copy_dot(spec, x, picks):
    high = lax.reduce_precision(x, exponent_bits=8, mantissa_bits=7)
    rest = x - high
    middle = lax.reduce_precision(rest, exponent_bits=8, mantissa_bits=7)
    low = rest - middle
    picks = picks.astype(jnp.bfloat16)
    part = [
        jnp.einsum(spec, p.astype(jnp.bfloat16), picks, preferred_element_type=jnp.float32)
        for p in (high, middle, low)
    ]
    return (part[0] + part[1]) + part[2]


def apply_planes(iterate, padded, noise, couplings):
    first = noise[0] * iterate[0] + noise[3] * iterate[1] + noise[4] * iterate[2]
    second = noise[3] * iterate[0] + noise[1] * iterate[1] + noise[5] * iterate[2]
    third = noise[4] * iterate[0] + noise[5] * iterate[1] + noise[2] * iterate[2]
    totals = couplings[0] + couplings[1] + couplings[2] + couplings[3]
    image = []
    for local, core, rim in zip((first, second, third), iterate, padded):
        neighbours = (
            couplings[0] * rim[2:, 1:-1]
            + couplings[1] * rim[:-2, 1:-1]
            + couplings[2] * rim[1:-1, 2:]
            + couplings[3] * rim[1:-1, :-2]
        )
        image.append(local + totals * core - neighbours)
    return image


def apply_ext(padded, noise, couplings):
    return apply_planes([p[1:-1, 1:-1] for p in padded], padded, noise, couplings)


def diagonal_of(noise, couplings):
    totals = couplings[0] + couplings[1] + couplings[2] + couplings[3]
    return [noise[k] + totals for k in range(3)]


def couplings_from(down, right):
    upward = jnp.pad(down, ((1, 0), (0, 0)))[:-1, :]
    leftward = jnp.pad(right, ((0, 0), (1, 0)))[:, :-1]
    return [down, upward, right, leftward]


def crops(planes, k):
    return [crop(p, k) for p in planes]


def smooth_whole(iterate, source, noise, couplings, diagonal):
    image = apply_planes(iterate, [jnp.pad(p, 1) for p in iterate], noise, couplings)
    return [i + OMEGA * (s - a) / d for i, s, a, d in zip(iterate, source, image, diagonal)]


def cycle_whole(source, hierarchy, level_index):
    noise, down, right = hierarchy[0]
    couplings = couplings_from(down, right)
    diagonal = diagonal_of(noise, couplings)
    iterate = [OMEGA * s / d for s, d in zip(source, diagonal)]
    if level_index == LEVELS - 1:
        for sweep_index in range(COARSE_SWEEPS - 1):
            iterate = smooth_whole(iterate, source, noise, couplings, diagonal)
        return iterate
    for sweep_index in range(PRE - 1):
        iterate = smooth_whole(iterate, source, noise, couplings, diagonal)
    image = apply_planes(iterate, [jnp.pad(p, 1) for p in iterate], noise, couplings)
    residual = restrict_sum(jnp.stack([s - a for s, a in zip(source, image)]))
    coarse = prolong(
        jnp.stack(cycle_whole([residual[k] for k in range(3)], hierarchy[1:], level_index + 1))
    )
    iterate = [iterate[k] + coarse[k] for k in range(3)]
    for sweep_index in range(POST):
        iterate = smooth_whole(iterate, source, noise, couplings, diagonal)
    return iterate


def gather_grid(block):
    return gather_grids([block])[0]


def gather_grids(blocks):
    count_rows = lax.axis_size(ROWS)
    count_cols = lax.axis_size(COLS)
    planes = blocks[0].shape[0]
    tiles = []
    for b in blocks:
        run = b.shape[1] * b.shape[2]
        padded = jnp.pad(b.reshape(planes, run), ((0, 0), (0, -run % 128)))
        tiles.append(padded.reshape(planes, -1, 128).transpose(1, 0, 2))
    packed = jnp.concatenate(tiles, axis=0)
    stacked = lax.all_gather(packed, GRID, axis=1, tiled=False)
    grids = []
    first = 0
    for b, t in zip(blocks, tiles):
        _, height, width = b.shape
        part = stacked[first:first + t.shape[0]]
        first += t.shape[0]
        if width % 128 == 0:
            part = part.reshape(height, width // 128, count_rows, count_cols, planes, 128)
            whole = part.transpose(4, 2, 0, 3, 1, 5)
        else:
            part = part.transpose(2, 1, 0, 3).reshape(planes, count_rows, count_cols, -1)
            part = part[..., : height * width].reshape(planes, count_rows, count_cols, height, width)
            whole = part.transpose(0, 1, 3, 2, 4)
        whole = whole.reshape(planes, count_rows * height, count_cols * width)
        grids.append([whole[k] for k in range(planes)])
    return grids


def own_window(whole, height, width, ring):
    row = lax.axis_index(ROWS) * height
    col = lax.axis_index(COLS) * width
    lead = whole.shape[:-2]
    pads = [(0, 0)] * len(lead) + [(ring, ring), (ring, ring)]
    padded = jnp.pad(whole, pads) if ring else whole
    return lax.dynamic_slice(
        padded, (0,) * len(lead) + (row, col), lead + (height + 2 * ring, width + 2 * ring)
    )


def inside(height, width, ext):
    rows = lax.axis_index(ROWS) * height - ext + lax.broadcasted_iota(
        jnp.int32, (height + 2 * ext, width + 2 * ext), 0
    )
    cols = lax.axis_index(COLS) * width - ext + lax.broadcasted_iota(
        jnp.int32, (height + 2 * ext, width + 2 * ext), 1
    )
    return (
        (rows >= 0)
        & (rows < lax.axis_size(ROWS) * height)
        & (cols >= 0)
        & (cols < lax.axis_size(COLS) * width)
    )


def sweep_ext(iterate, source, noise, couplings, diagonal, mask):
    image = apply_ext(iterate, noise, couplings)
    new = [
        i[1:-1, 1:-1] + OMEGA * (s - a) / d for i, s, a, d in zip(iterate, source, image, diagonal)
    ]
    if mask is None:
        return new
    return [jnp.where(mask, n, 0.0) for n in new]


def level_split(source, noise, couplings, below):
    height = source[0].shape[0] - 2 * HALO
    width = source[0].shape[1] - 2 * HALO
    diagonal = diagonal_of(noise, couplings)
    ext = HALO
    mask = inside(height, width, ext)
    iterate = [jnp.where(mask, OMEGA * s / d, 0.0) for s, d in zip(source, diagonal)]
    for sweep_index in range(PRE - 1):
        ext -= 1
        cut = HALO - ext
        iterate = sweep_ext(
            iterate, crops(source, cut), crops(noise, cut), crops(couplings, cut),
            crops(diagonal, cut), inside(height, width, ext),
        )
    image = apply_ext(crops(iterate, ext - 1), crops(noise, HALO), crops(couplings, HALO))
    residual = [s - a for s, a in zip(crops(source, HALO), image)]
    coarse = below(residual)
    ring = (POST + 1) // 2
    fine = crop(prolong(coarse), 2 * ring - POST)
    iterate = [i + fine[k] for k, i in enumerate(crops(iterate, ext - POST))]
    for sweep_index in range(POST):
        ext = POST - 1 - sweep_index
        cut = HALO - ext
        iterate = sweep_ext(
            iterate, crops(source, cut), crops(noise, cut), crops(couplings, cut),
            crops(diagonal, cut), inside(height, width, ext) if ext else None,
        )
    return iterate


def spans(n, pick_last):
    mats = []
    for level in range(1, LEVELS):
        size = 1 << level
        rows = lax.broadcasted_iota(jnp.int32, (n, n // size), 0)
        cols = lax.broadcasted_iota(jnp.int32, (n, n // size), 1)
        hit = (rows == cols * size + size - 1) if pick_last else (rows // size == cols)
        mats.append(hit.astype(jnp.float32))
    return jnp.concatenate(mats, axis=1)


def hierarchy_of(noise, down, right):
    height, width = down.shape
    row_sum, row_last = spans(height, False), spans(height, True)
    col_sum, col_last = spans(width, False), spans(width, True)
    tall = jnp.concatenate(
        [
            jnp.einsum("phw,hv->pvw", noise, row_sum, precision=HIGH),
            jnp.einsum("hw,hv->vw", down, row_last, precision=HIGH)[None],
        ]
    )
    both = jnp.einsum("pvw,wu->pvu", tall, col_sum, precision=HIGH)
    wide = jnp.einsum(
        "hv,hw->vw", row_sum, jnp.einsum("hw,wu->hu", right, col_last, precision=HIGH),
        precision=HIGH,
    )
    noises, downs, rights = [noise], [down], [right]
    row, col = 0, 0
    for level in range(1, LEVELS):
        rows, cols = height >> level, width >> level
        noises.append(both[:6, row:row + rows, col:col + cols])
        downs.append(both[6, row:row + rows, col:col + cols])
        rights.append(wide[row:row + rows, col:col + cols])
        row, col = row + rows, col + cols
    return noises, downs, rights


def on_device(right_side, noise_block, edges):
    count_rows = lax.axis_size(ROWS)
    count_cols = lax.axis_size(COLS)
    height0, width0 = right_side.shape[1], right_side.shape[2]

    noises, downs, rights = hierarchy_of(noise_block, edges[0], edges[1])

    gathered = LEVELS - 1
    for level in range(LEVELS):
        height, width = height0 >> level, width0 >> level
        whole = count_rows * height * count_cols * width
        if whole <= GATHER_PIXELS or height <= HALO or width <= HALO or level == LEVELS - 1:
            gathered = level
            break

    if gathered == 0:
        packed = gather_grids(
            [jnp.concatenate([noises[l], downs[l][None], rights[l][None]]) for l in range(LEVELS)]
        )
        hierarchy = [(p[:6], p[6], p[7]) for p in packed]
        correction = cycle_whole(gather_grid(right_side), hierarchy, 0)
        return jnp.stack([own_window(c, height0, width0, 0) for c in correction])

    packed = gather_grids(
        [
            jnp.concatenate([noises[l], downs[l][None], rights[l][None]])
            for l in range(gathered, LEVELS)
        ]
    )
    hierarchy = [(p[:6], p[6], p[7]) for p in packed]
    split_inputs = []
    for level in range(gathered):
        parts = [noises[level], downs[level][None], rights[level][None]]
        if level == 0:
            parts = [right_side] + parts
        ringed = with_halo(jnp.concatenate(parts), HALO + 1)
        ringed = [ringed[k] for k in range(ringed.shape[0])]
        source = crops(ringed[:3], 1) if level == 0 else None
        if level == 0:
            ringed = ringed[3:]
        down, right = ringed[6], ringed[7]
        couplings = [down[1:-1, 1:-1], down[:-2, 1:-1], right[1:-1, 1:-1], right[1:-1, :-2]]
        split_inputs.append((source, crops(ringed[:6], 1), couplings))

    ring = (POST + 1) // 2

    def run(level, source):
        height, width = height0 >> level, width0 >> level
        _, noise, couplings = split_inputs[level]

        def below(residual):
            coarse_source = restrict_sum(jnp.stack(residual))
            if level + 1 == gathered:
                correction = cycle_whole(gather_grid(coarse_source), hierarchy, gathered)
                return own_window(jnp.stack(correction), height // 2, width // 2, ring)
            coarse = run(level + 1, list(with_halo(coarse_source, HALO)))
            return with_halo(jnp.stack(coarse), ring)

        return level_split(source, noise, couplings, below)

    return jnp.stack(run(0, split_inputs[0][0]))


def solution(mesh):
    in_specs = (
        P(None, ("groups", "tiles"), ("band", "stokes")),
        P(None, ("groups", "tiles"), ("band", "stokes")),
        P(None, ("groups", "tiles"), ("band", "stokes")),
    )
    out_specs = P(None, ("groups", "tiles"), ("band", "stokes"))
    return jax.shard_map(
        on_device, mesh=mesh, in_specs=in_specs, out_specs=out_specs, check_vma=False
    )
```

```python
import jax
import jax.numpy as jnp
from jax import lax
from jax.sharding import PartitionSpec as P

LEVELS = 5
PRE = 2
POST = 2
COARSE_SWEEPS = 8

OMEGA = 0.8

ROWS = "tiles"
COLS = ("band", "stokes")
GRID = ("tiles", "band", "stokes")

HALO = PRE - 1 + POST
GATHER_PIXELS = 32768


def with_halo(cells, width):
    count_rows = lax.axis_size(ROWS)
    count_cols = lax.axis_size(COLS)
    height, breadth = cells.shape[1], cells.shape[2]
    top, bottom = cells[:, :width, :], cells[:, height - width:, :]
    left, right = cells[:, :, :width], cells[:, :, breadth - width:]

    def shift(block, axis, step):
        count = lax.axis_size(axis)
        return lax.ppermute(
            block, axis, [(i, i + step) for i in range(count) if 0 <= i + step < count]
        )

    def diagonal(block, down, across):
        pairs_ = []
        for t in range(count_rows):
            for c in range(count_cols):
                if 0 <= t + down < count_rows and 0 <= c + across < count_cols:
                    pairs_.append((t * count_cols + c, (t + down) * count_cols + c + across))
        return lax.ppermute(block, GRID, pairs_)

    north = shift(bottom, ROWS, 1)
    south = shift(top, ROWS, -1)
    west = shift(right, COLS, 1)
    east = shift(left, COLS, -1)
    north_west = diagonal(bottom[:, :, breadth - width:], 1, 1)
    north_east = diagonal(bottom[:, :, :width], 1, -1)
    south_west = diagonal(top[:, :, breadth - width:], -1, 1)
    south_east = diagonal(top[:, :, :width], -1, -1)
    return jnp.concatenate(
        [
            jnp.concatenate([north_west, north, north_east], axis=2),
            jnp.concatenate([west, cells, east], axis=2),
            jnp.concatenate([south_west, south, south_east], axis=2),
        ],
        axis=1,
    )


def crop(x, k):
    if k == 0:
        return x
    return x[..., k:-k, k:-k]


HIGH = lax.Precision.HIGHEST


def pairs(n, pick=None):
    rows = lax.broadcasted_iota(jnp.int32, (n, n // 2), 0)
    cols = lax.broadcasted_iota(jnp.int32, (n, n // 2), 1)
    hit = (rows // 2 == cols) if pick is None else (rows == 2 * cols + pick)
    return hit.astype(jnp.float32)


def sum_rows(x, m):
    return jnp.einsum("...hw,hv->...vw", x, m, precision=HIGH)


def sum_cols(x, m):
    return jnp.einsum("...hw,wv->...hv", x, m, precision=HIGH)


def restrict_sum(x):
    return sum_cols(sum_rows(x, pairs(x.shape[-2])), pairs(x.shape[-1]))


def restrict_down(down):
    return sum_cols(sum_rows(down, pairs(down.shape[-2], 1)), pairs(down.shape[-1]))


def restrict_right(right):
    return sum_rows(sum_cols(right, pairs(right.shape[-1], 1)), pairs(right.shape[-2]))


def prolong(coarse):
    height, width = coarse.shape[-2] * 2, coarse.shape[-1] * 2
    wider = jnp.einsum("...hv,wv->...hw", coarse, pairs(width), precision=HIGH)
    return jnp.einsum("...vw,hv->...hw", wider, pairs(height), precision=HIGH)


def apply_planes(iterate, padded, noise, couplings):
    first = noise[0] * iterate[0] + noise[3] * iterate[1] + noise[4] * iterate[2]
    second = noise[3] * iterate[0] + noise[1] * iterate[1] + noise[5] * iterate[2]
    third = noise[4] * iterate[0] + noise[5] * iterate[1] + noise[2] * iterate[2]
    totals = couplings[0] + couplings[1] + couplings[2] + couplings[3]
    image = []
    for local, core, rim in zip((first, second, third), iterate, padded):
        neighbours = (
            couplings[0] * rim[2:, 1:-1]
            + couplings[1] * rim[:-2, 1:-1]
            + couplings[2] * rim[1:-1, 2:]
            + couplings[3] * rim[1:-1, :-2]
        )
        image.append(local + totals * core - neighbours)
    return image


def apply_ext(padded, noise, couplings):
    return apply_planes([p[1:-1, 1:-1] for p in padded], padded, noise, couplings)


def diagonal_of(noise, couplings):
    totals = couplings[0] + couplings[1] + couplings[2] + couplings[3]
    return [noise[k] + totals for k in range(3)]


def couplings_from(down, right):
    upward = jnp.pad(down, ((1, 0), (0, 0)))[:-1, :]
    leftward = jnp.pad(right, ((0, 0), (1, 0)))[:, :-1]
    return [down, upward, right, leftward]


def crops(planes, k):
    return [crop(p, k) for p in planes]


def smooth_whole(iterate, source, noise, couplings, diagonal):
    image = apply_planes(iterate, [jnp.pad(p, 1) for p in iterate], noise, couplings)
    return [i + OMEGA * (s - a) / d for i, s, a, d in zip(iterate, source, image, diagonal)]


def cycle_whole(source, hierarchy, level_index):
    noise, down, right = hierarchy[0]
    couplings = couplings_from(down, right)
    diagonal = diagonal_of(noise, couplings)
    iterate = [OMEGA * s / d for s, d in zip(source, diagonal)]
    if level_index == LEVELS - 1:
        for sweep_index in range(COARSE_SWEEPS - 1):
            iterate = smooth_whole(iterate, source, noise, couplings, diagonal)
        return iterate
    for sweep_index in range(PRE - 1):
        iterate = smooth_whole(iterate, source, noise, couplings, diagonal)
    image = apply_planes(iterate, [jnp.pad(p, 1) for p in iterate], noise, couplings)
    residual = restrict_sum(jnp.stack([s - a for s, a in zip(source, image)]))
    coarse = prolong(
        jnp.stack(cycle_whole([residual[k] for k in range(3)], hierarchy[1:], level_index + 1))
    )
    iterate = [iterate[k] + coarse[k] for k in range(3)]
    for sweep_index in range(POST):
        iterate = smooth_whole(iterate, source, noise, couplings, diagonal)
    return iterate


def gather_grid(block):
    return gather_grids([block])[0]


def gather_grids(blocks):
    count_rows = lax.axis_size(ROWS)
    count_cols = lax.axis_size(COLS)
    planes = blocks[0].shape[0]
    tiles = []
    for b in blocks:
        run = b.shape[1] * b.shape[2]
        padded = jnp.pad(b.reshape(planes, run), ((0, 0), (0, -run % 128)))
        tiles.append(padded.reshape(planes, -1, 128).transpose(1, 0, 2))
    packed = jnp.concatenate(tiles, axis=0)
    stacked = lax.all_gather(packed, GRID, axis=1, tiled=False)
    grids = []
    first = 0
    for b, t in zip(blocks, tiles):
        _, height, width = b.shape
        part = stacked[first:first + t.shape[0]]
        first += t.shape[0]
        if width % 128 == 0:
            part = part.reshape(height, width // 128, count_rows, count_cols, planes, 128)
            whole = part.transpose(4, 2, 0, 3, 1, 5)
        else:
            part = part.transpose(2, 1, 0, 3).reshape(planes, count_rows, count_cols, -1)
            part = part[..., : height * width].reshape(planes, count_rows, count_cols, height, width)
            whole = part.transpose(0, 1, 3, 2, 4)
        whole = whole.reshape(planes, count_rows * height, count_cols * width)
        grids.append([whole[k] for k in range(planes)])
    return grids


def own_window(whole, height, width, ring):
    row = lax.axis_index(ROWS) * height
    col = lax.axis_index(COLS) * width
    lead = whole.shape[:-2]
    pads = [(0, 0)] * len(lead) + [(ring, ring), (ring, ring)]
    padded = jnp.pad(whole, pads) if ring else whole
    return lax.dynamic_slice(
        padded, (0,) * len(lead) + (row, col), lead + (height + 2 * ring, width + 2 * ring)
    )


def inside(height, width, ext):
    rows = lax.axis_index(ROWS) * height - ext + lax.broadcasted_iota(
        jnp.int32, (height + 2 * ext, width + 2 * ext), 0
    )
    cols = lax.axis_index(COLS) * width - ext + lax.broadcasted_iota(
        jnp.int32, (height + 2 * ext, width + 2 * ext), 1
    )
    return (
        (rows >= 0)
        & (rows < lax.axis_size(ROWS) * height)
        & (cols >= 0)
        & (cols < lax.axis_size(COLS) * width)
    )


def sweep_ext(iterate, source, noise, couplings, diagonal, mask):
    image = apply_ext(iterate, noise, couplings)
    new = [
        i[1:-1, 1:-1] + OMEGA * (s - a) / d for i, s, a, d in zip(iterate, source, image, diagonal)
    ]
    if mask is None:
        return new
    return [jnp.where(mask, n, 0.0) for n in new]


def level_split(source, noise, couplings, below):
    height = source[0].shape[0] - 2 * HALO
    width = source[0].shape[1] - 2 * HALO
    diagonal = diagonal_of(noise, couplings)
    ext = HALO
    mask = inside(height, width, ext)
    iterate = [jnp.where(mask, OMEGA * s / d, 0.0) for s, d in zip(source, diagonal)]
    for sweep_index in range(PRE - 1):
        ext -= 1
        cut = HALO - ext
        iterate = sweep_ext(
            iterate, crops(source, cut), crops(noise, cut), crops(couplings, cut),
            crops(diagonal, cut), inside(height, width, ext),
        )
    image = apply_ext(crops(iterate, ext - 1), crops(noise, HALO), crops(couplings, HALO))
    residual = [s - a for s, a in zip(crops(source, HALO), image)]
    coarse = below(residual)
    ring = (POST + 1) // 2
    fine = crop(prolong(coarse), 2 * ring - POST)
    iterate = [i + fine[k] for k, i in enumerate(crops(iterate, ext - POST))]
    for sweep_index in range(POST):
        ext = POST - 1 - sweep_index
        cut = HALO - ext
        iterate = sweep_ext(
            iterate, crops(source, cut), crops(noise, cut), crops(couplings, cut),
            crops(diagonal, cut), inside(height, width, ext) if ext else None,
        )
    return iterate


def spans(n, pick_last):
    mats = []
    for level in range(1, LEVELS):
        size = 1 << level
        rows = lax.broadcasted_iota(jnp.int32, (n, n // size), 0)
        cols = lax.broadcasted_iota(jnp.int32, (n, n // size), 1)
        hit = (rows == cols * size + size - 1) if pick_last else (rows // size == cols)
        mats.append(hit.astype(jnp.float32))
    return jnp.concatenate(mats, axis=1)


def hierarchy_of(noise, down, right):
    height, width = down.shape
    row_sum, row_last = spans(height, False), spans(height, True)
    col_sum, col_last = spans(width, False), spans(width, True)
    tall = jnp.concatenate(
        [
            jnp.einsum("phw,hv->pvw", noise, row_sum, precision=HIGH),
            jnp.einsum("hw,hv->vw", down, row_last, precision=HIGH)[None],
        ]
    )
    both = jnp.einsum("pvw,wu->pvu", tall, col_sum, precision=HIGH)
    wide = jnp.einsum(
        "hv,hw->vw", row_sum, jnp.einsum("hw,wu->hu", right, col_last, precision=HIGH),
        precision=HIGH,
    )
    noises, downs, rights = [noise], [down], [right]
    row, col = 0, 0
    for level in range(1, LEVELS):
        rows, cols = height >> level, width >> level
        noises.append(both[:6, row:row + rows, col:col + cols])
        downs.append(both[6, row:row + rows, col:col + cols])
        rights.append(wide[row:row + rows, col:col + cols])
        row, col = row + rows, col + cols
    return noises, downs, rights


def on_device(right_side, noise_block, edges):
    count_rows = lax.axis_size(ROWS)
    count_cols = lax.axis_size(COLS)
    height0, width0 = right_side.shape[1], right_side.shape[2]

    noises, downs, rights = hierarchy_of(noise_block, edges[0], edges[1])

    gathered = LEVELS - 1
    for level in range(LEVELS):
        height, width = height0 >> level, width0 >> level
        whole = count_rows * height * count_cols * width
        if whole <= GATHER_PIXELS or height <= HALO or width <= HALO or level == LEVELS - 1:
            gathered = level
            break

    if gathered == 0:
        packed = gather_grids(
            [jnp.concatenate([noises[l], downs[l][None], rights[l][None]]) for l in range(LEVELS)]
        )
        hierarchy = [(p[:6], p[6], p[7]) for p in packed]
        correction = cycle_whole(gather_grid(right_side), hierarchy, 0)
        return jnp.stack([own_window(c, height0, width0, 0) for c in correction])

    packed = gather_grids(
        [
            jnp.concatenate([noises[l], downs[l][None], rights[l][None]])
            for l in range(gathered, LEVELS)
        ]
    )
    hierarchy = [(p[:6], p[6], p[7]) for p in packed]
    split_inputs = []
    for level in range(gathered):
        parts = [noises[level], downs[level][None], rights[level][None]]
        if level == 0:
            parts = [right_side] + parts
        ringed = with_halo(jnp.concatenate(parts), HALO + 1)
        ringed = [ringed[k] for k in range(ringed.shape[0])]
        source = crops(ringed[:3], 1) if level == 0 else None
        if level == 0:
            ringed = ringed[3:]
        down, right = ringed[6], ringed[7]
        couplings = [down[1:-1, 1:-1], down[:-2, 1:-1], right[1:-1, 1:-1], right[1:-1, :-2]]
        split_inputs.append((source, crops(ringed[:6], 1), couplings))

    ring = (POST + 1) // 2

    def run(level, source):
        height, width = height0 >> level, width0 >> level
        _, noise, couplings = split_inputs[level]

        def below(residual):
            coarse_source = restrict_sum(jnp.stack(residual))
            if level + 1 == gathered:
                correction = cycle_whole(gather_grid(coarse_source), hierarchy, gathered)
                return own_window(jnp.stack(correction), height // 2, width // 2, ring)
            coarse = run(level + 1, list(with_halo(coarse_source, HALO)))
            return with_halo(jnp.stack(coarse), ring)

        return level_split(source, noise, couplings, below)

    return jnp.stack(run(0, split_inputs[0][0]))


def solution(mesh):
    in_specs = (
        P(None, ("groups", "tiles"), ("band", "stokes")),
        P(None, ("groups", "tiles"), ("band", "stokes")),
        P(None, ("groups", "tiles"), ("band", "stokes")),
    )
    out_specs = P(None, ("groups", "tiles"), ("band", "stokes"))
    return jax.shard_map(
        on_device, mesh=mesh, in_specs=in_specs, out_specs=out_specs, check_vma=False
    )
```

```python
import jax
import jax.numpy as jnp
from jax import lax
from jax.sharding import PartitionSpec as P

LEVELS = 5
PRE = 2
POST = 2
COARSE_SWEEPS = 8

OMEGA = 0.8

ROWS = "tiles"
COLS = ("band", "stokes")
GRID = ("tiles", "band", "stokes")

HALO = PRE - 1 + POST
GATHER_PIXELS = 32768


def with_halo(cells, width):
    for axis, dim in ((ROWS, 1), (COLS, 2)):
        count = lax.axis_size(axis)
        ends = count - 1
        head = lax.slice_in_dim(cells, 0, width, axis=dim)
        tail = lax.slice_in_dim(cells, cells.shape[dim] - width, cells.shape[dim], axis=dim)
        cells = jnp.concatenate(
            [
                lax.ppermute(tail, axis, [(i, i + 1) for i in range(ends)]),
                cells,
                lax.ppermute(head, axis, [(i + 1, i) for i in range(ends)]),
            ],
            axis=dim,
        )
    return cells


def crop(x, k):
    if k == 0:
        return x
    return x[..., k:-k, k:-k]


HIGH = lax.Precision.HIGHEST


def pairs(n, pick=None):
    rows = lax.broadcasted_iota(jnp.int32, (n, n // 2), 0)
    cols = lax.broadcasted_iota(jnp.int32, (n, n // 2), 1)
    hit = (rows // 2 == cols) if pick is None else (rows == 2 * cols + pick)
    return hit.astype(jnp.float32)


def sum_rows(x, m):
    return jnp.einsum("...hw,hv->...vw", x, m, precision=HIGH)


def sum_cols(x, m):
    return jnp.einsum("...hw,wv->...hv", x, m, precision=HIGH)


def restrict_sum(x):
    return sum_cols(sum_rows(x, pairs(x.shape[-2])), pairs(x.shape[-1]))


def restrict_down(down):
    return sum_cols(sum_rows(down, pairs(down.shape[-2], 1)), pairs(down.shape[-1]))


def restrict_right(right):
    return sum_rows(sum_cols(right, pairs(right.shape[-1], 1)), pairs(right.shape[-2]))


def prolong(coarse):
    height, width = coarse.shape[-2] * 2, coarse.shape[-1] * 2
    wider = jnp.einsum("...hv,wv->...hw", coarse, pairs(width), precision=HIGH)
    return jnp.einsum("...vw,hv->...hw", wider, pairs(height), precision=HIGH)


def apply_planes(iterate, padded, noise, couplings):
    first = noise[0] * iterate[0] + noise[3] * iterate[1] + noise[4] * iterate[2]
    second = noise[3] * iterate[0] + noise[1] * iterate[1] + noise[5] * iterate[2]
    third = noise[4] * iterate[0] + noise[5] * iterate[1] + noise[2] * iterate[2]
    totals = couplings[0] + couplings[1] + couplings[2] + couplings[3]
    image = []
    for local, core, rim in zip((first, second, third), iterate, padded):
        neighbours = (
            couplings[0] * rim[2:, 1:-1]
            + couplings[1] * rim[:-2, 1:-1]
            + couplings[2] * rim[1:-1, 2:]
            + couplings[3] * rim[1:-1, :-2]
        )
        image.append(local + totals * core - neighbours)
    return image


def apply_ext(padded, noise, couplings):
    return apply_planes([p[1:-1, 1:-1] for p in padded], padded, noise, couplings)


def diagonal_of(noise, couplings):
    totals = couplings[0] + couplings[1] + couplings[2] + couplings[3]
    return [noise[k] + totals for k in range(3)]


def couplings_from(down, right):
    upward = jnp.pad(down, ((1, 0), (0, 0)))[:-1, :]
    leftward = jnp.pad(right, ((0, 0), (1, 0)))[:, :-1]
    return [down, upward, right, leftward]


def crops(planes, k):
    return [crop(p, k) for p in planes]


def smooth_whole(iterate, source, noise, couplings, diagonal):
    image = apply_planes(iterate, [jnp.pad(p, 1) for p in iterate], noise, couplings)
    return [i + OMEGA * (s - a) / d for i, s, a, d in zip(iterate, source, image, diagonal)]


def cycle_whole(source, hierarchy, level_index):
    noise, down, right = hierarchy[0]
    couplings = couplings_from(down, right)
    diagonal = diagonal_of(noise, couplings)
    iterate = [OMEGA * s / d for s, d in zip(source, diagonal)]
    if level_index == LEVELS - 1:
        for sweep_index in range(COARSE_SWEEPS - 1):
            iterate = smooth_whole(iterate, source, noise, couplings, diagonal)
        return iterate
    for sweep_index in range(PRE - 1):
        iterate = smooth_whole(iterate, source, noise, couplings, diagonal)
    image = apply_planes(iterate, [jnp.pad(p, 1) for p in iterate], noise, couplings)
    residual = restrict_sum(jnp.stack([s - a for s, a in zip(source, image)]))
    coarse = prolong(
        jnp.stack(cycle_whole([residual[k] for k in range(3)], hierarchy[1:], level_index + 1))
    )
    iterate = [iterate[k] + coarse[k] for k in range(3)]
    for sweep_index in range(POST):
        iterate = smooth_whole(iterate, source, noise, couplings, diagonal)
    return iterate


def gather_grid(block):
    return gather_grids([block])[0]


def gather_grids(blocks):
    count_rows = lax.axis_size(ROWS)
    count_cols = lax.axis_size(COLS)
    planes = blocks[0].shape[0]
    tiles = []
    for b in blocks:
        run = b.shape[1] * b.shape[2]
        padded = jnp.pad(b.reshape(planes, run), ((0, 0), (0, -run % 128)))
        tiles.append(padded.reshape(planes, -1, 128).transpose(1, 0, 2))
    packed = jnp.concatenate(tiles, axis=0)
    stacked = lax.all_gather(packed, GRID, axis=1, tiled=False)
    grids = []
    first = 0
    for b, t in zip(blocks, tiles):
        _, height, width = b.shape
        part = stacked[first:first + t.shape[0]]
        first += t.shape[0]
        if width % 128 == 0:
            part = part.reshape(height, width // 128, count_rows, count_cols, planes, 128)
            grids.append(
                [
                    part[:, :, :, :, k, :]
                    .transpose(2, 0, 3, 1, 4)
                    .reshape(count_rows * height, count_cols * width)
                    for k in range(planes)
                ]
            )
            continue
        else:
            part = part.transpose(2, 1, 0, 3).reshape(planes, count_rows, count_cols, -1)
            part = part[..., : height * width].reshape(planes, count_rows, count_cols, height, width)
            whole = part.transpose(0, 1, 3, 2, 4)
        whole = whole.reshape(planes, count_rows * height, count_cols * width)
        grids.append([whole[k] for k in range(planes)])
    return grids


def own_window(whole, height, width, ring):
    row = lax.axis_index(ROWS) * height
    col = lax.axis_index(COLS) * width
    lead = whole.shape[:-2]
    pads = [(0, 0)] * len(lead) + [(ring, ring), (ring, ring)]
    padded = jnp.pad(whole, pads) if ring else whole
    return lax.dynamic_slice(
        padded, (0,) * len(lead) + (row, col), lead + (height + 2 * ring, width + 2 * ring)
    )


def inside(height, width, ext):
    rows = lax.axis_index(ROWS) * height - ext + lax.broadcasted_iota(
        jnp.int32, (height + 2 * ext, width + 2 * ext), 0
    )
    cols = lax.axis_index(COLS) * width - ext + lax.broadcasted_iota(
        jnp.int32, (height + 2 * ext, width + 2 * ext), 1
    )
    return (
        (rows >= 0)
        & (rows < lax.axis_size(ROWS) * height)
        & (cols >= 0)
        & (cols < lax.axis_size(COLS) * width)
    )


def sweep_ext(iterate, source, noise, couplings, diagonal, mask):
    image = apply_ext(iterate, noise, couplings)
    new = [
        i[1:-1, 1:-1] + OMEGA * (s - a) / d for i, s, a, d in zip(iterate, source, image, diagonal)
    ]
    if mask is None:
        return new
    return [jnp.where(mask, n, 0.0) for n in new]


def level_split(source, noise, couplings, below):
    height = source[0].shape[0] - 2 * HALO
    width = source[0].shape[1] - 2 * HALO
    diagonal = diagonal_of(noise, couplings)
    ext = HALO
    mask = inside(height, width, ext)
    iterate = [jnp.where(mask, OMEGA * s / d, 0.0) for s, d in zip(source, diagonal)]
    for sweep_index in range(PRE - 1):
        ext -= 1
        cut = HALO - ext
        iterate = sweep_ext(
            iterate, crops(source, cut), crops(noise, cut), crops(couplings, cut),
            crops(diagonal, cut), inside(height, width, ext),
        )
    image = apply_ext(crops(iterate, ext - 1), crops(noise, HALO), crops(couplings, HALO))
    residual = [s - a for s, a in zip(crops(source, HALO), image)]
    coarse = below(residual)
    ring = (POST + 1) // 2
    fine = crop(prolong(coarse), 2 * ring - POST)
    iterate = [i + fine[k] for k, i in enumerate(crops(iterate, ext - POST))]
    for sweep_index in range(POST):
        ext = POST - 1 - sweep_index
        cut = HALO - ext
        iterate = sweep_ext(
            iterate, crops(source, cut), crops(noise, cut), crops(couplings, cut),
            crops(diagonal, cut), inside(height, width, ext) if ext else None,
        )
    return iterate


def spans(n, pick_last):
    mats = []
    for level in range(1, LEVELS):
        size = 1 << level
        rows = lax.broadcasted_iota(jnp.int32, (n, n // size), 0)
        cols = lax.broadcasted_iota(jnp.int32, (n, n // size), 1)
        hit = (rows == cols * size + size - 1) if pick_last else (rows // size == cols)
        mats.append(hit.astype(jnp.float32))
    return jnp.concatenate(mats, axis=1)


def hierarchy_of(noise, down, right):
    height, width = down.shape
    row_sum, row_last = spans(height, False), spans(height, True)
    col_sum, col_last = spans(width, False), spans(width, True)
    tall = jnp.concatenate(
        [
            jnp.einsum("phw,hv->pvw", noise, row_sum, precision=HIGH),
            jnp.einsum("hw,hv->vw", down, row_last, precision=HIGH)[None],
        ]
    )
    both = jnp.einsum("pvw,wu->pvu", tall, col_sum, precision=HIGH)
    wide = jnp.einsum(
        "hv,hw->vw", row_sum, jnp.einsum("hw,wu->hu", right, col_last, precision=HIGH),
        precision=HIGH,
    )
    noises, downs, rights = [noise], [down], [right]
    row, col = 0, 0
    for level in range(1, LEVELS):
        rows, cols = height >> level, width >> level
        noises.append(both[:6, row:row + rows, col:col + cols])
        downs.append(both[6, row:row + rows, col:col + cols])
        rights.append(wide[row:row + rows, col:col + cols])
        row, col = row + rows, col + cols
    return noises, downs, rights


def on_device(right_side, noise_block, edges):
    count_rows = lax.axis_size(ROWS)
    count_cols = lax.axis_size(COLS)
    height0, width0 = right_side.shape[1], right_side.shape[2]

    noises, downs, rights = hierarchy_of(noise_block, edges[0], edges[1])

    gathered = LEVELS - 1
    for level in range(LEVELS):
        height, width = height0 >> level, width0 >> level
        whole = count_rows * height * count_cols * width
        if whole <= GATHER_PIXELS or height <= HALO or width <= HALO or level == LEVELS - 1:
            gathered = level
            break

    if gathered == 0:
        packed = gather_grids(
            [jnp.concatenate([noises[l], downs[l][None], rights[l][None]]) for l in range(LEVELS)]
        )
        hierarchy = [(p[:6], p[6], p[7]) for p in packed]
        correction = cycle_whole(gather_grid(right_side), hierarchy, 0)
        return jnp.stack([own_window(c, height0, width0, 0) for c in correction])

    packed = gather_grids(
        [
            jnp.concatenate([noises[l], downs[l][None], rights[l][None]])
            for l in range(gathered, LEVELS)
        ]
    )
    hierarchy = [(p[:6], p[6], p[7]) for p in packed]
    split_inputs = []
    for level in range(gathered):
        parts = [noises[level], downs[level][None], rights[level][None]]
        if level == 0:
            parts = [right_side] + parts
        ringed = with_halo(jnp.concatenate(parts), HALO + 1)
        ringed = [ringed[k] for k in range(ringed.shape[0])]
        source = crops(ringed[:3], 1) if level == 0 else None
        if level == 0:
            ringed = ringed[3:]
        down, right = ringed[6], ringed[7]
        couplings = [down[1:-1, 1:-1], down[:-2, 1:-1], right[1:-1, 1:-1], right[1:-1, :-2]]
        split_inputs.append((source, crops(ringed[:6], 1), couplings))

    ring = (POST + 1) // 2

    def run(level, source):
        height, width = height0 >> level, width0 >> level
        _, noise, couplings = split_inputs[level]

        def below(residual):
            coarse_source = restrict_sum(jnp.stack(residual))
            if level + 1 == gathered:
                correction = cycle_whole(gather_grid(coarse_source), hierarchy, gathered)
                return own_window(jnp.stack(correction), height // 2, width // 2, ring)
            coarse = run(level + 1, list(with_halo(coarse_source, HALO)))
            return with_halo(jnp.stack(coarse), ring)

        return level_split(source, noise, couplings, below)

    return jnp.stack(run(0, split_inputs[0][0]))


def solution(mesh):
    in_specs = (
        P(None, ("groups", "tiles"), ("band", "stokes")),
        P(None, ("groups", "tiles"), ("band", "stokes")),
        P(None, ("groups", "tiles"), ("band", "stokes")),
    )
    out_specs = P(None, ("groups", "tiles"), ("band", "stokes"))
    return jax.shard_map(
        on_device, mesh=mesh, in_specs=in_specs, out_specs=out_specs, check_vma=False
    )
```

```python
import jax
import jax.numpy as jnp
from jax import lax
from jax.sharding import PartitionSpec as P

LEVELS = 5
PRE = 2
POST = 2
COARSE_SWEEPS = 8

OMEGA = 0.8

ROWS = "tiles"
COLS = ("band", "stokes")
GRID = ("tiles", "band", "stokes")

HALO = PRE - 1 + POST
GATHER_PIXELS = 32768


def with_halo(cells, width):
    for axis, dim in ((ROWS, 1), (COLS, 2)):
        count = lax.axis_size(axis)
        ends = count - 1
        head = lax.slice_in_dim(cells, 0, width, axis=dim)
        tail = lax.slice_in_dim(cells, cells.shape[dim] - width, cells.shape[dim], axis=dim)
        cells = jnp.concatenate(
            [
                lax.ppermute(tail, axis, [(i, i + 1) for i in range(ends)]),
                cells,
                lax.ppermute(head, axis, [(i + 1, i) for i in range(ends)]),
            ],
            axis=dim,
        )
    return cells


def crop(x, k):
    if k == 0:
        return x
    return x[..., k:-k, k:-k]


HIGH = lax.Precision.HIGHEST


def pairs(n, pick=None):
    rows = lax.broadcasted_iota(jnp.int32, (n, n // 2), 0)
    cols = lax.broadcasted_iota(jnp.int32, (n, n // 2), 1)
    hit = (rows // 2 == cols) if pick is None else (rows == 2 * cols + pick)
    return hit.astype(jnp.float32)


def sum_rows(x, m):
    return jnp.einsum("...hw,hv->...vw", x, m, precision=HIGH)


def sum_cols(x, m):
    return jnp.einsum("...hw,wv->...hv", x, m, precision=HIGH)


def restrict_sum(x):
    return sum_cols(sum_rows(x, pairs(x.shape[-2])), pairs(x.shape[-1]))


def restrict_down(down):
    return sum_cols(sum_rows(down, pairs(down.shape[-2], 1)), pairs(down.shape[-1]))


def restrict_right(right):
    return sum_rows(sum_cols(right, pairs(right.shape[-1], 1)), pairs(right.shape[-2]))


def prolong(coarse):
    height, width = coarse.shape[-2] * 2, coarse.shape[-1] * 2
    wider = jnp.einsum("...hv,wv->...hw", coarse, pairs(width), precision=HIGH)
    return jnp.einsum("...vw,hv->...hw", wider, pairs(height), precision=HIGH)


def apply_planes(iterate, padded, noise, couplings):
    first = noise[0] * iterate[0] + noise[3] * iterate[1] + noise[4] * iterate[2]
    second = noise[3] * iterate[0] + noise[1] * iterate[1] + noise[5] * iterate[2]
    third = noise[4] * iterate[0] + noise[5] * iterate[1] + noise[2] * iterate[2]
    totals = couplings[0] + couplings[1] + couplings[2] + couplings[3]
    image = []
    for local, core, rim in zip((first, second, third), iterate, padded):
        neighbours = (
            couplings[0] * rim[2:, 1:-1]
            + couplings[1] * rim[:-2, 1:-1]
            + couplings[2] * rim[1:-1, 2:]
            + couplings[3] * rim[1:-1, :-2]
        )
        image.append(local + totals * core - neighbours)
    return image


def apply_ext(padded, noise, couplings):
    return apply_planes([p[1:-1, 1:-1] for p in padded], padded, noise, couplings)


def diagonal_of(noise, couplings):
    totals = couplings[0] + couplings[1] + couplings[2] + couplings[3]
    return [noise[k] + totals for k in range(3)]


def couplings_from(down, right):
    upward = jnp.pad(down, ((1, 0), (0, 0)))[:-1, :]
    leftward = jnp.pad(right, ((0, 0), (1, 0)))[:, :-1]
    return [down, upward, right, leftward]


def crops(planes, k):
    return [crop(p, k) for p in planes]


def smooth_whole(iterate, source, noise, couplings, diagonal):
    image = apply_planes(iterate, [jnp.pad(p, 1) for p in iterate], noise, couplings)
    return [i + OMEGA * (s - a) / d for i, s, a, d in zip(iterate, source, image, diagonal)]


def cycle_whole(source, hierarchy, level_index):
    noise, down, right = hierarchy[0]
    couplings = couplings_from(down, right)
    diagonal = diagonal_of(noise, couplings)
    iterate = [OMEGA * s / d for s, d in zip(source, diagonal)]
    if level_index == LEVELS - 1:
        for sweep_index in range(COARSE_SWEEPS - 1):
            iterate = smooth_whole(iterate, source, noise, couplings, diagonal)
        return iterate
    for sweep_index in range(PRE - 1):
        iterate = smooth_whole(iterate, source, noise, couplings, diagonal)
    image = apply_planes(iterate, [jnp.pad(p, 1) for p in iterate], noise, couplings)
    residual = restrict_sum(jnp.stack([s - a for s, a in zip(source, image)]))
    coarse = prolong(
        jnp.stack(cycle_whole([residual[k] for k in range(3)], hierarchy[1:], level_index + 1))
    )
    iterate = [iterate[k] + coarse[k] for k in range(3)]
    for sweep_index in range(POST):
        iterate = smooth_whole(iterate, source, noise, couplings, diagonal)
    return iterate


def gather_grid(block):
    return gather_grids([block])[0]


def gather_grids(blocks):
    count_rows = lax.axis_size(ROWS)
    count_cols = lax.axis_size(COLS)
    planes = blocks[0].shape[0]
    tiles = []
    for b in blocks:
        run = b.shape[1] * b.shape[2]
        padded = jnp.pad(b.reshape(planes, run), ((0, 0), (0, -run % 128)))
        tiles.append(padded.reshape(planes, -1, 128).transpose(1, 0, 2))
    packed = jnp.concatenate(tiles, axis=0)
    stacked = lax.all_gather(packed, GRID, axis=1, tiled=False)
    grids = []
    first = 0
    for b, t in zip(blocks, tiles):
        _, height, width = b.shape
        part = stacked[first:first + t.shape[0]]
        first += t.shape[0]
        if width % 128 == 0:
            part = part.reshape(height, width // 128, count_rows, count_cols, planes, 128)
            whole = part.transpose(4, 2, 0, 3, 1, 5)
        else:
            part = part.transpose(2, 1, 0, 3).reshape(planes, count_rows, count_cols, -1)
            part = part[..., : height * width].reshape(planes, count_rows, count_cols, height, width)
            whole = part.transpose(0, 1, 3, 2, 4)
        whole = whole.reshape(planes, count_rows * height, count_cols * width)
        grids.append([whole[k] for k in range(planes)])
    return grids


def own_window(whole, height, width, ring, rimmed=0):
    row = lax.axis_index(ROWS) * (height - 2 * rimmed)
    col = lax.axis_index(COLS) * (width - 2 * rimmed)
    lead = whole.shape[:-2]
    pads = [(0, 0)] * len(lead) + [(ring, ring), (ring, ring)]
    padded = jnp.pad(whole, pads) if ring else whole
    return lax.dynamic_slice(
        padded, (0,) * len(lead) + (row, col), lead + (height + 2 * ring, width + 2 * ring)
    )


def inside(height, width, ext):
    rows = lax.axis_index(ROWS) * height - ext + lax.broadcasted_iota(
        jnp.int32, (height + 2 * ext, width + 2 * ext), 0
    )
    cols = lax.axis_index(COLS) * width - ext + lax.broadcasted_iota(
        jnp.int32, (height + 2 * ext, width + 2 * ext), 1
    )
    return (
        (rows >= 0)
        & (rows < lax.axis_size(ROWS) * height)
        & (cols >= 0)
        & (cols < lax.axis_size(COLS) * width)
    )


def sweep_ext(iterate, source, noise, couplings, diagonal, mask):
    image = apply_ext(iterate, noise, couplings)
    new = [
        i[1:-1, 1:-1] + OMEGA * (s - a) / d for i, s, a, d in zip(iterate, source, image, diagonal)
    ]
    if mask is None:
        return new
    return [jnp.where(mask, n, 0.0) for n in new]


def level_split(source, noise, couplings, below):
    height = source[0].shape[0] - 2 * HALO
    width = source[0].shape[1] - 2 * HALO
    diagonal = diagonal_of(noise, couplings)
    ext = HALO
    mask = inside(height, width, ext)
    iterate = [jnp.where(mask, OMEGA * s / d, 0.0) for s, d in zip(source, diagonal)]
    for sweep_index in range(PRE - 1):
        ext -= 1
        cut = HALO - ext
        iterate = sweep_ext(
            iterate, crops(source, cut), crops(noise, cut), crops(couplings, cut),
            crops(diagonal, cut), inside(height, width, ext),
        )
    image = apply_ext(crops(iterate, ext - 1), crops(noise, HALO), crops(couplings, HALO))
    residual = [s - a for s, a in zip(crops(source, HALO), image)]
    coarse = below(residual)
    ring = (POST + 1) // 2
    fine = crop(prolong(coarse), 2 * ring - POST)
    iterate = [i + fine[k] for k, i in enumerate(crops(iterate, ext - POST))]
    for sweep_index in range(POST):
        ext = POST - 1 - sweep_index
        cut = HALO - ext
        iterate = sweep_ext(
            iterate, crops(source, cut), crops(noise, cut), crops(couplings, cut),
            crops(diagonal, cut), inside(height, width, ext) if ext else None,
        )
    return iterate


def spans(n, pick_last):
    mats = []
    for level in range(1, LEVELS):
        size = 1 << level
        rows = lax.broadcasted_iota(jnp.int32, (n, n // size), 0)
        cols = lax.broadcasted_iota(jnp.int32, (n, n // size), 1)
        hit = (rows == cols * size + size - 1) if pick_last else (rows // size == cols)
        mats.append(hit.astype(jnp.float32))
    return jnp.concatenate(mats, axis=1)


def hierarchy_of(noise, down, right):
    height, width = down.shape
    row_sum, row_last = spans(height, False), spans(height, True)
    col_sum, col_last = spans(width, False), spans(width, True)
    tall = jnp.concatenate(
        [
            jnp.einsum("phw,hv->pvw", noise, row_sum, precision=HIGH),
            jnp.einsum("hw,hv->vw", down, row_last, precision=HIGH)[None],
        ]
    )
    both = jnp.einsum("pvw,wu->pvu", tall, col_sum, precision=HIGH)
    wide = jnp.einsum(
        "hv,hw->vw", row_sum, jnp.einsum("hw,wu->hu", right, col_last, precision=HIGH),
        precision=HIGH,
    )
    noises, downs, rights = [noise], [down], [right]
    row, col = 0, 0
    for level in range(1, LEVELS):
        rows, cols = height >> level, width >> level
        noises.append(both[:6, row:row + rows, col:col + cols])
        downs.append(both[6, row:row + rows, col:col + cols])
        rights.append(wide[row:row + rows, col:col + cols])
        row, col = row + rows, col + cols
    return noises, downs, rights


def on_device(right_side, noise_block, edges):
    count_rows = lax.axis_size(ROWS)
    count_cols = lax.axis_size(COLS)
    height0, width0 = right_side.shape[1], right_side.shape[2]

    noises, downs, rights = hierarchy_of(noise_block, edges[0], edges[1])

    gathered = LEVELS - 1
    for level in range(LEVELS):
        height, width = height0 >> level, width0 >> level
        whole = count_rows * height * count_cols * width
        if whole <= GATHER_PIXELS or height <= HALO or width <= HALO or level == LEVELS - 1:
            gathered = level
            break

    if gathered == 0:
        packed = gather_grids(
            [jnp.concatenate([noises[l], downs[l][None], rights[l][None]]) for l in range(LEVELS)]
        )
        hierarchy = [(p[:6], p[6], p[7]) for p in packed]
        correction = cycle_whole(gather_grid(right_side), hierarchy, 0)
        return jnp.stack([own_window(c, height0, width0, 0) for c in correction])

    packed = gather_grids(
        [
            jnp.concatenate([noises[l], downs[l][None], rights[l][None]])
            for l in range(gathered, LEVELS)
        ]
    )
    hierarchy = [(p[:6], p[6], p[7]) for p in packed]
    split_inputs = []
    for level in range(gathered):
        parts = [noises[level], downs[level][None], rights[level][None]]
        if level == 0:
            parts = [right_side] + parts
        ringed = with_halo(jnp.concatenate(parts), HALO + 1)
        ringed = [ringed[k] for k in range(ringed.shape[0])]
        source = crops(ringed[:3], 1) if level == 0 else None
        if level == 0:
            ringed = ringed[3:]
        down, right = ringed[6], ringed[7]
        couplings = [down[1:-1, 1:-1], down[:-2, 1:-1], right[1:-1, 1:-1], right[1:-1, :-2]]
        split_inputs.append((source, crops(ringed[:6], 1), couplings))

    ring = (POST + 1) // 2

    def run(level, source):
        height, width = height0 >> level, width0 >> level
        _, noise, couplings = split_inputs[level]

        def below(residual):
            coarse_source = restrict_sum(jnp.stack(residual))
            if level + 1 == gathered:
                correction = cycle_whole(gather_grid(coarse_source), hierarchy, gathered)
                rimmed = jnp.stack([jnp.pad(c, ring) for c in correction])
                return own_window(rimmed, height // 2 + 2 * ring, width // 2 + 2 * ring, 0, ring)
            coarse = run(level + 1, list(with_halo(coarse_source, HALO)))
            return with_halo(jnp.stack(coarse), ring)

        return level_split(source, noise, couplings, below)

    return jnp.stack(run(0, split_inputs[0][0]))


def solution(mesh):
    in_specs = (
        P(None, ("groups", "tiles"), ("band", "stokes")),
        P(None, ("groups", "tiles"), ("band", "stokes")),
        P(None, ("groups", "tiles"), ("band", "stokes")),
    )
    out_specs = P(None, ("groups", "tiles"), ("band", "stokes"))
    return jax.shard_map(
        on_device, mesh=mesh, in_specs=in_specs, out_specs=out_specs, check_vma=False
    )
```
